32 devices in a mesh: row: 8 (over z, x), col: 4 (over y, core).
Axes of the slice: x: 2, y: 2, z: 4, core: 2. Of those that a mesh axis runs over, the one named last changes fastest.
Arguments:
- centers: float32 [3, 9472], P(None, ('row', 'col')), may hold values from -1 to 1
- panel_areas: float32 [9472], P(('row', 'col')), may hold values from 0.006164962 to 0.024659848
- jump_term: float32 [9472], P(('row', 'col')), may hold values from 1.5 to 3
- displacement: float32 [3, 9472], P(None, ('row', 'col')), may hold values from -0.3 to 0.3
- design_ids: int32 [9472], P(('row', 'col')), may hold values from 0 to 127
- primal_field: float32 [2, 9472], P(None, ('row', 'col')), may hold values from -6 to 6
- adjoint_start: float32 [9472, 8], P(('row', 'col')), may hold values from -6 to 6
- mic_panels: int32 [4, 4], replicated, may hold values from 0 to 9471
- wavenumber: float32 [1], replicated, may hold values from 10 to 20
Outputs:
- adjoint_field: float32 [9472, 8], P(('row', 'col'))
- sensitivity: float32 [4, 128], replicated
The draws below stay inside these ranges and needn't reach their ends.
All inputs are finite; a program needn't handle non-finite values.
Results may differ from the reference program's by a relative error of at most 0.0003.
Values sent between devices are 32-bit elements; how exact they have to be, the bound alone decides.
No kernel may reach another device: no remote copies, remote signals or barrier semaphores. Data moves between devices by JAX's collectives and lax.ppermute only.
A program may use at most 64 MiB of HBM per device.

```python
import math
import jax
import jax.numpy as jnp
from jax import lax

ZONES = 4
MICS = 4
DESIGN = 128
NPAN = 9472


def draw_centers(key, part):
    points = jax.random.uniform(key, (3, NPAN), jnp.float32, -1.0, 1.0)
    return points


def draw_panel_areas(key, part):
    scale = 1.0 / jnp.sqrt(jnp.float32(NPAN))
    spread = jnp.exp(jax.random.uniform(key, (NPAN,), jnp.float32, math.log(0.6), math.log(2.4)))
    return (spread * scale).astype(jnp.float32)


def plant(values, own_key, smallest, top_value):
    shape = values.shape
    index_at = [jax.random.randint(jax.random.fold_in(own_key, axis), (), 0, shape[axis]) for axis in range(len(shape))]
    values = values.at[tuple(index_at)].set(smallest)
    longest = shape.index(max(shape))
    index_at[longest] = (index_at[longest] + 1) % shape[longest]
    return values.at[tuple(index_at)].set(top_value)


def level_of(rng, dims, split, low, top_value):
    def one(dim, blocks):
        draws = jax.random.uniform(jax.random.fold_in(jax.random.fold_in(rng, 6), dim), (blocks,), jnp.float32, low / len(split), top_value / len(split))
        return jnp.repeat(jnp.exp(draws), dims[dim] // blocks).reshape((-1,) + (1,) * (len(dims) - dim - 1))

    factor_of = one(*split[0])
    for cut in split[1:]:
        factor_of = factor_of * one(*cut)
    return factor_of


def normal_values(stream_key, dims, scale, bound, split=(), kind=jnp.bfloat16):
    array = scale * jax.random.normal(stream_key, dims, jnp.float32)
    if split:
        array = array * level_of(stream_key, dims, split, -0.22, 0.18)
    return jnp.clip(array, -bound, bound).astype(kind)


def setup_inputs(seed: int = 0) -> dict:
    key_of = jax.random.split(jax.random.key(seed), 10)
    return {
        "centers": draw_centers(jax.random.fold_in(key_of[9], 71), 0),
        "panel_areas": draw_panel_areas(jax.random.fold_in(key_of[9], 71), 0),
        "jump_term": jnp.clip(1.5 + 1.5 * jax.random.uniform(key_of[2], (NPAN,), jnp.float32) ** level_of(key_of[2], (NPAN,), ((0, 32),), -0.2, 0.2), 1.5, 3.0),
        "displacement": normal_values(key_of[3], (3, NPAN), 0.05, 0.3, ((1, 32),), jnp.float32),
        "design_ids": plant(jax.random.randint(key_of[4], (NPAN,), 0, DESIGN), jax.random.fold_in(key_of[4], 1), 0, DESIGN - 1).astype(jnp.int32),
        "primal_field": normal_values(key_of[5], (2, NPAN), 1.0, 6.0, ((1, 32),), jnp.float32),
        "adjoint_start": normal_values(key_of[6], (NPAN, 2 * ZONES), 1.0, 6.0, ((0, 32),), jnp.float32),
        "mic_panels": plant(jax.random.randint(key_of[7], (ZONES, MICS), 0, NPAN), jax.random.fold_in(key_of[7], 1), 0, NPAN - 1).astype(jnp.int32),
        "wavenumber": jnp.clip(jnp.exp(jax.random.uniform(key_of[8], (1,), jnp.float32, math.log(10.0), math.log(20.0))), 10.0, 20.0),
    }


highest = lax.Precision.HIGHEST
four_pi = 4.0 * math.pi

def distances(rows_xyz, rows_area, cols_xyz, cols_area):
    diff_x = rows_xyz[0][:, None] - cols_xyz[0][None, :]
    diff_y = rows_xyz[1][:, None] - cols_xyz[1][None, :]
    diff_z = rows_xyz[2][:, None] - cols_xyz[2][None, :]
    square = diff_x * diff_x + diff_y * diff_y + diff_z * diff_z + 0.5 * (rows_area[:, None] + cols_area[None, :])
    return (diff_x, diff_y, diff_z, jnp.sqrt(square))

def kernel_parts(rows_xyz, rows_area, cols_xyz, cols_area, wave_value):
    radius = distances(rows_xyz, rows_area, cols_xyz, cols_area)[3]
    phase = wave_value * radius
    factor = 1.0 / (four_pi * radius)
    return (jnp.cos(phase) * factor, jnp.sin(phase) * factor)

def slope_parts(rows_xyz, rows_area, cols_xyz, cols_area, cols_move, wave_value):
    diff_x, diff_y, diff_z, radius = distances(rows_xyz, rows_area, cols_xyz, cols_area)
    along_move = diff_x * cols_move[0][None, :] + diff_y * cols_move[1][None, :] + diff_z * cols_move[2][None, :]
    phase = wave_value * radius
    cosine_part = jnp.cos(phase)
    sine_part = jnp.sin(phase)
    factor = along_move / (four_pi * radius * radius * radius)
    return ((-cosine_part - phase * sine_part) * factor, (phase * cosine_part - sine_part) * factor)

def contract_first(matrix, vector):
    return lax.dot_general(matrix, vector, (((0,), (0,)), ((), ())), precision=highest)

def conj_rows(real_part, imag_part, vector, zone_count):
    left_part = jnp.dot(real_part, vector, precision=highest)
    right_part = jnp.dot(imag_part, vector, precision=highest)
    return jnp.concatenate([left_part[:, :zone_count] + right_part[:, zone_count:], left_part[:, zone_count:] - right_part[:, :zone_count]], 1)

def inner_parts(left_part, right_part, zone_count):
    left_re, left_im = (left_part[:, :zone_count], left_part[:, zone_count:])
    right_re, right_im = (right_part[:, :zone_count], right_part[:, zone_count:])
    return (lax.optimization_barrier(jnp.sum(left_re * right_re + left_im * right_im, 0)), lax.optimization_barrier(jnp.sum(left_re * right_im - left_im * right_re, 0)))

def square_sum(vector):
    return lax.optimization_barrier(jnp.sum(vector * vector, 0)).reshape(2, -1).sum(0)

def complex_scale(scale_re, scale_im, vector, zone_count):
    vec_re, vec_im = (vector[:, :zone_count], vector[:, zone_count:])
    return jnp.concatenate([scale_re * vec_re - scale_im * vec_im, scale_re * vec_im + scale_im * vec_re], 1)

def least_squares(start_norm, first_re, first_im, first_norm, cross_re, cross_im, second_re, second_im, second_norm):
    gram_one = first_re * first_re + first_im * first_im + first_norm * first_norm
    gram_off_re = first_re * cross_re + first_im * cross_im + first_norm * second_re
    gram_off_im = first_re * cross_im - first_im * cross_re + first_norm * second_im
    gram_two = cross_re * cross_re + cross_im * cross_im + second_re * second_re + second_im * second_im + second_norm * second_norm
    rhs_one_re = start_norm * first_re
    rhs_one_im = -start_norm * first_im
    rhs_two_re = start_norm * cross_re
    rhs_two_im = -start_norm * cross_im
    determinant = gram_one * gram_two - gram_off_re * gram_off_re - gram_off_im * gram_off_im
    coef_one_re = (gram_two * rhs_one_re - (gram_off_re * rhs_two_re - gram_off_im * rhs_two_im)) / determinant
    coef_one_im = (gram_two * rhs_one_im - (gram_off_re * rhs_two_im + gram_off_im * rhs_two_re)) / determinant
    coef_two_re = (gram_one * rhs_two_re - (gram_off_re * rhs_one_re + gram_off_im * rhs_one_im)) / determinant
    coef_two_im = (gram_one * rhs_two_im - (gram_off_re * rhs_one_im - gram_off_im * rhs_one_re)) / determinant
    return (coef_one_re, coef_one_im, coef_two_re, coef_two_im)

def reference(centers, panel_areas, jump_term, displacement, design_ids, primal_field, adjoint_start, mic_panels, wavenumber):
    wave_value = wavenumber[0]
    panel_total = centers.shape[1]
    block_rows = math.gcd(512, panel_total)
    starts = jnp.arange(panel_total // block_rows, dtype=jnp.int32) * block_rows

    def apply_adjoint(vector):

        def one_block(offset):
            rows_xyz = lax.dynamic_slice_in_dim(centers, offset, block_rows, 1)
            rows_area = lax.dynamic_slice_in_dim(panel_areas, offset, block_rows, 0)
            real_part, imag_part = kernel_parts(rows_xyz, rows_area, centers, panel_areas, wave_value)
            return conj_rows(real_part, imag_part, vector, ZONES)
        summed = lax.map(one_block, starts).reshape(panel_total, 2 * ZONES)
        return panel_areas[:, None] * summed + jump_term[:, None] * vector
    panel_ids = jnp.arange(panel_total, dtype=jnp.int32)
    mic_hits = lax.optimization_barrier(jnp.sum((panel_ids[:, None, None] == mic_panels[None, :, :]).astype(jnp.float32), axis=2))
    right_side = jnp.concatenate([mic_hits * primal_field[0][:, None], mic_hits * primal_field[1][:, None]], 1)
    residual = right_side - apply_adjoint(adjoint_start)
    start_norm = jnp.sqrt(square_sum(residual))
    basis_one = residual / jnp.concatenate([start_norm, start_norm])[None, :]
    image_one = apply_adjoint(basis_one)
    first_re, first_im = inner_parts(basis_one, image_one, ZONES)
    lean_one = image_one - complex_scale(first_re, first_im, basis_one, ZONES)
    first_norm = jnp.sqrt(square_sum(lean_one))
    basis_two = lean_one / jnp.concatenate([first_norm, first_norm])[None, :]
    image_two = apply_adjoint(basis_two)
    cross_re, cross_im = inner_parts(basis_one, image_two, ZONES)
    second_re, second_im = inner_parts(basis_two, image_two, ZONES)
    lean_two = image_two - complex_scale(cross_re, cross_im, basis_one, ZONES) - complex_scale(second_re, second_im, basis_two, ZONES)
    second_norm = jnp.sqrt(square_sum(lean_two))
    coef_one_re, coef_one_im, coef_two_re, coef_two_im = least_squares(start_norm, first_re, first_im, first_norm, cross_re, cross_im, second_re, second_im, second_norm)
    adjoint_field = adjoint_start + complex_scale(coef_one_re, coef_one_im, basis_one, ZONES) + complex_scale(coef_two_re, coef_two_im, basis_two, ZONES)

    def column_block(offset):
        cols_xyz = lax.dynamic_slice_in_dim(centers, offset, block_rows, 1)
        cols_area = lax.dynamic_slice_in_dim(panel_areas, offset, block_rows, 0)
        cols_move = lax.dynamic_slice_in_dim(displacement, offset, block_rows, 1)
        slope_re, slope_im = slope_parts(centers, panel_areas, cols_xyz, cols_area, cols_move, wave_value)
        left_part = contract_first(slope_re, adjoint_field)
        right_part = contract_first(slope_im, adjoint_field)
        return jnp.concatenate([left_part[:, :ZONES] + right_part[:, ZONES:], right_part[:, :ZONES] - left_part[:, ZONES:]], 1)
    contracted = lax.map(column_block, starts).reshape(panel_total, 2 * ZONES)
    contrib = panel_areas[:, None] * (primal_field[0][:, None] * contracted[:, :ZONES] - primal_field[1][:, None] * contracted[:, ZONES:])
    onehot = (design_ids[:, None] == jnp.arange(DESIGN, dtype=jnp.int32)[None, :]).astype(jnp.float32)
    sensitivity = contract_first(contrib, onehot)
    return (adjoint_field, sensitivity)
```

```python
import math

import jax
import jax.numpy as jnp
from jax import lax
from jax.sharding import PartitionSpec as P

DESIGN = 128


highest = lax.Precision.HIGHEST
four_pi = 4.0 * math.pi


def distances(rows_xyz, rows_area, cols_xyz, cols_area):
    diff_x = rows_xyz[0][:, None] - cols_xyz[0][None, :]
    diff_y = rows_xyz[1][:, None] - cols_xyz[1][None, :]
    diff_z = rows_xyz[2][:, None] - cols_xyz[2][None, :]
    square = (
        diff_x * diff_x
        + diff_y * diff_y
        + diff_z * diff_z
        + 0.5 * (rows_area[:, None] + cols_area[None, :])
    )
    return (diff_x, diff_y, diff_z, jnp.sqrt(square))


def kernel_parts(rows_xyz, rows_area, cols_xyz, cols_area, wave_value):
    radius = distances(rows_xyz, rows_area, cols_xyz, cols_area)[3]
    phase = wave_value * radius
    factor = 1.0 / (four_pi * radius)
    return (jnp.cos(phase) * factor, jnp.sin(phase) * factor)


def slope_parts(rows_xyz, rows_area, cols_xyz, cols_area, cols_move, wave_value):
    diff_x, diff_y, diff_z, radius = distances(rows_xyz, rows_area, cols_xyz, cols_area)
    along_move = (
        diff_x * cols_move[0][None, :]
        + diff_y * cols_move[1][None, :]
        + diff_z * cols_move[2][None, :]
    )
    phase = wave_value * radius
    cosine_part = jnp.cos(phase)
    sine_part = jnp.sin(phase)
    factor = along_move / (four_pi * radius * radius * radius)
    return ((-cosine_part - phase * sine_part) * factor, (phase * cosine_part - sine_part) * factor)


def contract_first(matrix, vector):
    return lax.dot_general(matrix, vector, (((0,), (0,)), ((), ())), precision=highest)


def conj_columns(real_part, imag_part, vector, zone_count):
    left_part = contract_first(real_part, vector)
    right_part = contract_first(imag_part, vector)
    return jnp.concatenate(
        [
            left_part[:, :zone_count] + right_part[:, zone_count:],
            left_part[:, zone_count:] - right_part[:, :zone_count],
        ],
        1,
    )


def inner_parts(left_part, right_part, zone_count):
    left_re, left_im = (left_part[:, :zone_count], left_part[:, zone_count:])
    right_re, right_im = (right_part[:, :zone_count], right_part[:, zone_count:])
    return (
        jnp.sum(left_re * right_re + left_im * right_im, 0),
        jnp.sum(left_re * right_im - left_im * right_re, 0),
    )


def square_sum(vector):
    return jnp.sum(vector * vector, 0).reshape(2, -1).sum(0)


def complex_scale(scale_re, scale_im, vector, zone_count):
    vec_re, vec_im = (vector[:, :zone_count], vector[:, zone_count:])
    return jnp.concatenate(
        [scale_re * vec_re - scale_im * vec_im, scale_re * vec_im + scale_im * vec_re], 1
    )


def least_squares(
    start_norm,
    first_re,
    first_im,
    first_norm,
    cross_re,
    cross_im,
    second_re,
    second_im,
    second_norm,
):
    gram_one = first_re * first_re + first_im * first_im + first_norm * first_norm
    gram_off_re = first_re * cross_re + first_im * cross_im + first_norm * second_re
    gram_off_im = first_re * cross_im - first_im * cross_re + first_norm * second_im
    gram_two = (
        cross_re * cross_re
        + cross_im * cross_im
        + second_re * second_re
        + second_im * second_im
        + second_norm * second_norm
    )
    rhs_one_re = start_norm * first_re
    rhs_one_im = -start_norm * first_im
    rhs_two_re = start_norm * cross_re
    rhs_two_im = -start_norm * cross_im
    determinant = gram_one * gram_two - gram_off_re * gram_off_re - gram_off_im * gram_off_im
    coef_one_re = (
        gram_two * rhs_one_re - (gram_off_re * rhs_two_re - gram_off_im * rhs_two_im)
    ) / determinant
    coef_one_im = (
        gram_two * rhs_one_im - (gram_off_re * rhs_two_im + gram_off_im * rhs_two_re)
    ) / determinant
    coef_two_re = (
        gram_one * rhs_two_re - (gram_off_re * rhs_one_re + gram_off_im * rhs_one_im)
    ) / determinant
    coef_two_im = (
        gram_one * rhs_two_im - (gram_off_re * rhs_one_im - gram_off_im * rhs_one_re)
    ) / determinant
    return (coef_one_re, coef_one_im, coef_two_re, coef_two_im)


def slope_parts_t(own_xyz, own_area, own_move, all_xyz, all_area, wave_value):
    diff_x = all_xyz[0][None, :] - own_xyz[0][:, None]
    diff_y = all_xyz[1][None, :] - own_xyz[1][:, None]
    diff_z = all_xyz[2][None, :] - own_xyz[2][:, None]
    square = (
        diff_x * diff_x
        + diff_y * diff_y
        + diff_z * diff_z
        + 0.5 * (all_area[None, :] + own_area[:, None])
    )
    radius = jnp.sqrt(square)
    along_move = (
        diff_x * own_move[0][:, None]
        + diff_y * own_move[1][:, None]
        + diff_z * own_move[2][:, None]
    )
    phase = wave_value * radius
    cosine_part = jnp.cos(phase)
    sine_part = jnp.sin(phase)
    factor = along_move / (four_pi * radius * radius * radius)
    return ((-cosine_part - phase * sine_part) * factor, (phase * cosine_part - sine_part) * factor)


def chunk_size_of(count, limit):
    return math.gcd(count, limit)


def rows_sum(block_fn, count, limit):
    size = chunk_size_of(count, limit)
    starts = jnp.arange(count // size, dtype=jnp.int32) * size
    return jnp.sum(lax.map(lambda start: block_fn(start, size), starts), 0)


def local(
    centers,
    panel_areas,
    jump_term,
    displacement,
    design_ids,
    primal_field,
    adjoint_start,
    mic_panels,
    wavenumber,
):
    zone_count = adjoint_start.shape[1] // 2
    owned_count = centers.shape[1]
    axes = ("row", "col")
    wave_value = wavenumber[0]
    packed = jnp.concatenate([centers.T, panel_areas[:, None], adjoint_start], 1)
    gathered = lax.all_gather(packed, axes, axis=0, tiled=True)
    panel_total = gathered.shape[0]
    all_xyz = gathered[:, :3].T
    all_area = gathered[:, 3]
    start_full = gathered[:, 4:]
    limit = 2 * 4 * owned_count

    def apply_adjoint(vector_full, vector_own):
        def block(start, size):
            rows_xyz = lax.dynamic_slice_in_dim(all_xyz, start, size, 1)
            rows_area = lax.dynamic_slice_in_dim(all_area, start, size, 0)
            rows_vec = lax.dynamic_slice_in_dim(vector_full, start, size, 0)
            real_part, imag_part = kernel_parts(centers, panel_areas, rows_xyz, rows_area, wave_value)
            left_part = jnp.dot(real_part, rows_vec, precision=highest)
            right_part = jnp.dot(imag_part, rows_vec, precision=highest)
            return jnp.concatenate(
                [
                    left_part[:, :zone_count] + right_part[:, zone_count:],
                    left_part[:, zone_count:] - right_part[:, :zone_count],
                ],
                1,
            )

        summed = rows_sum(block, panel_total, limit)
        return panel_areas[:, None] * summed + jump_term[:, None] * vector_own

    first_panel = (
        lax.axis_index("row") * lax.axis_size("col") + lax.axis_index("col")
    ) * owned_count
    panel_ids = first_panel + jnp.arange(owned_count, dtype=jnp.int32)
    mic_hits = jnp.sum(
        (panel_ids[:, None, None] == mic_panels[None, :, :]).astype(jnp.float32), axis=2
    )
    right_side = jnp.concatenate(
        [mic_hits * primal_field[0][:, None], mic_hits * primal_field[1][:, None]], 1
    )
    residual = right_side - apply_adjoint(start_full, adjoint_start)
    residual_full = lax.all_gather(residual, axes, axis=0, tiled=True)
    start_norm = jnp.sqrt(square_sum(residual_full))
    start_scale = jnp.concatenate([start_norm, start_norm])[None, :]
    basis_one = residual / start_scale
    basis_one_full = residual_full / start_scale
    image_one = apply_adjoint(basis_one_full, basis_one)
    image_one_full = lax.all_gather(image_one, axes, axis=0, tiled=True)
    first_re, first_im = inner_parts(basis_one_full, image_one_full, zone_count)
    lean_one_full = image_one_full - complex_scale(first_re, first_im, basis_one_full, zone_count)
    lean_one = image_one - complex_scale(first_re, first_im, basis_one, zone_count)
    first_norm = jnp.sqrt(square_sum(lean_one_full))
    first_scale = jnp.concatenate([first_norm, first_norm])[None, :]
    basis_two = lean_one / first_scale
    basis_two_full = lean_one_full / first_scale
    image_two = apply_adjoint(basis_two_full, basis_two)
    image_two_full = lax.all_gather(image_two, axes, axis=0, tiled=True)
    cross_re, cross_im = inner_parts(basis_one_full, image_two_full, zone_count)
    second_re, second_im = inner_parts(basis_two_full, image_two_full, zone_count)
    lean_two_full = (
        image_two_full
        - complex_scale(cross_re, cross_im, basis_one_full, zone_count)
        - complex_scale(second_re, second_im, basis_two_full, zone_count)
    )
    second_norm = jnp.sqrt(square_sum(lean_two_full))
    coef_one_re, coef_one_im, coef_two_re, coef_two_im = least_squares(
        start_norm,
        first_re,
        first_im,
        first_norm,
        cross_re,
        cross_im,
        second_re,
        second_im,
        second_norm,
    )
    adjoint_field = (
        adjoint_start
        + complex_scale(coef_one_re, coef_one_im, basis_one, zone_count)
        + complex_scale(coef_two_re, coef_two_im, basis_two, zone_count)
    )
    field_full = (
        start_full
        + complex_scale(coef_one_re, coef_one_im, basis_one_full, zone_count)
        + complex_scale(coef_two_re, coef_two_im, basis_two_full, zone_count)
    )

    def slope_block(start, size):
        rows_xyz = lax.dynamic_slice_in_dim(all_xyz, start, size, 1)
        rows_area = lax.dynamic_slice_in_dim(all_area, start, size, 0)
        rows_vec = lax.dynamic_slice_in_dim(field_full, start, size, 0)
        slope_re, slope_im = slope_parts_t(
            centers, panel_areas, displacement, rows_xyz, rows_area, wave_value
        )
        left_part = jnp.dot(slope_re, rows_vec, precision=highest)
        right_part = jnp.dot(slope_im, rows_vec, precision=highest)
        return jnp.concatenate(
            [
                left_part[:, :zone_count] + right_part[:, zone_count:],
                right_part[:, :zone_count] - left_part[:, zone_count:],
            ],
            1,
        )

    contracted = rows_sum(slope_block, panel_total, limit)
    contrib = panel_areas[:, None] * (
        primal_field[0][:, None] * contracted[:, :zone_count]
        - primal_field[1][:, None] * contracted[:, zone_count:]
    )
    onehot = (design_ids[:, None] == jnp.arange(DESIGN, dtype=jnp.int32)[None, :]).astype(
        jnp.float32
    )
    local_sums = contract_first(contrib, onehot)
    sensitivity = lax.psum(local_sums, axes)
    return (adjoint_field, sensitivity)


def solution(mesh):
    return jax.shard_map(
        local,
        mesh=mesh,
        in_specs=(
            P(None, ("row", "col")),
            P(("row", "col")),
            P(("row", "col")),
            P(None, ("row", "col")),
            P(("row", "col")),
            P(None, ("row", "col")),
            P(("row", "col"), None),
            P(),
            P(),
        ),
        out_specs=(P(("row", "col"), None), P()),
        check_vma=False,
    )
```

```python
import functools
import math

import jax
import jax.numpy as jnp
from jax import lax
from jax.experimental import pallas as pl
from jax.experimental.pallas import tpu as pltpu
from jax.sharding import PartitionSpec as P

DESIGN = 128


highest = lax.Precision.HIGHEST
four_pi = 4.0 * math.pi


def distances(rows_xyz, rows_area, cols_xyz, cols_area):
    diff_x = rows_xyz[0][:, None] - cols_xyz[0][None, :]
    diff_y = rows_xyz[1][:, None] - cols_xyz[1][None, :]
    diff_z = rows_xyz[2][:, None] - cols_xyz[2][None, :]
    square = (
        diff_x * diff_x
        + diff_y * diff_y
        + diff_z * diff_z
        + 0.5 * (rows_area[:, None] + cols_area[None, :])
    )
    return (diff_x, diff_y, diff_z, jnp.sqrt(square))


def kernel_parts(rows_xyz, rows_area, cols_xyz, cols_area, wave_value):
    radius = distances(rows_xyz, rows_area, cols_xyz, cols_area)[3]
    phase = wave_value * radius
    factor = 1.0 / (four_pi * radius)
    return (jnp.cos(phase) * factor, jnp.sin(phase) * factor)


def slope_parts(rows_xyz, rows_area, cols_xyz, cols_area, cols_move, wave_value):
    diff_x, diff_y, diff_z, radius = distances(rows_xyz, rows_area, cols_xyz, cols_area)
    along_move = (
        diff_x * cols_move[0][None, :]
        + diff_y * cols_move[1][None, :]
        + diff_z * cols_move[2][None, :]
    )
    phase = wave_value * radius
    cosine_part = jnp.cos(phase)
    sine_part = jnp.sin(phase)
    factor = along_move / (four_pi * radius * radius * radius)
    return ((-cosine_part - phase * sine_part) * factor, (phase * cosine_part - sine_part) * factor)


def contract_first(matrix, vector):
    return lax.dot_general(matrix, vector, (((0,), (0,)), ((), ())), precision=highest)


def conj_columns(real_part, imag_part, vector, zone_count):
    left_part = contract_first(real_part, vector)
    right_part = contract_first(imag_part, vector)
    return jnp.concatenate(
        [
            left_part[:, :zone_count] + right_part[:, zone_count:],
            left_part[:, zone_count:] - right_part[:, :zone_count],
        ],
        1,
    )


def inner_parts(left_part, right_part, zone_count):
    left_re, left_im = (left_part[:, :zone_count], left_part[:, zone_count:])
    right_re, right_im = (right_part[:, :zone_count], right_part[:, zone_count:])
    return (
        jnp.sum(left_re * right_re + left_im * right_im, 0),
        jnp.sum(left_re * right_im - left_im * right_re, 0),
    )


def square_sum(vector):
    return jnp.sum(vector * vector, 0).reshape(2, -1).sum(0)


def complex_scale(scale_re, scale_im, vector, zone_count):
    vec_re, vec_im = (vector[:, :zone_count], vector[:, zone_count:])
    return jnp.concatenate(
        [scale_re * vec_re - scale_im * vec_im, scale_re * vec_im + scale_im * vec_re], 1
    )


def least_squares(
    start_norm,
    first_re,
    first_im,
    first_norm,
    cross_re,
    cross_im,
    second_re,
    second_im,
    second_norm,
):
    gram_one = first_re * first_re + first_im * first_im + first_norm * first_norm
    gram_off_re = first_re * cross_re + first_im * cross_im + first_norm * second_re
    gram_off_im = first_re * cross_im - first_im * cross_re + first_norm * second_im
    gram_two = (
        cross_re * cross_re
        + cross_im * cross_im
        + second_re * second_re
        + second_im * second_im
        + second_norm * second_norm
    )
    rhs_one_re = start_norm * first_re
    rhs_one_im = -start_norm * first_im
    rhs_two_re = start_norm * cross_re
    rhs_two_im = -start_norm * cross_im
    determinant = gram_one * gram_two - gram_off_re * gram_off_re - gram_off_im * gram_off_im
    coef_one_re = (
        gram_two * rhs_one_re - (gram_off_re * rhs_two_re - gram_off_im * rhs_two_im)
    ) / determinant
    coef_one_im = (
        gram_two * rhs_one_im - (gram_off_re * rhs_two_im + gram_off_im * rhs_two_re)
    ) / determinant
    coef_two_re = (
        gram_one * rhs_two_re - (gram_off_re * rhs_one_re + gram_off_im * rhs_one_im)
    ) / determinant
    coef_two_im = (
        gram_one * rhs_two_im - (gram_off_re * rhs_one_im - gram_off_im * rhs_one_re)
    ) / determinant
    return (coef_one_re, coef_one_im, coef_two_re, coef_two_im)


def slope_parts_t(own_xyz, own_area, own_move, all_xyz, all_area, wave_value):
    diff_x = all_xyz[0][None, :] - own_xyz[0][:, None]
    diff_y = all_xyz[1][None, :] - own_xyz[1][:, None]
    diff_z = all_xyz[2][None, :] - own_xyz[2][:, None]
    square = (
        diff_x * diff_x
        + diff_y * diff_y
        + diff_z * diff_z
        + 0.5 * (all_area[None, :] + own_area[:, None])
    )
    radius = jnp.sqrt(square)
    along_move = (
        diff_x * own_move[0][:, None]
        + diff_y * own_move[1][:, None]
        + diff_z * own_move[2][:, None]
    )
    phase = wave_value * radius
    cosine_part = jnp.cos(phase)
    sine_part = jnp.sin(phase)
    factor = along_move / (four_pi * radius * radius * radius)
    return ((-cosine_part - phase * sine_part) * factor, (phase * cosine_part - sine_part) * factor)


LANES = 256


def panel_kernel(slope_mode, wave_ref, own_ref, all_ref, vec_ref, out_ref):
    wave_value = wave_ref[0]
    own_total = own_ref.shape[0]
    panel_total = all_ref.shape[1]
    width = LANES if panel_total % LANES == 0 else 128
    chunk_count = panel_total // width

    def row_block(block, carry):
        first = pl.multiple_of(block * 8, 8)
        own = own_ref[pl.ds(first, 8), :]
        own_x = jnp.broadcast_to(own[:, 0:1], (8, width))
        own_y = jnp.broadcast_to(own[:, 1:2], (8, width))
        own_z = jnp.broadcast_to(own[:, 2:3], (8, width))
        own_a = jnp.broadcast_to(own[:, 3:4], (8, width))
        if slope_mode:
            move_x = jnp.broadcast_to(own[:, 4:5], (8, width))
            move_y = jnp.broadcast_to(own[:, 5:6], (8, width))
            move_z = jnp.broadcast_to(own[:, 6:7], (8, width))

        def lane_block(chunk, sums):
            start = pl.multiple_of(chunk * width, width)
            span = pl.ds(start, width)
            diff_x = all_ref[0:1, span] - own_x
            diff_y = all_ref[1:2, span] - own_y
            diff_z = all_ref[2:3, span] - own_z
            square = (
                diff_x * diff_x
                + diff_y * diff_y
                + diff_z * diff_z
                + 0.5 * (all_ref[3:4, span] + own_a)
            )
            radius = jnp.sqrt(square)
            phase = wave_value * radius
            cosine_part = jnp.cos(phase)
            sine_part = jnp.sin(phase)
            if slope_mode:
                along_move = diff_x * move_x + diff_y * move_y + diff_z * move_z
                factor = along_move / (four_pi * radius * radius * radius)
                first_part = (-cosine_part - phase * sine_part) * factor
                second_part = (phase * cosine_part - sine_part) * factor
            else:
                factor = 1.0 / (four_pi * radius)
                first_part = cosine_part * factor
                second_part = sine_part * factor
            zone_count = len(sums) // 2
            new_re = []
            new_im = []
            for zone in range(zone_count):
                vec_re = vec_ref[zone:zone + 1, span]
                vec_im = vec_ref[zone_count + zone:zone_count + zone + 1, span]
                new_re.append(sums[zone] + first_part * vec_re + second_part * vec_im)
                if slope_mode:
                    new_im.append(sums[zone_count + zone] + second_part * vec_re - first_part * vec_im)
                else:
                    new_im.append(sums[zone_count + zone] + first_part * vec_im - second_part * vec_re)
            return tuple(new_re + new_im)

        columns = vec_ref.shape[0]
        zeros = tuple(jnp.zeros((8, width), jnp.float32) for _ in range(columns))
        sums = lax.fori_loop(0, chunk_count, lane_block, zeros)
        lane = lax.broadcasted_iota(jnp.int32, (8, columns), 1)
        result = jnp.zeros((8, columns), jnp.float32)
        for column in range(columns):
            total = jnp.sum(sums[column], axis=1, keepdims=True)
            result = jnp.where(lane == column, total, result)
        out_ref[pl.ds(first, 8), :] = result
        return carry

    lax.fori_loop(0, own_total // 8, row_block, 0)


def panel_contract(slope_mode, wavenumber, own_table, all_table, vector_rows):
    own_total = own_table.shape[0]
    columns = vector_rows.shape[0]
    panel_total = all_table.shape[1]
    elements = own_total * panel_total
    return pl.pallas_call(
        functools.partial(panel_kernel, slope_mode),
        out_shape=jax.ShapeDtypeStruct((own_total, columns), jnp.float32),
        in_specs=[
            pl.BlockSpec(memory_space=pltpu.SMEM),
            pl.BlockSpec(memory_space=pltpu.VMEM),
            pl.BlockSpec(memory_space=pltpu.VMEM),
            pl.BlockSpec(memory_space=pltpu.VMEM),
        ],
        out_specs=pl.BlockSpec(memory_space=pltpu.VMEM),
        cost_estimate=pl.CostEstimate(
            flops=150 * elements,
            transcendentals=4 * elements,
            bytes_accessed=4 * (own_table.size + all_table.size + vector_rows.size + own_total * columns),
        ),
    )(wavenumber, own_table, all_table, vector_rows)


def chunk_size_of(count, limit):
    return math.gcd(count, limit)


def rows_sum(block_fn, count, limit):
    size = chunk_size_of(count, limit)
    starts = jnp.arange(count // size, dtype=jnp.int32) * size
    return jnp.sum(lax.map(lambda start: block_fn(start, size), starts), 0)


def local(
    centers,
    panel_areas,
    jump_term,
    displacement,
    design_ids,
    primal_field,
    adjoint_start,
    mic_panels,
    wavenumber,
):
    zone_count = adjoint_start.shape[1] // 2
    owned_count = centers.shape[1]
    axes = ("row", "col")
    wave_value = wavenumber[0]
    packed = jnp.concatenate([centers.T, panel_areas[:, None], adjoint_start], 1)
    gathered = lax.all_gather(packed, axes, axis=0, tiled=True)
    panel_total = gathered.shape[0]
    all_xyz = gathered[:, :3].T
    all_area = gathered[:, 3]
    start_full = gathered[:, 4:]
    all_table = gathered[:, :4].T
    own_table = jnp.concatenate(
        [centers.T, panel_areas[:, None], displacement.T, jnp.zeros((owned_count, 1), jnp.float32)], 1
    )

    def apply_adjoint(vector_full, vector_own):
        summed = panel_contract(False, wavenumber, own_table, all_table, vector_full.T)
        return panel_areas[:, None] * summed + jump_term[:, None] * vector_own

    first_panel = (
        lax.axis_index("row") * lax.axis_size("col") + lax.axis_index("col")
    ) * owned_count
    panel_ids = first_panel + jnp.arange(owned_count, dtype=jnp.int32)
    mic_hits = jnp.sum(
        (panel_ids[:, None, None] == mic_panels[None, :, :]).astype(jnp.float32), axis=2
    )
    right_side = jnp.concatenate(
        [mic_hits * primal_field[0][:, None], mic_hits * primal_field[1][:, None]], 1
    )
    residual = right_side - apply_adjoint(start_full, adjoint_start)
    residual_full = lax.all_gather(residual, axes, axis=0, tiled=True)
    start_norm = jnp.sqrt(square_sum(residual_full))
    start_scale = jnp.concatenate([start_norm, start_norm])[None, :]
    basis_one = residual / start_scale
    basis_one_full = residual_full / start_scale
    image_one = apply_adjoint(basis_one_full, basis_one)
    image_one_full = lax.all_gather(image_one, axes, axis=0, tiled=True)
    first_re, first_im = inner_parts(basis_one_full, image_one_full, zone_count)
    lean_one_full = image_one_full - complex_scale(first_re, first_im, basis_one_full, zone_count)
    lean_one = image_one - complex_scale(first_re, first_im, basis_one, zone_count)
    first_norm = jnp.sqrt(square_sum(lean_one_full))
    first_scale = jnp.concatenate([first_norm, first_norm])[None, :]
    basis_two = lean_one / first_scale
    basis_two_full = lean_one_full / first_scale
    image_two = apply_adjoint(basis_two_full, basis_two)
    image_two_full = lax.all_gather(image_two, axes, axis=0, tiled=True)
    cross_re, cross_im = inner_parts(basis_one_full, image_two_full, zone_count)
    second_re, second_im = inner_parts(basis_two_full, image_two_full, zone_count)
    lean_two_full = (
        image_two_full
        - complex_scale(cross_re, cross_im, basis_one_full, zone_count)
        - complex_scale(second_re, second_im, basis_two_full, zone_count)
    )
    second_norm = jnp.sqrt(square_sum(lean_two_full))
    coef_one_re, coef_one_im, coef_two_re, coef_two_im = least_squares(
        start_norm,
        first_re,
        first_im,
        first_norm,
        cross_re,
        cross_im,
        second_re,
        second_im,
        second_norm,
    )
    adjoint_field = (
        adjoint_start
        + complex_scale(coef_one_re, coef_one_im, basis_one, zone_count)
        + complex_scale(coef_two_re, coef_two_im, basis_two, zone_count)
    )
    field_full = (
        start_full
        + complex_scale(coef_one_re, coef_one_im, basis_one_full, zone_count)
        + complex_scale(coef_two_re, coef_two_im, basis_two_full, zone_count)
    )

    contracted = panel_contract(True, wavenumber, own_table, all_table, field_full.T)
    contrib = panel_areas[:, None] * (
        primal_field[0][:, None] * contracted[:, :zone_count]
        - primal_field[1][:, None] * contracted[:, zone_count:]
    )
    onehot = (design_ids[:, None] == jnp.arange(DESIGN, dtype=jnp.int32)[None, :]).astype(
        jnp.float32
    )
    local_sums = contract_first(contrib, onehot)
    sensitivity = lax.psum(local_sums, axes)
    return (adjoint_field, sensitivity)


def solution(mesh):
    return jax.shard_map(
        local,
        mesh=mesh,
        in_specs=(
            P(None, ("row", "col")),
            P(("row", "col")),
            P(("row", "col")),
            P(None, ("row", "col")),
            P(("row", "col")),
            P(None, ("row", "col")),
            P(("row", "col"), None),
            P(),
            P(),
        ),
        out_specs=(P(("row", "col"), None), P()),
        check_vma=False,
    )
```

```python
import functools
import math

import jax
import jax.numpy as jnp
from jax import lax
from jax.experimental import pallas as pl
from jax.experimental.pallas import tpu as pltpu
from jax.sharding import PartitionSpec as P

DESIGN = 128


highest = lax.Precision.HIGHEST
four_pi = 4.0 * math.pi


def distances(rows_xyz, rows_area, cols_xyz, cols_area):
    diff_x = rows_xyz[0][:, None] - cols_xyz[0][None, :]
    diff_y = rows_xyz[1][:, None] - cols_xyz[1][None, :]
    diff_z = rows_xyz[2][:, None] - cols_xyz[2][None, :]
    square = (
        diff_x * diff_x
        + diff_y * diff_y
        + diff_z * diff_z
        + 0.5 * (rows_area[:, None] + cols_area[None, :])
    )
    return (diff_x, diff_y, diff_z, jnp.sqrt(square))


def kernel_parts(rows_xyz, rows_area, cols_xyz, cols_area, wave_value):
    radius = distances(rows_xyz, rows_area, cols_xyz, cols_area)[3]
    phase = wave_value * radius
    factor = 1.0 / (four_pi * radius)
    return (jnp.cos(phase) * factor, jnp.sin(phase) * factor)


def slope_parts(rows_xyz, rows_area, cols_xyz, cols_area, cols_move, wave_value):
    diff_x, diff_y, diff_z, radius = distances(rows_xyz, rows_area, cols_xyz, cols_area)
    along_move = (
        diff_x * cols_move[0][None, :]
        + diff_y * cols_move[1][None, :]
        + diff_z * cols_move[2][None, :]
    )
    phase = wave_value * radius
    cosine_part = jnp.cos(phase)
    sine_part = jnp.sin(phase)
    factor = along_move / (four_pi * radius * radius * radius)
    return ((-cosine_part - phase * sine_part) * factor, (phase * cosine_part - sine_part) * factor)


def contract_first(matrix, vector):
    return lax.dot_general(matrix, vector, (((0,), (0,)), ((), ())), precision=highest)


def conj_columns(real_part, imag_part, vector, zone_count):
    left_part = contract_first(real_part, vector)
    right_part = contract_first(imag_part, vector)
    return jnp.concatenate(
        [
            left_part[:, :zone_count] + right_part[:, zone_count:],
            left_part[:, zone_count:] - right_part[:, :zone_count],
        ],
        1,
    )


def inner_parts(left_part, right_part, zone_count):
    left_re, left_im = (left_part[:, :zone_count], left_part[:, zone_count:])
    right_re, right_im = (right_part[:, :zone_count], right_part[:, zone_count:])
    return (
        jnp.sum(left_re * right_re + left_im * right_im, 0),
        jnp.sum(left_re * right_im - left_im * right_re, 0),
    )


def square_sum(vector):
    return jnp.sum(vector * vector, 0).reshape(2, -1).sum(0)


def complex_scale(scale_re, scale_im, vector, zone_count):
    vec_re, vec_im = (vector[:, :zone_count], vector[:, zone_count:])
    return jnp.concatenate(
        [scale_re * vec_re - scale_im * vec_im, scale_re * vec_im + scale_im * vec_re], 1
    )


def least_squares(
    start_norm,
    first_re,
    first_im,
    first_norm,
    cross_re,
    cross_im,
    second_re,
    second_im,
    second_norm,
):
    gram_one = first_re * first_re + first_im * first_im + first_norm * first_norm
    gram_off_re = first_re * cross_re + first_im * cross_im + first_norm * second_re
    gram_off_im = first_re * cross_im - first_im * cross_re + first_norm * second_im
    gram_two = (
        cross_re * cross_re
        + cross_im * cross_im
        + second_re * second_re
        + second_im * second_im
        + second_norm * second_norm
    )
    rhs_one_re = start_norm * first_re
    rhs_one_im = -start_norm * first_im
    rhs_two_re = start_norm * cross_re
    rhs_two_im = -start_norm * cross_im
    determinant = gram_one * gram_two - gram_off_re * gram_off_re - gram_off_im * gram_off_im
    coef_one_re = (
        gram_two * rhs_one_re - (gram_off_re * rhs_two_re - gram_off_im * rhs_two_im)
    ) / determinant
    coef_one_im = (
        gram_two * rhs_one_im - (gram_off_re * rhs_two_im + gram_off_im * rhs_two_re)
    ) / determinant
    coef_two_re = (
        gram_one * rhs_two_re - (gram_off_re * rhs_one_re + gram_off_im * rhs_one_im)
    ) / determinant
    coef_two_im = (
        gram_one * rhs_two_im - (gram_off_re * rhs_one_im - gram_off_im * rhs_one_re)
    ) / determinant
    return (coef_one_re, coef_one_im, coef_two_re, coef_two_im)


def slope_parts_t(own_xyz, own_area, own_move, all_xyz, all_area, wave_value):
    diff_x = all_xyz[0][None, :] - own_xyz[0][:, None]
    diff_y = all_xyz[1][None, :] - own_xyz[1][:, None]
    diff_z = all_xyz[2][None, :] - own_xyz[2][:, None]
    square = (
        diff_x * diff_x
        + diff_y * diff_y
        + diff_z * diff_z
        + 0.5 * (all_area[None, :] + own_area[:, None])
    )
    radius = jnp.sqrt(square)
    along_move = (
        diff_x * own_move[0][:, None]
        + diff_y * own_move[1][:, None]
        + diff_z * own_move[2][:, None]
    )
    phase = wave_value * radius
    cosine_part = jnp.cos(phase)
    sine_part = jnp.sin(phase)
    factor = along_move / (four_pi * radius * radius * radius)
    return ((-cosine_part - phase * sine_part) * factor, (phase * cosine_part - sine_part) * factor)


LANES = 256
STORE_LIMIT = 24 * 1024 * 1024


def panel_kernel(slope_mode, stored_in, store_out, wave_ref, own_ref, all_ref, vec_ref, *refs):
    if stored_in:
        real_ref, imag_ref, out_ref = refs
    elif store_out:
        out_ref, real_ref, imag_ref = refs
    else:
        (out_ref,) = refs
    wave_value = wave_ref[0]
    own_total = own_ref.shape[0]
    panel_total = all_ref.shape[1]
    width = LANES if panel_total % LANES == 0 else 128
    chunk_count = panel_total // width
    needs_geometry = slope_mode or not stored_in

    def row_block(block, carry):
        first = pl.multiple_of(block * 8, 8)
        rows = pl.ds(first, 8)
        own = own_ref[rows, :]
        own_x = jnp.broadcast_to(own[:, 0:1], (8, width))
        own_y = jnp.broadcast_to(own[:, 1:2], (8, width))
        own_z = jnp.broadcast_to(own[:, 2:3], (8, width))
        own_a = jnp.broadcast_to(own[:, 3:4], (8, width))
        if slope_mode:
            move_x = jnp.broadcast_to(own[:, 4:5], (8, width))
            move_y = jnp.broadcast_to(own[:, 5:6], (8, width))
            move_z = jnp.broadcast_to(own[:, 6:7], (8, width))

        def lane_block(chunk, sums):
            start = pl.multiple_of(chunk * width, width)
            span = pl.ds(start, width)
            if needs_geometry:
                diff_x = all_ref[0:1, span] - own_x
                diff_y = all_ref[1:2, span] - own_y
                diff_z = all_ref[2:3, span] - own_z
                square = (
                    diff_x * diff_x
                    + diff_y * diff_y
                    + diff_z * diff_z
                    + 0.5 * (all_ref[3:4, span] + own_a)
                )
                radius = jnp.sqrt(square)
                phase = wave_value * radius
            if stored_in:
                real_part = real_ref[rows, span]
                imag_part = imag_ref[rows, span]
                if slope_mode:
                    along_move = diff_x * move_x + diff_y * move_y + diff_z * move_z
                    factor = along_move / square
                    first_part = (-real_part - phase * imag_part) * factor
                    second_part = (phase * real_part - imag_part) * factor
                else:
                    first_part = real_part
                    second_part = imag_part
            else:
                cosine_part = jnp.cos(phase)
                sine_part = jnp.sin(phase)
                if slope_mode:
                    along_move = diff_x * move_x + diff_y * move_y + diff_z * move_z
                    factor = along_move / (four_pi * radius * radius * radius)
                    first_part = (-cosine_part - phase * sine_part) * factor
                    second_part = (phase * cosine_part - sine_part) * factor
                else:
                    factor = 1.0 / (four_pi * radius)
                    first_part = cosine_part * factor
                    second_part = sine_part * factor
                if store_out:
                    real_ref[rows, span] = first_part
                    imag_ref[rows, span] = second_part
            zone_count = len(sums) // 2
            new_re = []
            new_im = []
            for zone in range(zone_count):
                vec_re = vec_ref[zone:zone + 1, span]
                vec_im = vec_ref[zone_count + zone:zone_count + zone + 1, span]
                new_re.append(sums[zone] + first_part * vec_re + second_part * vec_im)
                if slope_mode:
                    new_im.append(sums[zone_count + zone] + second_part * vec_re - first_part * vec_im)
                else:
                    new_im.append(sums[zone_count + zone] + first_part * vec_im - second_part * vec_re)
            return tuple(new_re + new_im)

        columns = vec_ref.shape[0]
        zeros = tuple(jnp.zeros((8, width), jnp.float32) for _ in range(columns))
        sums = lax.fori_loop(0, chunk_count, lane_block, zeros)
        lane = lax.broadcasted_iota(jnp.int32, (8, columns), 1)
        result = jnp.zeros((8, columns), jnp.float32)
        for column in range(columns):
            total = jnp.sum(sums[column], axis=1, keepdims=True)
            result = jnp.where(lane == column, total, result)
        out_ref[rows, :] = result
        return carry

    lax.fori_loop(0, own_total // 8, row_block, 0)


def panel_contract(slope_mode, wavenumber, own_table, all_table, vector_rows, stored=None, store_out=False):
    own_total = own_table.shape[0]
    columns = vector_rows.shape[0]
    panel_total = all_table.shape[1]
    elements = own_total * panel_total
    stored_in = stored is not None
    operands = [wavenumber, own_table, all_table, vector_rows]
    out_shape = [jax.ShapeDtypeStruct((own_total, columns), jnp.float32)]
    matrix_bytes = 0
    if stored_in:
        operands += list(stored)
        matrix_bytes = 8 * elements
    if store_out:
        out_shape += [jax.ShapeDtypeStruct((own_total, panel_total), jnp.float32)] * 2
        matrix_bytes = 8 * elements
    vmem = pl.BlockSpec(memory_space=pltpu.VMEM)
    params = {}
    if matrix_bytes:
        params["compiler_params"] = pltpu.CompilerParams(vmem_limit_bytes=matrix_bytes + 16 * 1024 * 1024)
    if stored_in and not slope_mode:
        flops, transcendentals = 32 * elements, 0
    elif stored_in:
        flops, transcendentals = 60 * elements, 2 * elements
    else:
        flops, transcendentals = 150 * elements, 4 * elements
    return pl.pallas_call(
        functools.partial(panel_kernel, slope_mode, stored_in, store_out),
        out_shape=tuple(out_shape) if store_out else out_shape[0],
        in_specs=[pl.BlockSpec(memory_space=pltpu.SMEM)] + [vmem] * (len(operands) - 1),
        out_specs=tuple([vmem] * len(out_shape)) if store_out else vmem,
        cost_estimate=pl.CostEstimate(
            flops=flops,
            transcendentals=transcendentals,
            bytes_accessed=4 * (own_table.size + all_table.size + vector_rows.size + own_total * columns) + matrix_bytes,
        ),
        **params,
    )(*operands)


def chunk_size_of(count, limit):
    return math.gcd(count, limit)


def rows_sum(block_fn, count, limit):
    size = chunk_size_of(count, limit)
    starts = jnp.arange(count // size, dtype=jnp.int32) * size
    return jnp.sum(lax.map(lambda start: block_fn(start, size), starts), 0)


def local(
    centers,
    panel_areas,
    jump_term,
    displacement,
    design_ids,
    primal_field,
    adjoint_start,
    mic_panels,
    wavenumber,
):
    zone_count = adjoint_start.shape[1] // 2
    owned_count = centers.shape[1]
    axes = ("row", "col")
    wave_value = wavenumber[0]
    packed = jnp.concatenate([centers.T, panel_areas[:, None], adjoint_start], 1)
    gathered = lax.all_gather(packed, axes, axis=0, tiled=True)
    panel_total = gathered.shape[0]
    all_xyz = gathered[:, :3].T
    all_area = gathered[:, 3]
    start_full = gathered[:, 4:]
    all_table = gathered[:, :4].T
    own_table = jnp.concatenate(
        [centers.T, panel_areas[:, None], displacement.T, jnp.zeros((owned_count, 1), jnp.float32)], 1
    )

    store = 8 * owned_count * panel_total <= STORE_LIMIT
    saved = []

    def apply_adjoint(vector_full, vector_own):
        if store and saved:
            summed = panel_contract(False, wavenumber, own_table, all_table, vector_full.T, stored=saved)
        elif store:
            summed, real_part, imag_part = panel_contract(
                False, wavenumber, own_table, all_table, vector_full.T, store_out=True
            )
            saved.extend([real_part, imag_part])
        else:
            summed = panel_contract(False, wavenumber, own_table, all_table, vector_full.T)
        return panel_areas[:, None] * summed + jump_term[:, None] * vector_own

    first_panel = (
        lax.axis_index("row") * lax.axis_size("col") + lax.axis_index("col")
    ) * owned_count
    panel_ids = first_panel + jnp.arange(owned_count, dtype=jnp.int32)
    mic_hits = jnp.sum(
        (panel_ids[:, None, None] == mic_panels[None, :, :]).astype(jnp.float32), axis=2
    )
    right_side = jnp.concatenate(
        [mic_hits * primal_field[0][:, None], mic_hits * primal_field[1][:, None]], 1
    )
    residual = right_side - apply_adjoint(start_full, adjoint_start)
    residual_full = lax.all_gather(residual, axes, axis=0, tiled=True)
    start_norm = jnp.sqrt(square_sum(residual_full))
    start_scale = jnp.concatenate([start_norm, start_norm])[None, :]
    basis_one = residual / start_scale
    basis_one_full = residual_full / start_scale
    image_one = apply_adjoint(basis_one_full, basis_one)
    image_one_full = lax.all_gather(image_one, axes, axis=0, tiled=True)
    first_re, first_im = inner_parts(basis_one_full, image_one_full, zone_count)
    lean_one_full = image_one_full - complex_scale(first_re, first_im, basis_one_full, zone_count)
    lean_one = image_one - complex_scale(first_re, first_im, basis_one, zone_count)
    first_norm = jnp.sqrt(square_sum(lean_one_full))
    first_scale = jnp.concatenate([first_norm, first_norm])[None, :]
    basis_two = lean_one / first_scale
    basis_two_full = lean_one_full / first_scale
    image_two = apply_adjoint(basis_two_full, basis_two)
    image_two_full = lax.all_gather(image_two, axes, axis=0, tiled=True)
    cross_re, cross_im = inner_parts(basis_one_full, image_two_full, zone_count)
    second_re, second_im = inner_parts(basis_two_full, image_two_full, zone_count)
    lean_two_full = (
        image_two_full
        - complex_scale(cross_re, cross_im, basis_one_full, zone_count)
        - complex_scale(second_re, second_im, basis_two_full, zone_count)
    )
    second_norm = jnp.sqrt(square_sum(lean_two_full))
    coef_one_re, coef_one_im, coef_two_re, coef_two_im = least_squares(
        start_norm,
        first_re,
        first_im,
        first_norm,
        cross_re,
        cross_im,
        second_re,
        second_im,
        second_norm,
    )
    adjoint_field = (
        adjoint_start
        + complex_scale(coef_one_re, coef_one_im, basis_one, zone_count)
        + complex_scale(coef_two_re, coef_two_im, basis_two, zone_count)
    )
    field_full = (
        start_full
        + complex_scale(coef_one_re, coef_one_im, basis_one_full, zone_count)
        + complex_scale(coef_two_re, coef_two_im, basis_two_full, zone_count)
    )

    contracted = panel_contract(True, wavenumber, own_table, all_table, field_full.T, stored=saved or None)
    contrib = panel_areas[:, None] * (
        primal_field[0][:, None] * contracted[:, :zone_count]
        - primal_field[1][:, None] * contracted[:, zone_count:]
    )
    onehot = (design_ids[:, None] == jnp.arange(DESIGN, dtype=jnp.int32)[None, :]).astype(
        jnp.float32
    )
    local_sums = contract_first(contrib, onehot)
    sensitivity = lax.psum(local_sums, axes)
    return (adjoint_field, sensitivity)


def solution(mesh):
    return jax.shard_map(
        local,
        mesh=mesh,
        in_specs=(
            P(None, ("row", "col")),
            P(("row", "col")),
            P(("row", "col")),
            P(None, ("row", "col")),
            P(("row", "col")),
            P(None, ("row", "col")),
            P(("row", "col"), None),
            P(),
            P(),
        ),
        out_specs=(P(("row", "col"), None), P()),
        check_vma=False,
    )
```

```python
import functools
import math

import jax
import jax.numpy as jnp
from jax import lax
from jax.experimental import pallas as pl
from jax.experimental.pallas import tpu as pltpu
from jax.sharding import PartitionSpec as P

DESIGN = 128


highest = lax.Precision.HIGHEST
four_pi = 4.0 * math.pi


def distances(rows_xyz, rows_area, cols_xyz, cols_area):
    diff_x = rows_xyz[0][:, None] - cols_xyz[0][None, :]
    diff_y = rows_xyz[1][:, None] - cols_xyz[1][None, :]
    diff_z = rows_xyz[2][:, None] - cols_xyz[2][None, :]
    square = (
        diff_x * diff_x
        + diff_y * diff_y
        + diff_z * diff_z
        + 0.5 * (rows_area[:, None] + cols_area[None, :])
    )
    return (diff_x, diff_y, diff_z, jnp.sqrt(square))


def kernel_parts(rows_xyz, rows_area, cols_xyz, cols_area, wave_value):
    radius = distances(rows_xyz, rows_area, cols_xyz, cols_area)[3]
    phase = wave_value * radius
    factor = 1.0 / (four_pi * radius)
    return (jnp.cos(phase) * factor, jnp.sin(phase) * factor)


def slope_parts(rows_xyz, rows_area, cols_xyz, cols_area, cols_move, wave_value):
    diff_x, diff_y, diff_z, radius = distances(rows_xyz, rows_area, cols_xyz, cols_area)
    along_move = (
        diff_x * cols_move[0][None, :]
        + diff_y * cols_move[1][None, :]
        + diff_z * cols_move[2][None, :]
    )
    phase = wave_value * radius
    cosine_part = jnp.cos(phase)
    sine_part = jnp.sin(phase)
    factor = along_move / (four_pi * radius * radius * radius)
    return ((-cosine_part - phase * sine_part) * factor, (phase * cosine_part - sine_part) * factor)


def contract_first(matrix, vector):
    return lax.dot_general(matrix, vector, (((0,), (0,)), ((), ())), precision=highest)


def conj_columns(real_part, imag_part, vector, zone_count):
    left_part = contract_first(real_part, vector)
    right_part = contract_first(imag_part, vector)
    return jnp.concatenate(
        [
            left_part[:, :zone_count] + right_part[:, zone_count:],
            left_part[:, zone_count:] - right_part[:, :zone_count],
        ],
        1,
    )


def inner_parts(left_part, right_part, zone_count):
    left_re, left_im = (left_part[:, :zone_count], left_part[:, zone_count:])
    right_re, right_im = (right_part[:, :zone_count], right_part[:, zone_count:])
    return (
        jnp.sum(left_re * right_re + left_im * right_im, 0),
        jnp.sum(left_re * right_im - left_im * right_re, 0),
    )


def square_sum(vector):
    return jnp.sum(vector * vector, 0).reshape(2, -1).sum(0)


def complex_scale(scale_re, scale_im, vector, zone_count):
    vec_re, vec_im = (vector[:, :zone_count], vector[:, zone_count:])
    return jnp.concatenate(
        [scale_re * vec_re - scale_im * vec_im, scale_re * vec_im + scale_im * vec_re], 1
    )


def least_squares(
    start_norm,
    first_re,
    first_im,
    first_norm,
    cross_re,
    cross_im,
    second_re,
    second_im,
    second_norm,
):
    gram_one = first_re * first_re + first_im * first_im + first_norm * first_norm
    gram_off_re = first_re * cross_re + first_im * cross_im + first_norm * second_re
    gram_off_im = first_re * cross_im - first_im * cross_re + first_norm * second_im
    gram_two = (
        cross_re * cross_re
        + cross_im * cross_im
        + second_re * second_re
        + second_im * second_im
        + second_norm * second_norm
    )
    rhs_one_re = start_norm * first_re
    rhs_one_im = -start_norm * first_im
    rhs_two_re = start_norm * cross_re
    rhs_two_im = -start_norm * cross_im
    determinant = gram_one * gram_two - gram_off_re * gram_off_re - gram_off_im * gram_off_im
    coef_one_re = (
        gram_two * rhs_one_re - (gram_off_re * rhs_two_re - gram_off_im * rhs_two_im)
    ) / determinant
    coef_one_im = (
        gram_two * rhs_one_im - (gram_off_re * rhs_two_im + gram_off_im * rhs_two_re)
    ) / determinant
    coef_two_re = (
        gram_one * rhs_two_re - (gram_off_re * rhs_one_re + gram_off_im * rhs_one_im)
    ) / determinant
    coef_two_im = (
        gram_one * rhs_two_im - (gram_off_re * rhs_one_im - gram_off_im * rhs_one_re)
    ) / determinant
    return (coef_one_re, coef_one_im, coef_two_re, coef_two_im)


def slope_parts_t(own_xyz, own_area, own_move, all_xyz, all_area, wave_value):
    diff_x = all_xyz[0][None, :] - own_xyz[0][:, None]
    diff_y = all_xyz[1][None, :] - own_xyz[1][:, None]
    diff_z = all_xyz[2][None, :] - own_xyz[2][:, None]
    square = (
        diff_x * diff_x
        + diff_y * diff_y
        + diff_z * diff_z
        + 0.5 * (all_area[None, :] + own_area[:, None])
    )
    radius = jnp.sqrt(square)
    along_move = (
        diff_x * own_move[0][:, None]
        + diff_y * own_move[1][:, None]
        + diff_z * own_move[2][:, None]
    )
    phase = wave_value * radius
    cosine_part = jnp.cos(phase)
    sine_part = jnp.sin(phase)
    factor = along_move / (four_pi * radius * radius * radius)
    return ((-cosine_part - phase * sine_part) * factor, (phase * cosine_part - sine_part) * factor)


LANES = 256
STORE_LIMIT = 24 * 1024 * 1024


def panel_kernel(slope_mode, stored_in, store_out, wave_ref, own_ref, all_ref, vec_ref, *refs):
    if stored_in:
        real_ref, imag_ref, out_ref = refs
    elif store_out:
        out_ref, real_ref, imag_ref = refs
    else:
        (out_ref,) = refs
    wave_value = wave_ref[0]
    own_total = own_ref.shape[0]
    panel_total = all_ref.shape[1]
    width = LANES if panel_total % LANES == 0 else 128
    chunk_count = panel_total // width
    needs_geometry = slope_mode or not stored_in

    def row_block(block, carry):
        first = pl.multiple_of(block * 8, 8)
        rows = pl.ds(first, 8)
        own = own_ref[rows, :]
        own_x = jnp.broadcast_to(own[:, 0:1], (8, width))
        own_y = jnp.broadcast_to(own[:, 1:2], (8, width))
        own_z = jnp.broadcast_to(own[:, 2:3], (8, width))
        own_a = jnp.broadcast_to(own[:, 3:4], (8, width))
        if slope_mode:
            move_x = jnp.broadcast_to(own[:, 4:5], (8, width))
            move_y = jnp.broadcast_to(own[:, 5:6], (8, width))
            move_z = jnp.broadcast_to(own[:, 6:7], (8, width))

        def lane_block(chunk, sums):
            start = pl.multiple_of(chunk * width, width)
            span = pl.ds(start, width)
            if needs_geometry:
                diff_x = all_ref[0:1, span] - own_x
                diff_y = all_ref[1:2, span] - own_y
                diff_z = all_ref[2:3, span] - own_z
                square = (
                    diff_x * diff_x
                    + diff_y * diff_y
                    + diff_z * diff_z
                    + 0.5 * (all_ref[3:4, span] + own_a)
                )
                radius = jnp.sqrt(square)
                phase = wave_value * radius
            if stored_in:
                real_part = real_ref[rows, span]
                imag_part = imag_ref[rows, span]
                if slope_mode:
                    along_move = diff_x * move_x + diff_y * move_y + diff_z * move_z
                    factor = along_move / square
                    first_part = (-real_part - phase * imag_part) * factor
                    second_part = (phase * real_part - imag_part) * factor
                else:
                    first_part = real_part
                    second_part = imag_part
            else:
                cosine_part = jnp.cos(phase)
                sine_part = jnp.sin(phase)
                if slope_mode:
                    along_move = diff_x * move_x + diff_y * move_y + diff_z * move_z
                    factor = along_move / (four_pi * radius * radius * radius)
                    first_part = (-cosine_part - phase * sine_part) * factor
                    second_part = (phase * cosine_part - sine_part) * factor
                else:
                    factor = 1.0 / (four_pi * radius)
                    first_part = cosine_part * factor
                    second_part = sine_part * factor
                if store_out:
                    real_ref[rows, span] = first_part
                    imag_ref[rows, span] = second_part
            zone_count = len(sums) // 2
            new_re = []
            new_im = []
            for zone in range(zone_count):
                vec_re = vec_ref[zone:zone + 1, span]
                vec_im = vec_ref[zone_count + zone:zone_count + zone + 1, span]
                new_re.append(sums[zone] + first_part * vec_re + second_part * vec_im)
                if slope_mode:
                    new_im.append(sums[zone_count + zone] + second_part * vec_re - first_part * vec_im)
                else:
                    new_im.append(sums[zone_count + zone] + first_part * vec_im - second_part * vec_re)
            return tuple(new_re + new_im)

        columns = vec_ref.shape[0]
        zeros = tuple(jnp.zeros((8, width), jnp.float32) for _ in range(columns))
        sums = lax.fori_loop(0, chunk_count, lane_block, zeros)
        lane = lax.broadcasted_iota(jnp.int32, (8, columns), 1)
        result = jnp.zeros((8, columns), jnp.float32)
        for column in range(columns):
            total = jnp.sum(sums[column], axis=1, keepdims=True)
            result = jnp.where(lane == column, total, result)
        out_ref[rows, :] = result
        return carry

    lax.fori_loop(0, own_total // 8, row_block, 0)


def panel_contract(slope_mode, wavenumber, own_table, all_table, vector_rows, stored=None, store_out=False):
    own_total = own_table.shape[0]
    columns = vector_rows.shape[0]
    panel_total = all_table.shape[1]
    elements = own_total * panel_total
    stored_in = stored is not None
    operands = [wavenumber, own_table, all_table, vector_rows]
    out_shape = [jax.ShapeDtypeStruct((own_total, columns), jnp.float32)]
    matrix_bytes = 0
    if stored_in:
        operands += list(stored)
        matrix_bytes = 8 * elements
    if store_out:
        out_shape += [jax.ShapeDtypeStruct((own_total, panel_total), jnp.float32)] * 2
        matrix_bytes = 8 * elements
    vmem = pl.BlockSpec(memory_space=pltpu.VMEM)
    params = {}
    if matrix_bytes:
        params["compiler_params"] = pltpu.CompilerParams(vmem_limit_bytes=matrix_bytes + 16 * 1024 * 1024)
    if stored_in and not slope_mode:
        flops, transcendentals = 32 * elements, 0
    elif stored_in:
        flops, transcendentals = 60 * elements, 2 * elements
    else:
        flops, transcendentals = 150 * elements, 4 * elements
    return pl.pallas_call(
        functools.partial(panel_kernel, slope_mode, stored_in, store_out),
        out_shape=tuple(out_shape) if store_out else out_shape[0],
        in_specs=[pl.BlockSpec(memory_space=pltpu.SMEM)] + [vmem] * (len(operands) - 1),
        out_specs=tuple([vmem] * len(out_shape)) if store_out else vmem,
        cost_estimate=pl.CostEstimate(
            flops=flops,
            transcendentals=transcendentals,
            bytes_accessed=4 * (own_table.size + all_table.size + vector_rows.size + own_total * columns) + matrix_bytes,
        ),
        **params,
    )(*operands)


def gather_axis(vector, name):
    count = lax.axis_size(name)
    if count > 8:
        return lax.all_gather(vector, name, axis=0, tiled=True)
    index = lax.axis_index(name)
    parts = [vector]
    for shift in range(1, count):
        parts.append(lax.ppermute(vector, name, [(i, (i + shift) % count) for i in range(count)]))
    stacked = jnp.stack([parts[(-offset) % count] for offset in range(count)])
    ordered = jnp.roll(stacked, index, axis=0)
    return ordered.reshape((count * vector.shape[0],) + vector.shape[1:])


def gather_panels(vector):
    return gather_axis(gather_axis(vector, "col"), "row")


def chunk_size_of(count, limit):
    return math.gcd(count, limit)


def rows_sum(block_fn, count, limit):
    size = chunk_size_of(count, limit)
    starts = jnp.arange(count // size, dtype=jnp.int32) * size
    return jnp.sum(lax.map(lambda start: block_fn(start, size), starts), 0)


def local(
    centers,
    panel_areas,
    jump_term,
    displacement,
    design_ids,
    primal_field,
    adjoint_start,
    mic_panels,
    wavenumber,
):
    zone_count = adjoint_start.shape[1] // 2
    owned_count = centers.shape[1]
    axes = ("row", "col")
    wave_value = wavenumber[0]
    packed = jnp.concatenate([centers.T, panel_areas[:, None], adjoint_start], 1)
    gathered = gather_panels(packed)
    panel_total = gathered.shape[0]
    all_xyz = gathered[:, :3].T
    all_area = gathered[:, 3]
    start_full = gathered[:, 4:]
    all_table = gathered[:, :4].T
    own_table = jnp.concatenate(
        [centers.T, panel_areas[:, None], displacement.T, jnp.zeros((owned_count, 1), jnp.float32)], 1
    )

    store = 8 * owned_count * panel_total <= STORE_LIMIT
    saved = []

    def apply_adjoint(vector_full, vector_own):
        if store and saved:
            summed = panel_contract(False, wavenumber, own_table, all_table, vector_full.T, stored=saved)
        elif store:
            summed, real_part, imag_part = panel_contract(
                False, wavenumber, own_table, all_table, vector_full.T, store_out=True
            )
            saved.extend([real_part, imag_part])
        else:
            summed = panel_contract(False, wavenumber, own_table, all_table, vector_full.T)
        return panel_areas[:, None] * summed + jump_term[:, None] * vector_own

    first_panel = (
        lax.axis_index("row") * lax.axis_size("col") + lax.axis_index("col")
    ) * owned_count
    panel_ids = first_panel + jnp.arange(owned_count, dtype=jnp.int32)
    mic_hits = jnp.sum(
        (panel_ids[:, None, None] == mic_panels[None, :, :]).astype(jnp.float32), axis=2
    )
    right_side = jnp.concatenate(
        [mic_hits * primal_field[0][:, None], mic_hits * primal_field[1][:, None]], 1
    )
    residual = right_side - apply_adjoint(start_full, adjoint_start)
    residual_full = gather_panels(residual)
    start_norm = jnp.sqrt(square_sum(residual_full))
    start_scale = jnp.concatenate([start_norm, start_norm])[None, :]
    basis_one = residual / start_scale
    basis_one_full = residual_full / start_scale
    image_one = apply_adjoint(basis_one_full, basis_one)
    image_one_full = gather_panels(image_one)
    first_re, first_im = inner_parts(basis_one_full, image_one_full, zone_count)
    lean_one_full = image_one_full - complex_scale(first_re, first_im, basis_one_full, zone_count)
    lean_one = image_one - complex_scale(first_re, first_im, basis_one, zone_count)
    first_norm = jnp.sqrt(square_sum(lean_one_full))
    first_scale = jnp.concatenate([first_norm, first_norm])[None, :]
    basis_two = lean_one / first_scale
    basis_two_full = lean_one_full / first_scale
    image_two = apply_adjoint(basis_two_full, basis_two)
    image_two_full = gather_panels(image_two)
    cross_re, cross_im = inner_parts(basis_one_full, image_two_full, zone_count)
    second_re, second_im = inner_parts(basis_two_full, image_two_full, zone_count)
    lean_two_full = (
        image_two_full
        - complex_scale(cross_re, cross_im, basis_one_full, zone_count)
        - complex_scale(second_re, second_im, basis_two_full, zone_count)
    )
    second_norm = jnp.sqrt(square_sum(lean_two_full))
    coef_one_re, coef_one_im, coef_two_re, coef_two_im = least_squares(
        start_norm,
        first_re,
        first_im,
        first_norm,
        cross_re,
        cross_im,
        second_re,
        second_im,
        second_norm,
    )
    adjoint_field = (
        adjoint_start
        + complex_scale(coef_one_re, coef_one_im, basis_one, zone_count)
        + complex_scale(coef_two_re, coef_two_im, basis_two, zone_count)
    )
    field_full = (
        start_full
        + complex_scale(coef_one_re, coef_one_im, basis_one_full, zone_count)
        + complex_scale(coef_two_re, coef_two_im, basis_two_full, zone_count)
    )

    contracted = panel_contract(True, wavenumber, own_table, all_table, field_full.T, stored=saved or None)
    contrib = panel_areas[:, None] * (
        primal_field[0][:, None] * contracted[:, :zone_count]
        - primal_field[1][:, None] * contracted[:, zone_count:]
    )
    onehot = (design_ids[:, None] == jnp.arange(DESIGN, dtype=jnp.int32)[None, :]).astype(
        jnp.float32
    )
    local_sums = contract_first(contrib, onehot)
    sensitivity = lax.psum(lax.psum(local_sums, "col"), "row")
    return (adjoint_field, sensitivity)


def solution(mesh):
    return jax.shard_map(
        local,
        mesh=mesh,
        in_specs=(
            P(None, ("row", "col")),
            P(("row", "col")),
            P(("row", "col")),
            P(None, ("row", "col")),
            P(("row", "col")),
            P(None, ("row", "col")),
            P(("row", "col"), None),
            P(),
            P(),
        ),
        out_specs=(P(("row", "col"), None), P()),
        check_vma=False,
    )
```

```python
import functools
import math

import jax
import jax.numpy as jnp
from jax import lax
from jax.experimental import pallas as pl
from jax.experimental.pallas import tpu as pltpu
from jax.sharding import PartitionSpec as P

DESIGN = 128


highest = lax.Precision.HIGHEST
four_pi = 4.0 * math.pi


def distances(rows_xyz, rows_area, cols_xyz, cols_area):
    diff_x = rows_xyz[0][:, None] - cols_xyz[0][None, :]
    diff_y = rows_xyz[1][:, None] - cols_xyz[1][None, :]
    diff_z = rows_xyz[2][:, None] - cols_xyz[2][None, :]
    square = (
        diff_x * diff_x
        + diff_y * diff_y
        + diff_z * diff_z
        + 0.5 * (rows_area[:, None] + cols_area[None, :])
    )
    return (diff_x, diff_y, diff_z, jnp.sqrt(square))


def kernel_parts(rows_xyz, rows_area, cols_xyz, cols_area, wave_value):
    radius = distances(rows_xyz, rows_area, cols_xyz, cols_area)[3]
    phase = wave_value * radius
    factor = 1.0 / (four_pi * radius)
    return (jnp.cos(phase) * factor, jnp.sin(phase) * factor)


def slope_parts(rows_xyz, rows_area, cols_xyz, cols_area, cols_move, wave_value):
    diff_x, diff_y, diff_z, radius = distances(rows_xyz, rows_area, cols_xyz, cols_area)
    along_move = (
        diff_x * cols_move[0][None, :]
        + diff_y * cols_move[1][None, :]
        + diff_z * cols_move[2][None, :]
    )
    phase = wave_value * radius
    cosine_part = jnp.cos(phase)
    sine_part = jnp.sin(phase)
    factor = along_move / (four_pi * radius * radius * radius)
    return ((-cosine_part - phase * sine_part) * factor, (phase * cosine_part - sine_part) * factor)


def contract_first(matrix, vector):
    return lax.dot_general(matrix, vector, (((0,), (0,)), ((), ())), precision=highest)


def conj_columns(real_part, imag_part, vector, zone_count):
    left_part = contract_first(real_part, vector)
    right_part = contract_first(imag_part, vector)
    return jnp.concatenate(
        [
            left_part[:, :zone_count] + right_part[:, zone_count:],
            left_part[:, zone_count:] - right_part[:, :zone_count],
        ],
        1,
    )


def inner_parts(left_part, right_part, zone_count):
    left_re, left_im = (left_part[:, :zone_count], left_part[:, zone_count:])
    right_re, right_im = (right_part[:, :zone_count], right_part[:, zone_count:])
    return (
        jnp.sum(left_re * right_re + left_im * right_im, 0),
        jnp.sum(left_re * right_im - left_im * right_re, 0),
    )


def square_sum(vector):
    return jnp.sum(vector * vector, 0).reshape(2, -1).sum(0)


def complex_scale(scale_re, scale_im, vector, zone_count):
    vec_re, vec_im = (vector[:, :zone_count], vector[:, zone_count:])
    return jnp.concatenate(
        [scale_re * vec_re - scale_im * vec_im, scale_re * vec_im + scale_im * vec_re], 1
    )


def least_squares(
    start_norm,
    first_re,
    first_im,
    first_norm,
    cross_re,
    cross_im,
    second_re,
    second_im,
    second_norm,
):
    gram_one = first_re * first_re + first_im * first_im + first_norm * first_norm
    gram_off_re = first_re * cross_re + first_im * cross_im + first_norm * second_re
    gram_off_im = first_re * cross_im - first_im * cross_re + first_norm * second_im
    gram_two = (
        cross_re * cross_re
        + cross_im * cross_im
        + second_re * second_re
        + second_im * second_im
        + second_norm * second_norm
    )
    rhs_one_re = start_norm * first_re
    rhs_one_im = -start_norm * first_im
    rhs_two_re = start_norm * cross_re
    rhs_two_im = -start_norm * cross_im
    determinant = gram_one * gram_two - gram_off_re * gram_off_re - gram_off_im * gram_off_im
    coef_one_re = (
        gram_two * rhs_one_re - (gram_off_re * rhs_two_re - gram_off_im * rhs_two_im)
    ) / determinant
    coef_one_im = (
        gram_two * rhs_one_im - (gram_off_re * rhs_two_im + gram_off_im * rhs_two_re)
    ) / determinant
    coef_two_re = (
        gram_one * rhs_two_re - (gram_off_re * rhs_one_re + gram_off_im * rhs_one_im)
    ) / determinant
    coef_two_im = (
        gram_one * rhs_two_im - (gram_off_re * rhs_one_im - gram_off_im * rhs_one_re)
    ) / determinant
    return (coef_one_re, coef_one_im, coef_two_re, coef_two_im)


def slope_parts_t(own_xyz, own_area, own_move, all_xyz, all_area, wave_value):
    diff_x = all_xyz[0][None, :] - own_xyz[0][:, None]
    diff_y = all_xyz[1][None, :] - own_xyz[1][:, None]
    diff_z = all_xyz[2][None, :] - own_xyz[2][:, None]
    square = (
        diff_x * diff_x
        + diff_y * diff_y
        + diff_z * diff_z
        + 0.5 * (all_area[None, :] + own_area[:, None])
    )
    radius = jnp.sqrt(square)
    along_move = (
        diff_x * own_move[0][:, None]
        + diff_y * own_move[1][:, None]
        + diff_z * own_move[2][:, None]
    )
    phase = wave_value * radius
    cosine_part = jnp.cos(phase)
    sine_part = jnp.sin(phase)
    factor = along_move / (four_pi * radius * radius * radius)
    return ((-cosine_part - phase * sine_part) * factor, (phase * cosine_part - sine_part) * factor)


TWO_OVER_PI = 0.6366197723675814
HALF_PI_HI = 1.5703125
HALF_PI_MID = 4.837512969970703125e-4
HALF_PI_LO = 7.54978995489188216e-8


def sin_cos(angle):
    turns = jnp.floor(angle * TWO_OVER_PI + 0.5)
    rest = angle - turns * HALF_PI_HI
    rest = rest - turns * HALF_PI_MID
    rest = rest - turns * HALF_PI_LO
    rest2 = rest * rest
    sine = rest + rest * rest2 * (
        -1.6666654611e-1 + rest2 * (8.3321608736e-3 + rest2 * (-1.9515295891e-4))
    )
    cosine = 1.0 - 0.5 * rest2 + rest2 * rest2 * (
        4.166664568298827e-2 + rest2 * (-1.388731625493765e-3 + rest2 * 2.443315711809948e-5)
    )
    quarter = turns.astype(jnp.int32)
    swap = (quarter & 1) == 1
    sine_out = jnp.where(swap, cosine, sine)
    cosine_out = jnp.where(swap, sine, cosine)
    sine_out = jnp.where((quarter & 2) == 2, -sine_out, sine_out)
    cosine_out = jnp.where(((quarter + 1) & 2) == 2, -cosine_out, cosine_out)
    return sine_out, cosine_out


LANES = 256
STORE_LIMIT = 24 * 1024 * 1024


def panel_kernel(slope_mode, stored_in, store_out, wave_ref, own_ref, all_ref, vec_ref, *refs):
    if stored_in:
        real_ref, imag_ref, out_ref = refs
    elif store_out:
        out_ref, real_ref, imag_ref = refs
    else:
        (out_ref,) = refs
    wave_value = wave_ref[0]
    own_total = own_ref.shape[0]
    panel_total = all_ref.shape[1]
    width = LANES if panel_total % LANES == 0 else 128
    chunk_count = panel_total // width
    needs_geometry = slope_mode or not stored_in

    def row_block(block, carry):
        first = pl.multiple_of(block * 8, 8)
        rows = pl.ds(first, 8)
        own = own_ref[rows, :]
        own_x = jnp.broadcast_to(own[:, 0:1], (8, width))
        own_y = jnp.broadcast_to(own[:, 1:2], (8, width))
        own_z = jnp.broadcast_to(own[:, 2:3], (8, width))
        own_a = jnp.broadcast_to(own[:, 3:4], (8, width))
        if slope_mode:
            move_x = jnp.broadcast_to(own[:, 4:5], (8, width))
            move_y = jnp.broadcast_to(own[:, 5:6], (8, width))
            move_z = jnp.broadcast_to(own[:, 6:7], (8, width))

        def lane_block(chunk, sums):
            start = pl.multiple_of(chunk * width, width)
            span = pl.ds(start, width)
            if needs_geometry:
                diff_x = all_ref[0:1, span] - own_x
                diff_y = all_ref[1:2, span] - own_y
                diff_z = all_ref[2:3, span] - own_z
                square = (
                    diff_x * diff_x
                    + diff_y * diff_y
                    + diff_z * diff_z
                    + 0.5 * (all_ref[3:4, span] + own_a)
                )
                inverse = lax.rsqrt(square)
                radius = square * inverse
                phase = wave_value * radius
            if stored_in:
                real_part = real_ref[rows, span]
                imag_part = imag_ref[rows, span]
                if slope_mode:
                    along_move = diff_x * move_x + diff_y * move_y + diff_z * move_z
                    factor = along_move * (inverse * inverse)
                    first_part = (-real_part - phase * imag_part) * factor
                    second_part = (phase * real_part - imag_part) * factor
                else:
                    first_part = real_part
                    second_part = imag_part
            else:
                sine_part, cosine_part = sin_cos(phase)
                if slope_mode:
                    along_move = diff_x * move_x + diff_y * move_y + diff_z * move_z
                    factor = along_move * (inverse * inverse * inverse) * (1.0 / four_pi)
                    first_part = (-cosine_part - phase * sine_part) * factor
                    second_part = (phase * cosine_part - sine_part) * factor
                else:
                    factor = inverse * (1.0 / four_pi)
                    first_part = cosine_part * factor
                    second_part = sine_part * factor
                if store_out:
                    real_ref[rows, span] = first_part
                    imag_ref[rows, span] = second_part
            zone_count = len(sums) // 2
            new_re = []
            new_im = []
            for zone in range(zone_count):
                vec_re = vec_ref[zone:zone + 1, span]
                vec_im = vec_ref[zone_count + zone:zone_count + zone + 1, span]
                new_re.append(sums[zone] + first_part * vec_re + second_part * vec_im)
                if slope_mode:
                    new_im.append(sums[zone_count + zone] + second_part * vec_re - first_part * vec_im)
                else:
                    new_im.append(sums[zone_count + zone] + first_part * vec_im - second_part * vec_re)
            return tuple(new_re + new_im)

        columns = vec_ref.shape[0]
        zeros = tuple(jnp.zeros((8, width), jnp.float32) for _ in range(columns))
        sums = lax.fori_loop(0, chunk_count, lane_block, zeros)
        lane = lax.broadcasted_iota(jnp.int32, (8, columns), 1)
        result = jnp.zeros((8, columns), jnp.float32)
        for column in range(columns):
            total = jnp.sum(sums[column], axis=1, keepdims=True)
            result = jnp.where(lane == column, total, result)
        out_ref[rows, :] = result
        return carry

    lax.fori_loop(0, own_total // 8, row_block, 0)


def panel_contract(slope_mode, wavenumber, own_table, all_table, vector_rows, stored=None, store_out=False):
    own_total = own_table.shape[0]
    columns = vector_rows.shape[0]
    panel_total = all_table.shape[1]
    elements = own_total * panel_total
    stored_in = stored is not None
    operands = [wavenumber, own_table, all_table, vector_rows]
    out_shape = [jax.ShapeDtypeStruct((own_total, columns), jnp.float32)]
    matrix_bytes = 0
    if stored_in:
        operands += list(stored)
        matrix_bytes = 8 * elements
    if store_out:
        out_shape += [jax.ShapeDtypeStruct((own_total, panel_total), jnp.float32)] * 2
        matrix_bytes = 8 * elements
    vmem = pl.BlockSpec(memory_space=pltpu.VMEM)
    params = {}
    if matrix_bytes:
        params["compiler_params"] = pltpu.CompilerParams(vmem_limit_bytes=matrix_bytes + 16 * 1024 * 1024)
    if stored_in and not slope_mode:
        flops, transcendentals = 32 * elements, 0
    elif stored_in:
        flops, transcendentals = 60 * elements, 2 * elements
    else:
        flops, transcendentals = 150 * elements, 4 * elements
    return pl.pallas_call(
        functools.partial(panel_kernel, slope_mode, stored_in, store_out),
        out_shape=tuple(out_shape) if store_out else out_shape[0],
        in_specs=[pl.BlockSpec(memory_space=pltpu.SMEM)] + [vmem] * (len(operands) - 1),
        out_specs=tuple([vmem] * len(out_shape)) if store_out else vmem,
        cost_estimate=pl.CostEstimate(
            flops=flops,
            transcendentals=transcendentals,
            bytes_accessed=4 * (own_table.size + all_table.size + vector_rows.size + own_total * columns) + matrix_bytes,
        ),
        **params,
    )(*operands)


def gather_axis(vector, name):
    count = lax.axis_size(name)
    if count > 8:
        return lax.all_gather(vector, name, axis=0, tiled=True)
    index = lax.axis_index(name)
    parts = [vector]
    for shift in range(1, count):
        parts.append(lax.ppermute(vector, name, [(i, (i + shift) % count) for i in range(count)]))
    stacked = jnp.stack([parts[(-offset) % count] for offset in range(count)])
    ordered = jnp.roll(stacked, index, axis=0)
    return ordered.reshape((count * vector.shape[0],) + vector.shape[1:])


def gather_panels(vector):
    return gather_axis(gather_axis(vector, "col"), "row")


def chunk_size_of(count, limit):
    return math.gcd(count, limit)


def rows_sum(block_fn, count, limit):
    size = chunk_size_of(count, limit)
    starts = jnp.arange(count // size, dtype=jnp.int32) * size
    return jnp.sum(lax.map(lambda start: block_fn(start, size), starts), 0)


def local(
    centers,
    panel_areas,
    jump_term,
    displacement,
    design_ids,
    primal_field,
    adjoint_start,
    mic_panels,
    wavenumber,
):
    zone_count = adjoint_start.shape[1] // 2
    owned_count = centers.shape[1]
    axes = ("row", "col")
    wave_value = wavenumber[0]
    packed = jnp.concatenate([centers.T, panel_areas[:, None], adjoint_start], 1)
    gathered = gather_panels(packed)
    panel_total = gathered.shape[0]
    all_xyz = gathered[:, :3].T
    all_area = gathered[:, 3]
    start_full = gathered[:, 4:]
    all_table = gathered[:, :4].T
    own_table = jnp.concatenate(
        [centers.T, panel_areas[:, None], displacement.T, jnp.zeros((owned_count, 1), jnp.float32)], 1
    )

    store = 8 * owned_count * panel_total <= STORE_LIMIT
    saved = []

    def apply_adjoint(vector_full, vector_own):
        if store and saved:
            summed = panel_contract(False, wavenumber, own_table, all_table, vector_full.T, stored=saved)
        elif store:
            summed, real_part, imag_part = panel_contract(
                False, wavenumber, own_table, all_table, vector_full.T, store_out=True
            )
            saved.extend([real_part, imag_part])
        else:
            summed = panel_contract(False, wavenumber, own_table, all_table, vector_full.T)
        return panel_areas[:, None] * summed + jump_term[:, None] * vector_own

    first_panel = (
        lax.axis_index("row") * lax.axis_size("col") + lax.axis_index("col")
    ) * owned_count
    panel_ids = first_panel + jnp.arange(owned_count, dtype=jnp.int32)
    mic_hits = jnp.sum(
        (panel_ids[:, None, None] == mic_panels[None, :, :]).astype(jnp.float32), axis=2
    )
    right_side = jnp.concatenate(
        [mic_hits * primal_field[0][:, None], mic_hits * primal_field[1][:, None]], 1
    )
    residual = right_side - apply_adjoint(start_full, adjoint_start)
    residual_full = gather_panels(residual)
    start_norm = jnp.sqrt(square_sum(residual_full))
    start_scale = jnp.concatenate([start_norm, start_norm])[None, :]
    basis_one = residual / start_scale
    basis_one_full = residual_full / start_scale
    image_one = apply_adjoint(basis_one_full, basis_one)
    image_one_full = gather_panels(image_one)
    first_re, first_im = inner_parts(basis_one_full, image_one_full, zone_count)
    lean_one_full = image_one_full - complex_scale(first_re, first_im, basis_one_full, zone_count)
    lean_one = image_one - complex_scale(first_re, first_im, basis_one, zone_count)
    first_norm = jnp.sqrt(square_sum(lean_one_full))
    first_scale = jnp.concatenate([first_norm, first_norm])[None, :]
    basis_two = lean_one / first_scale
    basis_two_full = lean_one_full / first_scale
    image_two = apply_adjoint(basis_two_full, basis_two)
    image_two_full = gather_panels(image_two)
    cross_re, cross_im = inner_parts(basis_one_full, image_two_full, zone_count)
    second_re, second_im = inner_parts(basis_two_full, image_two_full, zone_count)
    lean_two_full = (
        image_two_full
        - complex_scale(cross_re, cross_im, basis_one_full, zone_count)
        - complex_scale(second_re, second_im, basis_two_full, zone_count)
    )
    second_norm = jnp.sqrt(square_sum(lean_two_full))
    coef_one_re, coef_one_im, coef_two_re, coef_two_im = least_squares(
        start_norm,
        first_re,
        first_im,
        first_norm,
        cross_re,
        cross_im,
        second_re,
        second_im,
        second_norm,
    )
    adjoint_field = (
        adjoint_start
        + complex_scale(coef_one_re, coef_one_im, basis_one, zone_count)
        + complex_scale(coef_two_re, coef_two_im, basis_two, zone_count)
    )
    field_full = (
        start_full
        + complex_scale(coef_one_re, coef_one_im, basis_one_full, zone_count)
        + complex_scale(coef_two_re, coef_two_im, basis_two_full, zone_count)
    )

    contracted = panel_contract(True, wavenumber, own_table, all_table, field_full.T, stored=saved or None)
    contrib = panel_areas[:, None] * (
        primal_field[0][:, None] * contracted[:, :zone_count]
        - primal_field[1][:, None] * contracted[:, zone_count:]
    )
    onehot = (design_ids[:, None] == jnp.arange(DESIGN, dtype=jnp.int32)[None, :]).astype(
        jnp.float32
    )
    local_sums = contract_first(contrib, onehot)
    sensitivity = lax.psum(lax.psum(local_sums, "col"), "row")
    return (adjoint_field, sensitivity)


def solution(mesh):
    return jax.shard_map(
        local,
        mesh=mesh,
        in_specs=(
            P(None, ("row", "col")),
            P(("row", "col")),
            P(("row", "col")),
            P(None, ("row", "col")),
            P(("row", "col")),
            P(None, ("row", "col")),
            P(("row", "col"), None),
            P(),
            P(),
        ),
        out_specs=(P(("row", "col"), None), P()),
        check_vma=False,
    )
```

```python
import functools
import math

import jax
import jax.numpy as jnp
from jax import lax
from jax.experimental import pallas as pl
from jax.experimental.pallas import tpu as pltpu
from jax.sharding import PartitionSpec as P

DESIGN = 128


highest = lax.Precision.HIGHEST
four_pi = 4.0 * math.pi


def distances(rows_xyz, rows_area, cols_xyz, cols_area):
    diff_x = rows_xyz[0][:, None] - cols_xyz[0][None, :]
    diff_y = rows_xyz[1][:, None] - cols_xyz[1][None, :]
    diff_z = rows_xyz[2][:, None] - cols_xyz[2][None, :]
    square = (
        diff_x * diff_x
        + diff_y * diff_y
        + diff_z * diff_z
        + 0.5 * (rows_area[:, None] + cols_area[None, :])
    )
    return (diff_x, diff_y, diff_z, jnp.sqrt(square))


def kernel_parts(rows_xyz, rows_area, cols_xyz, cols_area, wave_value):
    radius = distances(rows_xyz, rows_area, cols_xyz, cols_area)[3]
    phase = wave_value * radius
    factor = 1.0 / (four_pi * radius)
    return (jnp.cos(phase) * factor, jnp.sin(phase) * factor)


def slope_parts(rows_xyz, rows_area, cols_xyz, cols_area, cols_move, wave_value):
    diff_x, diff_y, diff_z, radius = distances(rows_xyz, rows_area, cols_xyz, cols_area)
    along_move = (
        diff_x * cols_move[0][None, :]
        + diff_y * cols_move[1][None, :]
        + diff_z * cols_move[2][None, :]
    )
    phase = wave_value * radius
    cosine_part = jnp.cos(phase)
    sine_part = jnp.sin(phase)
    factor = along_move / (four_pi * radius * radius * radius)
    return ((-cosine_part - phase * sine_part) * factor, (phase * cosine_part - sine_part) * factor)


def contract_first(matrix, vector):
    return lax.dot_general(matrix, vector, (((0,), (0,)), ((), ())), precision=highest)


def conj_columns(real_part, imag_part, vector, zone_count):
    left_part = contract_first(real_part, vector)
    right_part = contract_first(imag_part, vector)
    return jnp.concatenate(
        [
            left_part[:, :zone_count] + right_part[:, zone_count:],
            left_part[:, zone_count:] - right_part[:, :zone_count],
        ],
        1,
    )


def inner_parts(left_part, right_part, zone_count):
    left_re, left_im = (left_part[:, :zone_count], left_part[:, zone_count:])
    right_re, right_im = (right_part[:, :zone_count], right_part[:, zone_count:])
    return (
        jnp.sum(left_re * right_re + left_im * right_im, 0),
        jnp.sum(left_re * right_im - left_im * right_re, 0),
    )


def square_sum(vector):
    return jnp.sum(vector * vector, 0).reshape(2, -1).sum(0)


def complex_scale(scale_re, scale_im, vector, zone_count):
    vec_re, vec_im = (vector[:, :zone_count], vector[:, zone_count:])
    return jnp.concatenate(
        [scale_re * vec_re - scale_im * vec_im, scale_re * vec_im + scale_im * vec_re], 1
    )


def least_squares(
    start_norm,
    first_re,
    first_im,
    first_norm,
    cross_re,
    cross_im,
    second_re,
    second_im,
    second_norm,
):
    gram_one = first_re * first_re + first_im * first_im + first_norm * first_norm
    gram_off_re = first_re * cross_re + first_im * cross_im + first_norm * second_re
    gram_off_im = first_re * cross_im - first_im * cross_re + first_norm * second_im
    gram_two = (
        cross_re * cross_re
        + cross_im * cross_im
        + second_re * second_re
        + second_im * second_im
        + second_norm * second_norm
    )
    rhs_one_re = start_norm * first_re
    rhs_one_im = -start_norm * first_im
    rhs_two_re = start_norm * cross_re
    rhs_two_im = -start_norm * cross_im
    determinant = gram_one * gram_two - gram_off_re * gram_off_re - gram_off_im * gram_off_im
    coef_one_re = (
        gram_two * rhs_one_re - (gram_off_re * rhs_two_re - gram_off_im * rhs_two_im)
    ) / determinant
    coef_one_im = (
        gram_two * rhs_one_im - (gram_off_re * rhs_two_im + gram_off_im * rhs_two_re)
    ) / determinant
    coef_two_re = (
        gram_one * rhs_two_re - (gram_off_re * rhs_one_re + gram_off_im * rhs_one_im)
    ) / determinant
    coef_two_im = (
        gram_one * rhs_two_im - (gram_off_re * rhs_one_im - gram_off_im * rhs_one_re)
    ) / determinant
    return (coef_one_re, coef_one_im, coef_two_re, coef_two_im)


def slope_parts_t(own_xyz, own_area, own_move, all_xyz, all_area, wave_value):
    diff_x = all_xyz[0][None, :] - own_xyz[0][:, None]
    diff_y = all_xyz[1][None, :] - own_xyz[1][:, None]
    diff_z = all_xyz[2][None, :] - own_xyz[2][:, None]
    square = (
        diff_x * diff_x
        + diff_y * diff_y
        + diff_z * diff_z
        + 0.5 * (all_area[None, :] + own_area[:, None])
    )
    radius = jnp.sqrt(square)
    along_move = (
        diff_x * own_move[0][:, None]
        + diff_y * own_move[1][:, None]
        + diff_z * own_move[2][:, None]
    )
    phase = wave_value * radius
    cosine_part = jnp.cos(phase)
    sine_part = jnp.sin(phase)
    factor = along_move / (four_pi * radius * radius * radius)
    return ((-cosine_part - phase * sine_part) * factor, (phase * cosine_part - sine_part) * factor)


TWO_OVER_PI = 0.6366197723675814
HALF_PI_HI = 1.5703125
HALF_PI_MID = 4.837512969970703125e-4
HALF_PI_LO = 7.54978995489188216e-8


def sin_cos(angle):
    turns = jnp.floor(angle * TWO_OVER_PI + 0.5)
    rest = angle - turns * HALF_PI_HI
    rest = rest - turns * HALF_PI_MID
    rest = rest - turns * HALF_PI_LO
    rest2 = rest * rest
    sine = rest + rest * rest2 * (
        -1.6666654611e-1 + rest2 * (8.3321608736e-3 + rest2 * (-1.9515295891e-4))
    )
    cosine = 1.0 - 0.5 * rest2 + rest2 * rest2 * (
        4.166664568298827e-2 + rest2 * (-1.388731625493765e-3 + rest2 * 2.443315711809948e-5)
    )
    quarter = turns.astype(jnp.int32)
    swap = (quarter & 1) == 1
    sine_out = jnp.where(swap, cosine, sine)
    cosine_out = jnp.where(swap, sine, cosine)
    sine_out = jnp.where((quarter & 2) == 2, -sine_out, sine_out)
    cosine_out = jnp.where(((quarter + 1) & 2) == 2, -cosine_out, cosine_out)
    return sine_out, cosine_out


LANES = 256
STORE_LIMIT = 24 * 1024 * 1024


def panel_kernel(slope_mode, stored_in, store_out, wave_ref, own_ref, all_ref, vec_ref, *refs):
    if stored_in:
        real_ref, imag_ref, out_ref = refs
    elif store_out:
        out_ref, real_ref, imag_ref = refs
    else:
        (out_ref,) = refs
    wave_value = wave_ref[0]
    own_total = own_ref.shape[0]
    panel_total = all_ref.shape[1]
    width = LANES if panel_total % LANES == 0 else 128
    chunk_count = panel_total // width
    needs_geometry = slope_mode or not stored_in

    def row_block(block, carry):
        first = pl.multiple_of(block * 8, 8)
        rows = pl.ds(first, 8)
        own = own_ref[rows, :]
        own_x = jnp.broadcast_to(own[:, 0:1], (8, width))
        own_y = jnp.broadcast_to(own[:, 1:2], (8, width))
        own_z = jnp.broadcast_to(own[:, 2:3], (8, width))
        own_a = jnp.broadcast_to(own[:, 3:4], (8, width))
        if slope_mode:
            move_x = jnp.broadcast_to(own[:, 4:5], (8, width))
            move_y = jnp.broadcast_to(own[:, 5:6], (8, width))
            move_z = jnp.broadcast_to(own[:, 6:7], (8, width))

        def lane_block(chunk, sums):
            start = pl.multiple_of(chunk * width, width)
            span = pl.ds(start, width)
            if needs_geometry:
                diff_x = all_ref[0:1, span] - own_x
                diff_y = all_ref[1:2, span] - own_y
                diff_z = all_ref[2:3, span] - own_z
                square = (
                    diff_x * diff_x
                    + diff_y * diff_y
                    + diff_z * diff_z
                    + 0.5 * (all_ref[3:4, span] + own_a)
                )
                inverse = lax.rsqrt(square)
                radius = square * inverse
                phase = wave_value * radius
            if stored_in:
                real_part = real_ref[rows, span]
                imag_part = imag_ref[rows, span]
                if slope_mode:
                    along_move = diff_x * move_x + diff_y * move_y + diff_z * move_z
                    factor = along_move * (inverse * inverse)
                    first_part = (-real_part - phase * imag_part) * factor
                    second_part = (phase * real_part - imag_part) * factor
                else:
                    first_part = real_part
                    second_part = imag_part
            else:
                sine_part, cosine_part = sin_cos(phase)
                if slope_mode:
                    along_move = diff_x * move_x + diff_y * move_y + diff_z * move_z
                    factor = along_move * (inverse * inverse * inverse) * (1.0 / four_pi)
                    first_part = (-cosine_part - phase * sine_part) * factor
                    second_part = (phase * cosine_part - sine_part) * factor
                else:
                    factor = inverse * (1.0 / four_pi)
                    first_part = cosine_part * factor
                    second_part = sine_part * factor
                if store_out:
                    real_ref[rows, span] = first_part
                    imag_ref[rows, span] = second_part
            zone_count = len(sums) // 3
            both_parts = first_part + second_part
            new_sums = []
            for zone in range(zone_count):
                new_sums.append(sums[zone] + first_part * vec_ref[zone:zone + 1, span])
            for zone in range(zone_count, 2 * zone_count):
                new_sums.append(sums[zone] + second_part * vec_ref[zone:zone + 1, span])
            for zone in range(2 * zone_count, 3 * zone_count):
                new_sums.append(sums[zone] + both_parts * vec_ref[zone:zone + 1, span])
            return tuple(new_sums)

        columns = vec_ref.shape[0]
        zeros = tuple(jnp.zeros((8, width), jnp.float32) for _ in range(columns))
        sums = lax.fori_loop(0, chunk_count, lane_block, zeros)
        lane = lax.broadcasted_iota(jnp.int32, (8, columns), 1)
        result = jnp.zeros((8, columns), jnp.float32)
        for column in range(columns):
            total = jnp.sum(sums[column], axis=1, keepdims=True)
            result = jnp.where(lane == column, total, result)
        out_ref[rows, :] = result
        return carry

    lax.fori_loop(0, own_total // 8, row_block, 0)


def panel_contract(slope_mode, wavenumber, own_table, all_table, vector_full, stored=None, store_out=False):
    zone_count = vector_full.shape[1] // 2
    vector_rows = jnp.concatenate(
        [vector_full.T, (vector_full[:, :zone_count] - vector_full[:, zone_count:]).T], 0
    )
    outs = panel_call(slope_mode, wavenumber, own_table, all_table, vector_rows, stored, store_out)
    sums = outs[0] if store_out else outs
    first_sum = sums[:, :zone_count]
    second_sum = sums[:, zone_count:2 * zone_count]
    both_sum = sums[:, 2 * zone_count:]
    if slope_mode:
        imag_sum = both_sum - first_sum + second_sum
    else:
        imag_sum = first_sum - second_sum - both_sum
    combined = jnp.concatenate([first_sum + second_sum, imag_sum], 1)
    if store_out:
        return (combined,) + tuple(outs[1:])
    return combined


def panel_call(slope_mode, wavenumber, own_table, all_table, vector_rows, stored, store_out):
    own_total = own_table.shape[0]
    columns = vector_rows.shape[0]
    panel_total = all_table.shape[1]
    elements = own_total * panel_total
    stored_in = stored is not None
    operands = [wavenumber, own_table, all_table, vector_rows]
    out_shape = [jax.ShapeDtypeStruct((own_total, columns), jnp.float32)]
    matrix_bytes = 0
    if stored_in:
        operands += list(stored)
        matrix_bytes = 8 * elements
    if store_out:
        out_shape += [jax.ShapeDtypeStruct((own_total, panel_total), jnp.float32)] * 2
        matrix_bytes = 8 * elements
    vmem = pl.BlockSpec(memory_space=pltpu.VMEM)
    params = {}
    if matrix_bytes:
        params["compiler_params"] = pltpu.CompilerParams(vmem_limit_bytes=matrix_bytes + 16 * 1024 * 1024)
    if stored_in and not slope_mode:
        flops, transcendentals = 32 * elements, 0
    elif stored_in:
        flops, transcendentals = 60 * elements, 2 * elements
    else:
        flops, transcendentals = 150 * elements, 4 * elements
    return pl.pallas_call(
        functools.partial(panel_kernel, slope_mode, stored_in, store_out),
        out_shape=tuple(out_shape) if store_out else out_shape[0],
        in_specs=[pl.BlockSpec(memory_space=pltpu.SMEM)] + [vmem] * (len(operands) - 1),
        out_specs=tuple([vmem] * len(out_shape)) if store_out else vmem,
        cost_estimate=pl.CostEstimate(
            flops=flops,
            transcendentals=transcendentals,
            bytes_accessed=4 * (own_table.size + all_table.size + vector_rows.size + own_total * columns) + matrix_bytes,
        ),
        **params,
    )(*operands)


def gather_axis(vector, name):
    count = lax.axis_size(name)
    if count > 8:
        return lax.all_gather(vector, name, axis=0, tiled=True)
    index = lax.axis_index(name)
    parts = [vector]
    for shift in range(1, count):
        parts.append(lax.ppermute(vector, name, [(i, (i + shift) % count) for i in range(count)]))
    stacked = jnp.stack([parts[(-offset) % count] for offset in range(count)])
    ordered = jnp.roll(stacked, index, axis=0)
    return ordered.reshape((count * vector.shape[0],) + vector.shape[1:])


def gather_panels(vector):
    return gather_axis(gather_axis(vector, "col"), "row")


def chunk_size_of(count, limit):
    return math.gcd(count, limit)


def rows_sum(block_fn, count, limit):
    size = chunk_size_of(count, limit)
    starts = jnp.arange(count // size, dtype=jnp.int32) * size
    return jnp.sum(lax.map(lambda start: block_fn(start, size), starts), 0)


def local(
    centers,
    panel_areas,
    jump_term,
    displacement,
    design_ids,
    primal_field,
    adjoint_start,
    mic_panels,
    wavenumber,
):
    zone_count = adjoint_start.shape[1] // 2
    owned_count = centers.shape[1]
    axes = ("row", "col")
    wave_value = wavenumber[0]
    packed = jnp.concatenate([centers.T, panel_areas[:, None], adjoint_start], 1)
    gathered = gather_panels(packed)
    panel_total = gathered.shape[0]
    all_xyz = gathered[:, :3].T
    all_area = gathered[:, 3]
    start_full = gathered[:, 4:]
    all_table = gathered[:, :4].T
    own_table = jnp.concatenate(
        [centers.T, panel_areas[:, None], displacement.T, jnp.zeros((owned_count, 1), jnp.float32)], 1
    )

    store = 8 * owned_count * panel_total <= STORE_LIMIT
    saved = []

    def apply_adjoint(vector_full, vector_own):
        if store and saved:
            summed = panel_contract(False, wavenumber, own_table, all_table, vector_full, stored=saved)
        elif store:
            summed, real_part, imag_part = panel_contract(
                False, wavenumber, own_table, all_table, vector_full, store_out=True
            )
            saved.extend([real_part, imag_part])
        else:
            summed = panel_contract(False, wavenumber, own_table, all_table, vector_full)
        return panel_areas[:, None] * summed + jump_term[:, None] * vector_own

    first_panel = (
        lax.axis_index("row") * lax.axis_size("col") + lax.axis_index("col")
    ) * owned_count
    panel_ids = first_panel + jnp.arange(owned_count, dtype=jnp.int32)
    mic_hits = jnp.sum(
        (panel_ids[:, None, None] == mic_panels[None, :, :]).astype(jnp.float32), axis=2
    )
    right_side = jnp.concatenate(
        [mic_hits * primal_field[0][:, None], mic_hits * primal_field[1][:, None]], 1
    )
    residual = right_side - apply_adjoint(start_full, adjoint_start)
    residual_full = gather_panels(residual)
    start_norm = jnp.sqrt(square_sum(residual_full))
    start_scale = jnp.concatenate([start_norm, start_norm])[None, :]
    basis_one = residual / start_scale
    basis_one_full = residual_full / start_scale
    image_one = apply_adjoint(basis_one_full, basis_one)
    image_one_full = gather_panels(image_one)
    first_re, first_im = inner_parts(basis_one_full, image_one_full, zone_count)
    lean_one_full = image_one_full - complex_scale(first_re, first_im, basis_one_full, zone_count)
    lean_one = image_one - complex_scale(first_re, first_im, basis_one, zone_count)
    first_norm = jnp.sqrt(square_sum(lean_one_full))
    first_scale = jnp.concatenate([first_norm, first_norm])[None, :]
    basis_two = lean_one / first_scale
    basis_two_full = lean_one_full / first_scale
    image_two = apply_adjoint(basis_two_full, basis_two)
    image_two_full = gather_panels(image_two)
    cross_re, cross_im = inner_parts(basis_one_full, image_two_full, zone_count)
    second_re, second_im = inner_parts(basis_two_full, image_two_full, zone_count)
    lean_two_full = (
        image_two_full
        - complex_scale(cross_re, cross_im, basis_one_full, zone_count)
        - complex_scale(second_re, second_im, basis_two_full, zone_count)
    )
    second_norm = jnp.sqrt(square_sum(lean_two_full))
    coef_one_re, coef_one_im, coef_two_re, coef_two_im = least_squares(
        start_norm,
        first_re,
        first_im,
        first_norm,
        cross_re,
        cross_im,
        second_re,
        second_im,
        second_norm,
    )
    adjoint_field = (
        adjoint_start
        + complex_scale(coef_one_re, coef_one_im, basis_one, zone_count)
        + complex_scale(coef_two_re, coef_two_im, basis_two, zone_count)
    )
    field_full = (
        start_full
        + complex_scale(coef_one_re, coef_one_im, basis_one_full, zone_count)
        + complex_scale(coef_two_re, coef_two_im, basis_two_full, zone_count)
    )

    contracted = panel_contract(True, wavenumber, own_table, all_table, field_full, stored=saved or None)
    contrib = panel_areas[:, None] * (
        primal_field[0][:, None] * contracted[:, :zone_count]
        - primal_field[1][:, None] * contracted[:, zone_count:]
    )
    onehot = (design_ids[:, None] == jnp.arange(DESIGN, dtype=jnp.int32)[None, :]).astype(
        jnp.float32
    )
    local_sums = contract_first(contrib, onehot)
    sensitivity = lax.psum(lax.psum(local_sums, "col"), "row")
    return (adjoint_field, sensitivity)


def solution(mesh):
    return jax.shard_map(
        local,
        mesh=mesh,
        in_specs=(
            P(None, ("row", "col")),
            P(("row", "col")),
            P(("row", "col")),
            P(None, ("row", "col")),
            P(("row", "col")),
            P(None, ("row", "col")),
            P(("row", "col"), None),
            P(),
            P(),
        ),
        out_specs=(P(("row", "col"), None), P()),
        check_vma=False,
    )
```

```python
import functools
import math

import jax
import jax.numpy as jnp
from jax import lax
from jax.experimental import pallas as pl
from jax.experimental.pallas import tpu as pltpu
from jax.sharding import PartitionSpec as P

DESIGN = 128


highest = lax.Precision.HIGHEST
four_pi = 4.0 * math.pi


def distances(rows_xyz, rows_area, cols_xyz, cols_area):
    diff_x = rows_xyz[0][:, None] - cols_xyz[0][None, :]
    diff_y = rows_xyz[1][:, None] - cols_xyz[1][None, :]
    diff_z = rows_xyz[2][:, None] - cols_xyz[2][None, :]
    square = (
        diff_x * diff_x
        + diff_y * diff_y
        + diff_z * diff_z
        + 0.5 * (rows_area[:, None] + cols_area[None, :])
    )
    return (diff_x, diff_y, diff_z, jnp.sqrt(square))


def kernel_parts(rows_xyz, rows_area, cols_xyz, cols_area, wave_value):
    radius = distances(rows_xyz, rows_area, cols_xyz, cols_area)[3]
    phase = wave_value * radius
    factor = 1.0 / (four_pi * radius)
    return (jnp.cos(phase) * factor, jnp.sin(phase) * factor)


def slope_parts(rows_xyz, rows_area, cols_xyz, cols_area, cols_move, wave_value):
    diff_x, diff_y, diff_z, radius = distances(rows_xyz, rows_area, cols_xyz, cols_area)
    along_move = (
        diff_x * cols_move[0][None, :]
        + diff_y * cols_move[1][None, :]
        + diff_z * cols_move[2][None, :]
    )
    phase = wave_value * radius
    cosine_part = jnp.cos(phase)
    sine_part = jnp.sin(phase)
    factor = along_move / (four_pi * radius * radius * radius)
    return ((-cosine_part - phase * sine_part) * factor, (phase * cosine_part - sine_part) * factor)


def contract_first(matrix, vector):
    return lax.dot_general(matrix, vector, (((0,), (0,)), ((), ())), precision=highest)


def conj_columns(real_part, imag_part, vector, zone_count):
    left_part = contract_first(real_part, vector)
    right_part = contract_first(imag_part, vector)
    return jnp.concatenate(
        [
            left_part[:, :zone_count] + right_part[:, zone_count:],
            left_part[:, zone_count:] - right_part[:, :zone_count],
        ],
        1,
    )


def inner_parts(left_part, right_part, zone_count):
    left_re, left_im = (left_part[:, :zone_count], left_part[:, zone_count:])
    right_re, right_im = (right_part[:, :zone_count], right_part[:, zone_count:])
    return (
        jnp.sum(left_re * right_re + left_im * right_im, 0),
        jnp.sum(left_re * right_im - left_im * right_re, 0),
    )


def square_sum(vector):
    return jnp.sum(vector * vector, 0).reshape(2, -1).sum(0)


def complex_scale(scale_re, scale_im, vector, zone_count):
    vec_re, vec_im = (vector[:, :zone_count], vector[:, zone_count:])
    return jnp.concatenate(
        [scale_re * vec_re - scale_im * vec_im, scale_re * vec_im + scale_im * vec_re], 1
    )


def least_squares(
    start_norm,
    first_re,
    first_im,
    first_norm,
    cross_re,
    cross_im,
    second_re,
    second_im,
    second_norm,
):
    gram_one = first_re * first_re + first_im * first_im + first_norm * first_norm
    gram_off_re = first_re * cross_re + first_im * cross_im + first_norm * second_re
    gram_off_im = first_re * cross_im - first_im * cross_re + first_norm * second_im
    gram_two = (
        cross_re * cross_re
        + cross_im * cross_im
        + second_re * second_re
        + second_im * second_im
        + second_norm * second_norm
    )
    rhs_one_re = start_norm * first_re
    rhs_one_im = -start_norm * first_im
    rhs_two_re = start_norm * cross_re
    rhs_two_im = -start_norm * cross_im
    determinant = gram_one * gram_two - gram_off_re * gram_off_re - gram_off_im * gram_off_im
    coef_one_re = (
        gram_two * rhs_one_re - (gram_off_re * rhs_two_re - gram_off_im * rhs_two_im)
    ) / determinant
    coef_one_im = (
        gram_two * rhs_one_im - (gram_off_re * rhs_two_im + gram_off_im * rhs_two_re)
    ) / determinant
    coef_two_re = (
        gram_one * rhs_two_re - (gram_off_re * rhs_one_re + gram_off_im * rhs_one_im)
    ) / determinant
    coef_two_im = (
        gram_one * rhs_two_im - (gram_off_re * rhs_one_im - gram_off_im * rhs_one_re)
    ) / determinant
    return (coef_one_re, coef_one_im, coef_two_re, coef_two_im)


def slope_parts_t(own_xyz, own_area, own_move, all_xyz, all_area, wave_value):
    diff_x = all_xyz[0][None, :] - own_xyz[0][:, None]
    diff_y = all_xyz[1][None, :] - own_xyz[1][:, None]
    diff_z = all_xyz[2][None, :] - own_xyz[2][:, None]
    square = (
        diff_x * diff_x
        + diff_y * diff_y
        + diff_z * diff_z
        + 0.5 * (all_area[None, :] + own_area[:, None])
    )
    radius = jnp.sqrt(square)
    along_move = (
        diff_x * own_move[0][:, None]
        + diff_y * own_move[1][:, None]
        + diff_z * own_move[2][:, None]
    )
    phase = wave_value * radius
    cosine_part = jnp.cos(phase)
    sine_part = jnp.sin(phase)
    factor = along_move / (four_pi * radius * radius * radius)
    return ((-cosine_part - phase * sine_part) * factor, (phase * cosine_part - sine_part) * factor)


TWO_OVER_PI = 0.6366197723675814
HALF_PI_HI = 1.5703125
HALF_PI_MID = 4.837512969970703125e-4
HALF_PI_LO = 7.54978995489188216e-8


def sin_cos(angle):
    turns = jnp.floor(angle * TWO_OVER_PI + 0.5)
    rest = angle - turns * HALF_PI_HI
    rest = rest - turns * HALF_PI_MID
    rest = rest - turns * HALF_PI_LO
    rest2 = rest * rest
    sine = rest + rest * rest2 * (
        -1.6666654611e-1 + rest2 * (8.3321608736e-3 + rest2 * (-1.9515295891e-4))
    )
    cosine = 1.0 - 0.5 * rest2 + rest2 * rest2 * (
        4.166664568298827e-2 + rest2 * (-1.388731625493765e-3 + rest2 * 2.443315711809948e-5)
    )
    quarter = turns.astype(jnp.int32)
    swap = (quarter & 1) == 1
    sine_out = jnp.where(swap, cosine, sine)
    cosine_out = jnp.where(swap, sine, cosine)
    sine_out = jnp.where((quarter & 2) == 2, -sine_out, sine_out)
    cosine_out = jnp.where(((quarter + 1) & 2) == 2, -cosine_out, cosine_out)
    return sine_out, cosine_out


LANES = 256
STORE_LIMIT = 24 * 1024 * 1024


def panel_kernel(slope_mode, stored_in, store_out, wave_ref, own_ref, all_ref, vec_ref, *refs):
    if stored_in:
        real_ref, imag_ref, out_ref = refs
    elif store_out:
        out_ref, real_ref, imag_ref = refs
    else:
        (out_ref,) = refs
    wave_value = wave_ref[0]
    own_total = own_ref.shape[0]
    panel_total = all_ref.shape[1]
    width = LANES if panel_total % LANES == 0 else 128
    chunk_count = panel_total // width
    needs_geometry = slope_mode or not stored_in

    def row_block(block, carry):
        first = pl.multiple_of(block * 8, 8)
        rows = pl.ds(first, 8)
        own = own_ref[rows, :]
        own_x = jnp.broadcast_to(own[:, 0:1], (8, width))
        own_y = jnp.broadcast_to(own[:, 1:2], (8, width))
        own_z = jnp.broadcast_to(own[:, 2:3], (8, width))
        own_a = jnp.broadcast_to(own[:, 3:4], (8, width))
        if slope_mode:
            move_x = jnp.broadcast_to(own[:, 4:5], (8, width))
            move_y = jnp.broadcast_to(own[:, 5:6], (8, width))
            move_z = jnp.broadcast_to(own[:, 6:7], (8, width))

        def lane_block(chunk, sums):
            start = pl.multiple_of(chunk * width, width)
            span = pl.ds(start, width)
            if needs_geometry:
                diff_x = all_ref[0:1, span] - own_x
                diff_y = all_ref[1:2, span] - own_y
                diff_z = all_ref[2:3, span] - own_z
                square = (
                    diff_x * diff_x
                    + diff_y * diff_y
                    + diff_z * diff_z
                    + 0.5 * (all_ref[3:4, span] + own_a)
                )
                inverse = lax.rsqrt(square)
                radius = square * inverse
                phase = wave_value * radius
            if stored_in:
                real_part = real_ref[rows, span]
                imag_part = imag_ref[rows, span]
                if slope_mode:
                    along_move = diff_x * move_x + diff_y * move_y + diff_z * move_z
                    factor = along_move * (inverse * inverse)
                    first_part = (-real_part - phase * imag_part) * factor
                    second_part = (phase * real_part - imag_part) * factor
                else:
                    first_part = real_part
                    second_part = imag_part
            else:
                sine_part, cosine_part = sin_cos(phase)
                if slope_mode:
                    along_move = diff_x * move_x + diff_y * move_y + diff_z * move_z
                    factor = along_move * (inverse * inverse * inverse) * (1.0 / four_pi)
                    first_part = (-cosine_part - phase * sine_part) * factor
                    second_part = (phase * cosine_part - sine_part) * factor
                else:
                    factor = inverse * (1.0 / four_pi)
                    first_part = cosine_part * factor
                    second_part = sine_part * factor
                if store_out:
                    real_ref[rows, span] = first_part
                    imag_ref[rows, span] = second_part
            zone_count = len(sums) // 3
            both_parts = first_part + second_part
            new_sums = []
            for zone in range(zone_count):
                new_sums.append(sums[zone] + first_part * vec_ref[zone:zone + 1, span])
            for zone in range(zone_count, 2 * zone_count):
                new_sums.append(sums[zone] + second_part * vec_ref[zone:zone + 1, span])
            for zone in range(2 * zone_count, 3 * zone_count):
                new_sums.append(sums[zone] + both_parts * vec_ref[zone:zone + 1, span])
            return tuple(new_sums)

        columns = vec_ref.shape[0]
        zeros = tuple(jnp.zeros((8, width), jnp.float32) for _ in range(columns))
        sums = lax.fori_loop(0, chunk_count, lane_block, zeros, unroll=2)
        lane = lax.broadcasted_iota(jnp.int32, (8, columns), 1)
        result = jnp.zeros((8, columns), jnp.float32)
        for column in range(columns):
            total = jnp.sum(sums[column], axis=1, keepdims=True)
            result = jnp.where(lane == column, total, result)
        out_ref[rows, :] = result
        return carry

    lax.fori_loop(0, own_total // 8, row_block, 0)


def panel_contract(slope_mode, wavenumber, own_table, all_table, vector_full, stored=None, store_out=False):
    zone_count = vector_full.shape[1] // 2
    vector_rows = jnp.concatenate(
        [vector_full.T, (vector_full[:, :zone_count] - vector_full[:, zone_count:]).T], 0
    )
    outs = panel_call(slope_mode, wavenumber, own_table, all_table, vector_rows, stored, store_out)
    sums = outs[0] if store_out else outs
    first_sum = sums[:, :zone_count]
    second_sum = sums[:, zone_count:2 * zone_count]
    both_sum = sums[:, 2 * zone_count:]
    if slope_mode:
        imag_sum = both_sum - first_sum + second_sum
    else:
        imag_sum = first_sum - second_sum - both_sum
    combined = jnp.concatenate([first_sum + second_sum, imag_sum], 1)
    if store_out:
        return (combined,) + tuple(outs[1:])
    return combined


def panel_call(slope_mode, wavenumber, own_table, all_table, vector_rows, stored, store_out):
    own_total = own_table.shape[0]
    columns = vector_rows.shape[0]
    panel_total = all_table.shape[1]
    elements = own_total * panel_total
    stored_in = stored is not None
    operands = [wavenumber, own_table, all_table, vector_rows]
    out_shape = [jax.ShapeDtypeStruct((own_total, columns), jnp.float32)]
    matrix_bytes = 0
    if stored_in:
        operands += list(stored)
        matrix_bytes = 8 * elements
    if store_out:
        out_shape += [jax.ShapeDtypeStruct((own_total, panel_total), jnp.float32)] * 2
        matrix_bytes = 8 * elements
    vmem = pl.BlockSpec(memory_space=pltpu.VMEM)
    params = {}
    if matrix_bytes:
        params["compiler_params"] = pltpu.CompilerParams(vmem_limit_bytes=matrix_bytes + 16 * 1024 * 1024)
    if stored_in and not slope_mode:
        flops, transcendentals = 32 * elements, 0
    elif stored_in:
        flops, transcendentals = 60 * elements, 2 * elements
    else:
        flops, transcendentals = 150 * elements, 4 * elements
    return pl.pallas_call(
        functools.partial(panel_kernel, slope_mode, stored_in, store_out),
        out_shape=tuple(out_shape) if store_out else out_shape[0],
        in_specs=[pl.BlockSpec(memory_space=pltpu.SMEM)] + [vmem] * (len(operands) - 1),
        out_specs=tuple([vmem] * len(out_shape)) if store_out else vmem,
        cost_estimate=pl.CostEstimate(
            flops=flops,
            transcendentals=transcendentals,
            bytes_accessed=4 * (own_table.size + all_table.size + vector_rows.size + own_total * columns) + matrix_bytes,
        ),
        **params,
    )(*operands)


def gather_axis(vector, name):
    count = lax.axis_size(name)
    if count > 8:
        return lax.all_gather(vector, name, axis=0, tiled=True)
    index = lax.axis_index(name)
    parts = [vector]
    for shift in range(1, count):
        parts.append(lax.ppermute(vector, name, [(i, (i + shift) % count) for i in range(count)]))
    stacked = jnp.stack([parts[(-offset) % count] for offset in range(count)])
    ordered = jnp.roll(stacked, index, axis=0)
    return ordered.reshape((count * vector.shape[0],) + vector.shape[1:])


def gather_panels(vector):
    return gather_axis(gather_axis(vector, "col"), "row")


def chunk_size_of(count, limit):
    return math.gcd(count, limit)


def rows_sum(block_fn, count, limit):
    size = chunk_size_of(count, limit)
    starts = jnp.arange(count // size, dtype=jnp.int32) * size
    return jnp.sum(lax.map(lambda start: block_fn(start, size), starts), 0)


def local(
    centers,
    panel_areas,
    jump_term,
    displacement,
    design_ids,
    primal_field,
    adjoint_start,
    mic_panels,
    wavenumber,
):
    zone_count = adjoint_start.shape[1] // 2
    owned_count = centers.shape[1]
    axes = ("row", "col")
    wave_value = wavenumber[0]
    packed = jnp.concatenate([centers.T, panel_areas[:, None], adjoint_start], 1)
    gathered = gather_panels(packed)
    panel_total = gathered.shape[0]
    all_xyz = gathered[:, :3].T
    all_area = gathered[:, 3]
    start_full = gathered[:, 4:]
    all_table = gathered[:, :4].T
    own_table = jnp.concatenate(
        [centers.T, panel_areas[:, None], displacement.T, jnp.zeros((owned_count, 1), jnp.float32)], 1
    )

    store = 8 * owned_count * panel_total <= STORE_LIMIT
    saved = []

    def apply_adjoint(vector_full, vector_own):
        if store and saved:
            summed = panel_contract(False, wavenumber, own_table, all_table, vector_full, stored=saved)
        elif store:
            summed, real_part, imag_part = panel_contract(
                False, wavenumber, own_table, all_table, vector_full, store_out=True
            )
            saved.extend([real_part, imag_part])
        else:
            summed = panel_contract(False, wavenumber, own_table, all_table, vector_full)
        return panel_areas[:, None] * summed + jump_term[:, None] * vector_own

    first_panel = (
        lax.axis_index("row") * lax.axis_size("col") + lax.axis_index("col")
    ) * owned_count
    panel_ids = first_panel + jnp.arange(owned_count, dtype=jnp.int32)
    mic_hits = jnp.sum(
        (panel_ids[:, None, None] == mic_panels[None, :, :]).astype(jnp.float32), axis=2
    )
    right_side = jnp.concatenate(
        [mic_hits * primal_field[0][:, None], mic_hits * primal_field[1][:, None]], 1
    )
    residual = right_side - apply_adjoint(start_full, adjoint_start)
    residual_full = gather_panels(residual)
    start_norm = jnp.sqrt(square_sum(residual_full))
    start_scale = jnp.concatenate([start_norm, start_norm])[None, :]
    basis_one = residual / start_scale
    basis_one_full = residual_full / start_scale
    image_one = apply_adjoint(basis_one_full, basis_one)
    image_one_full = gather_panels(image_one)
    first_re, first_im = inner_parts(basis_one_full, image_one_full, zone_count)
    lean_one_full = image_one_full - complex_scale(first_re, first_im, basis_one_full, zone_count)
    lean_one = image_one - complex_scale(first_re, first_im, basis_one, zone_count)
    first_norm = jnp.sqrt(square_sum(lean_one_full))
    first_scale = jnp.concatenate([first_norm, first_norm])[None, :]
    basis_two = lean_one / first_scale
    basis_two_full = lean_one_full / first_scale
    image_two = apply_adjoint(basis_two_full, basis_two)
    image_two_full = gather_panels(image_two)
    cross_re, cross_im = inner_parts(basis_one_full, image_two_full, zone_count)
    second_re, second_im = inner_parts(basis_two_full, image_two_full, zone_count)
    lean_two_full = (
        image_two_full
        - complex_scale(cross_re, cross_im, basis_one_full, zone_count)
        - complex_scale(second_re, second_im, basis_two_full, zone_count)
    )
    second_norm = jnp.sqrt(square_sum(lean_two_full))
    coef_one_re, coef_one_im, coef_two_re, coef_two_im = least_squares(
        start_norm,
        first_re,
        first_im,
        first_norm,
        cross_re,
        cross_im,
        second_re,
        second_im,
        second_norm,
    )
    adjoint_field = (
        adjoint_start
        + complex_scale(coef_one_re, coef_one_im, basis_one, zone_count)
        + complex_scale(coef_two_re, coef_two_im, basis_two, zone_count)
    )
    field_full = (
        start_full
        + complex_scale(coef_one_re, coef_one_im, basis_one_full, zone_count)
        + complex_scale(coef_two_re, coef_two_im, basis_two_full, zone_count)
    )

    contracted = panel_contract(True, wavenumber, own_table, all_table, field_full, stored=saved or None)
    contrib = panel_areas[:, None] * (
        primal_field[0][:, None] * contracted[:, :zone_count]
        - primal_field[1][:, None] * contracted[:, zone_count:]
    )
    onehot = (design_ids[:, None] == jnp.arange(DESIGN, dtype=jnp.int32)[None, :]).astype(
        jnp.float32
    )
    local_sums = contract_first(contrib, onehot)
    sensitivity = lax.psum(lax.psum(local_sums, "col"), "row")
    return (adjoint_field, sensitivity)


def solution(mesh):
    return jax.shard_map(
        local,
        mesh=mesh,
        in_specs=(
            P(None, ("row", "col")),
            P(("row", "col")),
            P(("row", "col")),
            P(None, ("row", "col")),
            P(("row", "col")),
            P(None, ("row", "col")),
            P(("row", "col"), None),
            P(),
            P(),
        ),
        out_specs=(P(("row", "col"), None), P()),
        check_vma=False,
    )
```

```python
import functools
import math

import jax
import jax.numpy as jnp
from jax import lax
from jax.experimental import pallas as pl
from jax.experimental.pallas import tpu as pltpu
from jax.sharding import PartitionSpec as P

DESIGN = 128


highest = lax.Precision.HIGHEST
four_pi = 4.0 * math.pi


def distances(rows_xyz, rows_area, cols_xyz, cols_area):
    diff_x = rows_xyz[0][:, None] - cols_xyz[0][None, :]
    diff_y = rows_xyz[1][:, None] - cols_xyz[1][None, :]
    diff_z = rows_xyz[2][:, None] - cols_xyz[2][None, :]
    square = (
        diff_x * diff_x
        + diff_y * diff_y
        + diff_z * diff_z
        + 0.5 * (rows_area[:, None] + cols_area[None, :])
    )
    return (diff_x, diff_y, diff_z, jnp.sqrt(square))


def kernel_parts(rows_xyz, rows_area, cols_xyz, cols_area, wave_value):
    radius = distances(rows_xyz, rows_area, cols_xyz, cols_area)[3]
    phase = wave_value * radius
    factor = 1.0 / (four_pi * radius)
    return (jnp.cos(phase) * factor, jnp.sin(phase) * factor)


def slope_parts(rows_xyz, rows_area, cols_xyz, cols_area, cols_move, wave_value):
    diff_x, diff_y, diff_z, radius = distances(rows_xyz, rows_area, cols_xyz, cols_area)
    along_move = (
        diff_x * cols_move[0][None, :]
        + diff_y * cols_move[1][None, :]
        + diff_z * cols_move[2][None, :]
    )
    phase = wave_value * radius
    cosine_part = jnp.cos(phase)
    sine_part = jnp.sin(phase)
    factor = along_move / (four_pi * radius * radius * radius)
    return ((-cosine_part - phase * sine_part) * factor, (phase * cosine_part - sine_part) * factor)


def contract_first(matrix, vector):
    return lax.dot_general(matrix, vector, (((0,), (0,)), ((), ())), precision=highest)


def conj_columns(real_part, imag_part, vector, zone_count):
    left_part = contract_first(real_part, vector)
    right_part = contract_first(imag_part, vector)
    return jnp.concatenate(
        [
            left_part[:, :zone_count] + right_part[:, zone_count:],
            left_part[:, zone_count:] - right_part[:, :zone_count],
        ],
        1,
    )


def inner_parts(left_part, right_part, zone_count):
    left_re, left_im = (left_part[:, :zone_count], left_part[:, zone_count:])
    right_re, right_im = (right_part[:, :zone_count], right_part[:, zone_count:])
    return (
        jnp.sum(left_re * right_re + left_im * right_im, 0),
        jnp.sum(left_re * right_im - left_im * right_re, 0),
    )


def square_sum(vector):
    return jnp.sum(vector * vector, 0).reshape(2, -1).sum(0)


def complex_scale(scale_re, scale_im, vector, zone_count):
    vec_re, vec_im = (vector[:, :zone_count], vector[:, zone_count:])
    return jnp.concatenate(
        [scale_re * vec_re - scale_im * vec_im, scale_re * vec_im + scale_im * vec_re], 1
    )


def least_squares(
    start_norm,
    first_re,
    first_im,
    first_norm,
    cross_re,
    cross_im,
    second_re,
    second_im,
    second_norm,
):
    gram_one = first_re * first_re + first_im * first_im + first_norm * first_norm
    gram_off_re = first_re * cross_re + first_im * cross_im + first_norm * second_re
    gram_off_im = first_re * cross_im - first_im * cross_re + first_norm * second_im
    gram_two = (
        cross_re * cross_re
        + cross_im * cross_im
        + second_re * second_re
        + second_im * second_im
        + second_norm * second_norm
    )
    rhs_one_re = start_norm * first_re
    rhs_one_im = -start_norm * first_im
    rhs_two_re = start_norm * cross_re
    rhs_two_im = -start_norm * cross_im
    determinant = gram_one * gram_two - gram_off_re * gram_off_re - gram_off_im * gram_off_im
    coef_one_re = (
        gram_two * rhs_one_re - (gram_off_re * rhs_two_re - gram_off_im * rhs_two_im)
    ) / determinant
    coef_one_im = (
        gram_two * rhs_one_im - (gram_off_re * rhs_two_im + gram_off_im * rhs_two_re)
    ) / determinant
    coef_two_re = (
        gram_one * rhs_two_re - (gram_off_re * rhs_one_re + gram_off_im * rhs_one_im)
    ) / determinant
    coef_two_im = (
        gram_one * rhs_two_im - (gram_off_re * rhs_one_im - gram_off_im * rhs_one_re)
    ) / determinant
    return (coef_one_re, coef_one_im, coef_two_re, coef_two_im)


def slope_parts_t(own_xyz, own_area, own_move, all_xyz, all_area, wave_value):
    diff_x = all_xyz[0][None, :] - own_xyz[0][:, None]
    diff_y = all_xyz[1][None, :] - own_xyz[1][:, None]
    diff_z = all_xyz[2][None, :] - own_xyz[2][:, None]
    square = (
        diff_x * diff_x
        + diff_y * diff_y
        + diff_z * diff_z
        + 0.5 * (all_area[None, :] + own_area[:, None])
    )
    radius = jnp.sqrt(square)
    along_move = (
        diff_x * own_move[0][:, None]
        + diff_y * own_move[1][:, None]
        + diff_z * own_move[2][:, None]
    )
    phase = wave_value * radius
    cosine_part = jnp.cos(phase)
    sine_part = jnp.sin(phase)
    factor = along_move / (four_pi * radius * radius * radius)
    return ((-cosine_part - phase * sine_part) * factor, (phase * cosine_part - sine_part) * factor)


TWO_OVER_PI = 0.6366197723675814
HALF_PI_HI = 1.5703125
HALF_PI_MID = 4.837512969970703125e-4
HALF_PI_LO = 7.54978995489188216e-8


def sin_cos(angle):
    turns = jnp.floor(angle * TWO_OVER_PI + 0.5)
    rest = angle - turns * HALF_PI_HI
    rest = rest - turns * HALF_PI_MID
    rest = rest - turns * HALF_PI_LO
    rest2 = rest * rest
    sine = rest + rest * rest2 * (
        -1.6666654611e-1 + rest2 * (8.3321608736e-3 + rest2 * (-1.9515295891e-4))
    )
    cosine = 1.0 - 0.5 * rest2 + rest2 * rest2 * (
        4.166664568298827e-2 + rest2 * (-1.388731625493765e-3 + rest2 * 2.443315711809948e-5)
    )
    quarter = turns.astype(jnp.int32)
    swap = (quarter & 1) == 1
    sine_out = jnp.where(swap, cosine, sine)
    cosine_out = jnp.where(swap, sine, cosine)
    sine_out = jnp.where((quarter & 2) == 2, -sine_out, sine_out)
    cosine_out = jnp.where(((quarter + 1) & 2) == 2, -cosine_out, cosine_out)
    return sine_out, cosine_out


LANES = 256
STORE_LIMIT = 24 * 1024 * 1024


def panel_kernel(slope_mode, stored_in, store_out, wave_ref, own_ref, all_ref, vec_ref, *refs):
    if stored_in:
        real_ref, imag_ref, out_ref = refs
    elif store_out:
        out_ref, real_ref, imag_ref = refs
    else:
        (out_ref,) = refs
    wave_value = wave_ref[0]
    own_total = own_ref.shape[0]
    panel_total = all_ref.shape[1]
    width = LANES if panel_total % LANES == 0 else 128
    chunk_count = panel_total // width
    needs_geometry = slope_mode or not stored_in

    def row_block(block, carry):
        first = pl.multiple_of(block * 8, 8)
        rows = pl.ds(first, 8)
        own = own_ref[rows, :]
        own_x = jnp.broadcast_to(own[:, 0:1], (8, width))
        own_y = jnp.broadcast_to(own[:, 1:2], (8, width))
        own_z = jnp.broadcast_to(own[:, 2:3], (8, width))
        own_a = jnp.broadcast_to(own[:, 3:4], (8, width))
        if slope_mode:
            move_x = jnp.broadcast_to(own[:, 4:5], (8, width))
            move_y = jnp.broadcast_to(own[:, 5:6], (8, width))
            move_z = jnp.broadcast_to(own[:, 6:7], (8, width))

        def lane_block(chunk, sums):
            start = pl.multiple_of(chunk * width, width)
            span = pl.ds(start, width)
            if needs_geometry:
                diff_x = all_ref[0:1, span] - own_x
                diff_y = all_ref[1:2, span] - own_y
                diff_z = all_ref[2:3, span] - own_z
                square = (
                    diff_x * diff_x
                    + diff_y * diff_y
                    + diff_z * diff_z
                    + 0.5 * (all_ref[3:4, span] + own_a)
                )
                inverse = lax.rsqrt(square)
                radius = square * inverse
                phase = wave_value * radius
            if stored_in:
                real_part = real_ref[rows, span]
                imag_part = imag_ref[rows, span]
                if slope_mode:
                    along_move = diff_x * move_x + diff_y * move_y + diff_z * move_z
                    factor = along_move * (inverse * inverse)
                    first_part = (-real_part - phase * imag_part) * factor
                    second_part = (phase * real_part - imag_part) * factor
                else:
                    first_part = real_part
                    second_part = imag_part
            else:
                sine_part, cosine_part = sin_cos(phase)
                if slope_mode:
                    along_move = diff_x * move_x + diff_y * move_y + diff_z * move_z
                    factor = along_move * (inverse * inverse * inverse) * (1.0 / four_pi)
                    first_part = (-cosine_part - phase * sine_part) * factor
                    second_part = (phase * cosine_part - sine_part) * factor
                else:
                    factor = inverse * (1.0 / four_pi)
                    first_part = cosine_part * factor
                    second_part = sine_part * factor
                if store_out:
                    real_ref[rows, span] = first_part
                    imag_ref[rows, span] = second_part
            zone_count = len(sums) // 3
            both_parts = first_part + second_part
            new_sums = []
            for zone in range(zone_count):
                new_sums.append(sums[zone] + first_part * vec_ref[zone:zone + 1, span])
            for zone in range(zone_count, 2 * zone_count):
                new_sums.append(sums[zone] + second_part * vec_ref[zone:zone + 1, span])
            for zone in range(2 * zone_count, 3 * zone_count):
                new_sums.append(sums[zone] + both_parts * vec_ref[zone:zone + 1, span])
            return tuple(new_sums)

        columns = vec_ref.shape[0]
        zeros = tuple(jnp.zeros((8, width), jnp.float32) for _ in range(columns))
        sums = lax.fori_loop(0, chunk_count, lane_block, zeros, unroll=4 if stored_in and not slope_mode else 3)
        lane = lax.broadcasted_iota(jnp.int32, (8, columns), 1)
        result = jnp.zeros((8, columns), jnp.float32)
        for column in range(columns):
            total = jnp.sum(sums[column], axis=1, keepdims=True)
            result = jnp.where(lane == column, total, result)
        out_ref[rows, :] = result
        return carry

    lax.fori_loop(0, own_total // 8, row_block, 0)


def panel_contract(slope_mode, wavenumber, own_table, all_table, vector_full, stored=None, store_out=False):
    zone_count = vector_full.shape[1] // 2
    vector_rows = jnp.concatenate(
        [vector_full.T, (vector_full[:, :zone_count] - vector_full[:, zone_count:]).T], 0
    )
    outs = panel_call(slope_mode, wavenumber, own_table, all_table, vector_rows, stored, store_out)
    sums = outs[0] if store_out else outs
    first_sum = sums[:, :zone_count]
    second_sum = sums[:, zone_count:2 * zone_count]
    both_sum = sums[:, 2 * zone_count:]
    if slope_mode:
        imag_sum = both_sum - first_sum + second_sum
    else:
        imag_sum = first_sum - second_sum - both_sum
    combined = jnp.concatenate([first_sum + second_sum, imag_sum], 1)
    if store_out:
        return (combined,) + tuple(outs[1:])
    return combined


def panel_call(slope_mode, wavenumber, own_table, all_table, vector_rows, stored, store_out):
    own_total = own_table.shape[0]
    columns = vector_rows.shape[0]
    panel_total = all_table.shape[1]
    elements = own_total * panel_total
    stored_in = stored is not None
    operands = [wavenumber, own_table, all_table, vector_rows]
    out_shape = [jax.ShapeDtypeStruct((own_total, columns), jnp.float32)]
    matrix_bytes = 0
    if stored_in:
        operands += list(stored)
        matrix_bytes = 8 * elements
    if store_out:
        out_shape += [jax.ShapeDtypeStruct((own_total, panel_total), jnp.float32)] * 2
        matrix_bytes = 8 * elements
    vmem = pl.BlockSpec(memory_space=pltpu.VMEM)
    params = {}
    if matrix_bytes:
        params["compiler_params"] = pltpu.CompilerParams(vmem_limit_bytes=matrix_bytes + 16 * 1024 * 1024)
    if stored_in and not slope_mode:
        flops, transcendentals = 32 * elements, 0
    elif stored_in:
        flops, transcendentals = 60 * elements, 2 * elements
    else:
        flops, transcendentals = 150 * elements, 4 * elements
    return pl.pallas_call(
        functools.partial(panel_kernel, slope_mode, stored_in, store_out),
        out_shape=tuple(out_shape) if store_out else out_shape[0],
        in_specs=[pl.BlockSpec(memory_space=pltpu.SMEM)] + [vmem] * (len(operands) - 1),
        out_specs=tuple([vmem] * len(out_shape)) if store_out else vmem,
        cost_estimate=pl.CostEstimate(
            flops=flops,
            transcendentals=transcendentals,
            bytes_accessed=4 * (own_table.size + all_table.size + vector_rows.size + own_total * columns) + matrix_bytes,
        ),
        **params,
    )(*operands)


def gather_axis(vector, name):
    count = lax.axis_size(name)
    if count > 8:
        return lax.all_gather(vector, name, axis=0, tiled=True)
    index = lax.axis_index(name)
    parts = [vector]
    for shift in range(1, count):
        parts.append(lax.ppermute(vector, name, [(i, (i + shift) % count) for i in range(count)]))
    stacked = jnp.stack([parts[(-offset) % count] for offset in range(count)])
    ordered = jnp.roll(stacked, index, axis=0)
    return ordered.reshape((count * vector.shape[0],) + vector.shape[1:])


def gather_panels(vector):
    return gather_axis(gather_axis(vector, "col"), "row")


def chunk_size_of(count, limit):
    return math.gcd(count, limit)


def rows_sum(block_fn, count, limit):
    size = chunk_size_of(count, limit)
    starts = jnp.arange(count // size, dtype=jnp.int32) * size
    return jnp.sum(lax.map(lambda start: block_fn(start, size), starts), 0)


def local(
    centers,
    panel_areas,
    jump_term,
    displacement,
    design_ids,
    primal_field,
    adjoint_start,
    mic_panels,
    wavenumber,
):
    zone_count = adjoint_start.shape[1] // 2
    owned_count = centers.shape[1]
    axes = ("row", "col")
    wave_value = wavenumber[0]
    packed = jnp.concatenate([centers.T, panel_areas[:, None], adjoint_start], 1)
    gathered = gather_panels(packed)
    panel_total = gathered.shape[0]
    all_xyz = gathered[:, :3].T
    all_area = gathered[:, 3]
    start_full = gathered[:, 4:]
    all_table = gathered[:, :4].T
    own_table = jnp.concatenate(
        [centers.T, panel_areas[:, None], displacement.T, jnp.zeros((owned_count, 1), jnp.float32)], 1
    )

    store = 8 * owned_count * panel_total <= STORE_LIMIT
    saved = []

    def apply_adjoint(vector_full, vector_own):
        if store and saved:
            summed = panel_contract(False, wavenumber, own_table, all_table, vector_full, stored=saved)
        elif store:
            summed, real_part, imag_part = panel_contract(
                False, wavenumber, own_table, all_table, vector_full, store_out=True
            )
            saved.extend([real_part, imag_part])
        else:
            summed = panel_contract(False, wavenumber, own_table, all_table, vector_full)
        return panel_areas[:, None] * summed + jump_term[:, None] * vector_own

    first_panel = (
        lax.axis_index("row") * lax.axis_size("col") + lax.axis_index("col")
    ) * owned_count
    panel_ids = first_panel + jnp.arange(owned_count, dtype=jnp.int32)
    mic_hits = jnp.sum(
        (panel_ids[:, None, None] == mic_panels[None, :, :]).astype(jnp.float32), axis=2
    )
    right_side = jnp.concatenate(
        [mic_hits * primal_field[0][:, None], mic_hits * primal_field[1][:, None]], 1
    )
    residual = right_side - apply_adjoint(start_full, adjoint_start)
    residual_full = gather_panels(residual)
    start_norm = jnp.sqrt(square_sum(residual_full))
    start_scale = jnp.concatenate([start_norm, start_norm])[None, :]
    basis_one = residual / start_scale
    basis_one_full = residual_full / start_scale
    image_one = apply_adjoint(basis_one_full, basis_one)
    image_one_full = gather_panels(image_one)
    first_re, first_im = inner_parts(basis_one_full, image_one_full, zone_count)
    lean_one_full = image_one_full - complex_scale(first_re, first_im, basis_one_full, zone_count)
    lean_one = image_one - complex_scale(first_re, first_im, basis_one, zone_count)
    first_norm = jnp.sqrt(square_sum(lean_one_full))
    first_scale = jnp.concatenate([first_norm, first_norm])[None, :]
    basis_two = lean_one / first_scale
    basis_two_full = lean_one_full / first_scale
    image_two = apply_adjoint(basis_two_full, basis_two)
    image_two_full = gather_panels(image_two)
    cross_re, cross_im = inner_parts(basis_one_full, image_two_full, zone_count)
    second_re, second_im = inner_parts(basis_two_full, image_two_full, zone_count)
    lean_two_full = (
        image_two_full
        - complex_scale(cross_re, cross_im, basis_one_full, zone_count)
        - complex_scale(second_re, second_im, basis_two_full, zone_count)
    )
    second_norm = jnp.sqrt(square_sum(lean_two_full))
    coef_one_re, coef_one_im, coef_two_re, coef_two_im = least_squares(
        start_norm,
        first_re,
        first_im,
        first_norm,
        cross_re,
        cross_im,
        second_re,
        second_im,
        second_norm,
    )
    adjoint_field = (
        adjoint_start
        + complex_scale(coef_one_re, coef_one_im, basis_one, zone_count)
        + complex_scale(coef_two_re, coef_two_im, basis_two, zone_count)
    )
    field_full = (
        start_full
        + complex_scale(coef_one_re, coef_one_im, basis_one_full, zone_count)
        + complex_scale(coef_two_re, coef_two_im, basis_two_full, zone_count)
    )

    contracted = panel_contract(True, wavenumber, own_table, all_table, field_full, stored=saved or None)
    contrib = panel_areas[:, None] * (
        primal_field[0][:, None] * contracted[:, :zone_count]
        - primal_field[1][:, None] * contracted[:, zone_count:]
    )
    onehot = (design_ids[:, None] == jnp.arange(DESIGN, dtype=jnp.int32)[None, :]).astype(
        jnp.float32
    )
    local_sums = contract_first(contrib, onehot)
    sensitivity = lax.psum(lax.psum(local_sums, "col"), "row")
    return (adjoint_field, sensitivity)


def solution(mesh):
    return jax.shard_map(
        local,
        mesh=mesh,
        in_specs=(
            P(None, ("row", "col")),
            P(("row", "col")),
            P(("row", "col")),
            P(None, ("row", "col")),
            P(("row", "col")),
            P(None, ("row", "col")),
            P(("row", "col"), None),
            P(),
            P(),
        ),
        out_specs=(P(("row", "col"), None), P()),
        check_vma=False,
    )
```

```python
import functools
import math

import jax
import jax.numpy as jnp
from jax import lax
from jax.experimental import pallas as pl
from jax.experimental.pallas import tpu as pltpu
from jax.sharding import PartitionSpec as P

DESIGN = 128


highest = lax.Precision.HIGHEST
four_pi = 4.0 * math.pi


def distances(rows_xyz, rows_area, cols_xyz, cols_area):
    diff_x = rows_xyz[0][:, None] - cols_xyz[0][None, :]
    diff_y = rows_xyz[1][:, None] - cols_xyz[1][None, :]
    diff_z = rows_xyz[2][:, None] - cols_xyz[2][None, :]
    square = (
        diff_x * diff_x
        + diff_y * diff_y
        + diff_z * diff_z
        + 0.5 * (rows_area[:, None] + cols_area[None, :])
    )
    return (diff_x, diff_y, diff_z, jnp.sqrt(square))


def kernel_parts(rows_xyz, rows_area, cols_xyz, cols_area, wave_value):
    radius = distances(rows_xyz, rows_area, cols_xyz, cols_area)[3]
    phase = wave_value * radius
    factor = 1.0 / (four_pi * radius)
    return (jnp.cos(phase) * factor, jnp.sin(phase) * factor)


def slope_parts(rows_xyz, rows_area, cols_xyz, cols_area, cols_move, wave_value):
    diff_x, diff_y, diff_z, radius = distances(rows_xyz, rows_area, cols_xyz, cols_area)
    along_move = (
        diff_x * cols_move[0][None, :]
        + diff_y * cols_move[1][None, :]
        + diff_z * cols_move[2][None, :]
    )
    phase = wave_value * radius
    cosine_part = jnp.cos(phase)
    sine_part = jnp.sin(phase)
    factor = along_move / (four_pi * radius * radius * radius)
    return ((-cosine_part - phase * sine_part) * factor, (phase * cosine_part - sine_part) * factor)


def contract_first(matrix, vector):
    return lax.dot_general(matrix, vector, (((0,), (0,)), ((), ())), precision=highest)


def conj_columns(real_part, imag_part, vector, zone_count):
    left_part = contract_first(real_part, vector)
    right_part = contract_first(imag_part, vector)
    return jnp.concatenate(
        [
            left_part[:, :zone_count] + right_part[:, zone_count:],
            left_part[:, zone_count:] - right_part[:, :zone_count],
        ],
        1,
    )


def inner_parts(left_part, right_part, zone_count):
    left_re, left_im = (left_part[:, :zone_count], left_part[:, zone_count:])
    right_re, right_im = (right_part[:, :zone_count], right_part[:, zone_count:])
    return (
        jnp.sum(left_re * right_re + left_im * right_im, 0),
        jnp.sum(left_re * right_im - left_im * right_re, 0),
    )


def square_sum(vector):
    return jnp.sum(vector * vector, 0).reshape(2, -1).sum(0)


def complex_scale(scale_re, scale_im, vector, zone_count):
    vec_re, vec_im = (vector[:, :zone_count], vector[:, zone_count:])
    return jnp.concatenate(
        [scale_re * vec_re - scale_im * vec_im, scale_re * vec_im + scale_im * vec_re], 1
    )


def least_squares(
    start_norm,
    first_re,
    first_im,
    first_norm,
    cross_re,
    cross_im,
    second_re,
    second_im,
    second_norm,
):
    gram_one = first_re * first_re + first_im * first_im + first_norm * first_norm
    gram_off_re = first_re * cross_re + first_im * cross_im + first_norm * second_re
    gram_off_im = first_re * cross_im - first_im * cross_re + first_norm * second_im
    gram_two = (
        cross_re * cross_re
        + cross_im * cross_im
        + second_re * second_re
        + second_im * second_im
        + second_norm * second_norm
    )
    rhs_one_re = start_norm * first_re
    rhs_one_im = -start_norm * first_im
    rhs_two_re = start_norm * cross_re
    rhs_two_im = -start_norm * cross_im
    determinant = gram_one * gram_two - gram_off_re * gram_off_re - gram_off_im * gram_off_im
    coef_one_re = (
        gram_two * rhs_one_re - (gram_off_re * rhs_two_re - gram_off_im * rhs_two_im)
    ) / determinant
    coef_one_im = (
        gram_two * rhs_one_im - (gram_off_re * rhs_two_im + gram_off_im * rhs_two_re)
    ) / determinant
    coef_two_re = (
        gram_one * rhs_two_re - (gram_off_re * rhs_one_re + gram_off_im * rhs_one_im)
    ) / determinant
    coef_two_im = (
        gram_one * rhs_two_im - (gram_off_re * rhs_one_im - gram_off_im * rhs_one_re)
    ) / determinant
    return (coef_one_re, coef_one_im, coef_two_re, coef_two_im)


def slope_parts_t(own_xyz, own_area, own_move, all_xyz, all_area, wave_value):
    diff_x = all_xyz[0][None, :] - own_xyz[0][:, None]
    diff_y = all_xyz[1][None, :] - own_xyz[1][:, None]
    diff_z = all_xyz[2][None, :] - own_xyz[2][:, None]
    square = (
        diff_x * diff_x
        + diff_y * diff_y
        + diff_z * diff_z
        + 0.5 * (all_area[None, :] + own_area[:, None])
    )
    radius = jnp.sqrt(square)
    along_move = (
        diff_x * own_move[0][:, None]
        + diff_y * own_move[1][:, None]
        + diff_z * own_move[2][:, None]
    )
    phase = wave_value * radius
    cosine_part = jnp.cos(phase)
    sine_part = jnp.sin(phase)
    factor = along_move / (four_pi * radius * radius * radius)
    return ((-cosine_part - phase * sine_part) * factor, (phase * cosine_part - sine_part) * factor)


TWO_OVER_PI = 0.6366197723675814
HALF_PI_HI = 1.5703125
HALF_PI_MID = 4.837512969970703125e-4
HALF_PI_LO = 7.54978995489188216e-8


def sin_cos(angle):
    turns = jnp.floor(angle * TWO_OVER_PI + 0.5)
    rest = angle - turns * HALF_PI_HI
    rest = rest - turns * HALF_PI_MID
    rest = rest - turns * HALF_PI_LO
    rest2 = rest * rest
    sine = rest + rest * rest2 * (
        -1.6666654611e-1 + rest2 * (8.3321608736e-3 + rest2 * (-1.9515295891e-4))
    )
    cosine = 1.0 - 0.5 * rest2 + rest2 * rest2 * (
        4.166664568298827e-2 + rest2 * (-1.388731625493765e-3 + rest2 * 2.443315711809948e-5)
    )
    quarter = turns.astype(jnp.int32)
    swap = (quarter & 1) == 1
    sine_out = jnp.where(swap, cosine, sine)
    cosine_out = jnp.where(swap, sine, cosine)
    sine_out = jnp.where((quarter & 2) == 2, -sine_out, sine_out)
    cosine_out = jnp.where(((quarter + 1) & 2) == 2, -cosine_out, cosine_out)
    return sine_out, cosine_out


LANES = 256
STORE_LIMIT = 24 * 1024 * 1024


def panel_kernel(slope_mode, stored_in, store_out, wave_ref, own_ref, all_ref, vec_ref, *refs):
    if stored_in:
        real_hbm, imag_hbm, out_ref, real_buf, imag_buf, sems = refs
    elif store_out:
        out_ref, real_hbm, imag_hbm, real_buf, imag_buf, sems = refs
    else:
        (out_ref,) = refs
    block_count = own_ref.shape[0] // 8

    def copies(block, slot):
        rows = pl.ds(pl.multiple_of(block * 8, 8), 8)
        pairs = [(real_hbm, real_buf), (imag_hbm, imag_buf)]
        if stored_in:
            return [pltpu.make_async_copy(hbm.at[rows], buf.at[slot], sems.at[k, slot]) for k, (hbm, buf) in enumerate(pairs)]
        return [pltpu.make_async_copy(buf.at[slot], hbm.at[rows], sems.at[k, slot]) for k, (hbm, buf) in enumerate(pairs)]
    wave_value = wave_ref[0]
    own_total = own_ref.shape[0]
    panel_total = all_ref.shape[1]
    width = LANES if panel_total % LANES == 0 else 128
    chunk_count = panel_total // width
    needs_geometry = slope_mode or not stored_in

    def row_block(block, carry):
        first = pl.multiple_of(block * 8, 8)
        rows = pl.ds(first, 8)
        slot = lax.rem(block, 2)
        if stored_in:
            for copy in copies(block, slot):
                copy.wait()

            @pl.when(block + 1 < block_count)
            def _():
                for copy in copies(block + 1, 1 - slot):
                    copy.start()

        if store_out:

            @pl.when(block >= 2)
            def _():
                for copy in copies(block - 2, slot):
                    copy.wait()

        own = own_ref[rows, :]
        own_x = jnp.broadcast_to(own[:, 0:1], (8, width))
        own_y = jnp.broadcast_to(own[:, 1:2], (8, width))
        own_z = jnp.broadcast_to(own[:, 2:3], (8, width))
        own_a = jnp.broadcast_to(own[:, 3:4], (8, width))
        if slope_mode:
            move_x = jnp.broadcast_to(own[:, 4:5], (8, width))
            move_y = jnp.broadcast_to(own[:, 5:6], (8, width))
            move_z = jnp.broadcast_to(own[:, 6:7], (8, width))

        def lane_block(chunk, sums):
            start = pl.multiple_of(chunk * width, width)
            span = pl.ds(start, width)
            if needs_geometry:
                diff_x = all_ref[0:1, span] - own_x
                diff_y = all_ref[1:2, span] - own_y
                diff_z = all_ref[2:3, span] - own_z
                square = (
                    diff_x * diff_x
                    + diff_y * diff_y
                    + diff_z * diff_z
                    + 0.5 * (all_ref[3:4, span] + own_a)
                )
                inverse = lax.rsqrt(square)
                radius = square * inverse
                phase = wave_value * radius
            if stored_in:
                real_part = real_buf[slot, :, span]
                imag_part = imag_buf[slot, :, span]
                if slope_mode:
                    along_move = diff_x * move_x + diff_y * move_y + diff_z * move_z
                    factor = along_move * (inverse * inverse)
                    first_part = (-real_part - phase * imag_part) * factor
                    second_part = (phase * real_part - imag_part) * factor
                else:
                    first_part = real_part
                    second_part = imag_part
            else:
                sine_part, cosine_part = sin_cos(phase)
                if slope_mode:
                    along_move = diff_x * move_x + diff_y * move_y + diff_z * move_z
                    factor = along_move * (inverse * inverse * inverse) * (1.0 / four_pi)
                    first_part = (-cosine_part - phase * sine_part) * factor
                    second_part = (phase * cosine_part - sine_part) * factor
                else:
                    factor = inverse * (1.0 / four_pi)
                    first_part = cosine_part * factor
                    second_part = sine_part * factor
                if store_out:
                    real_buf[slot, :, span] = first_part
                    imag_buf[slot, :, span] = second_part
            zone_count = len(sums) // 3
            both_parts = first_part + second_part
            new_sums = []
            for zone in range(zone_count):
                new_sums.append(sums[zone] + first_part * vec_ref[zone:zone + 1, span])
            for zone in range(zone_count, 2 * zone_count):
                new_sums.append(sums[zone] + second_part * vec_ref[zone:zone + 1, span])
            for zone in range(2 * zone_count, 3 * zone_count):
                new_sums.append(sums[zone] + both_parts * vec_ref[zone:zone + 1, span])
            return tuple(new_sums)

        columns = vec_ref.shape[0]
        zeros = tuple(jnp.zeros((8, width), jnp.float32) for _ in range(columns))
        sums = lax.fori_loop(0, chunk_count, lane_block, zeros, unroll=4 if stored_in and not slope_mode else 3)
        lane = lax.broadcasted_iota(jnp.int32, (8, columns), 1)
        result = jnp.zeros((8, columns), jnp.float32)
        for column in range(columns):
            total = jnp.sum(sums[column], axis=1, keepdims=True)
            result = jnp.where(lane == column, total, result)
        out_ref[rows, :] = result
        if store_out:
            for copy in copies(block, slot):
                copy.start()
        return carry

    if stored_in:
        for copy in copies(0, 0):
            copy.start()
    lax.fori_loop(0, block_count, row_block, 0)
    if store_out:
        for block in range(max(0, block_count - 2), block_count):
            for copy in copies(block, block % 2):
                copy.wait()


def panel_contract(slope_mode, wavenumber, own_table, all_table, vector_full, stored=None, store_out=False):
    zone_count = vector_full.shape[1] // 2
    vector_rows = jnp.concatenate(
        [vector_full.T, (vector_full[:, :zone_count] - vector_full[:, zone_count:]).T], 0
    )
    outs = panel_call(slope_mode, wavenumber, own_table, all_table, vector_rows, stored, store_out)
    sums = outs[0] if store_out else outs
    first_sum = sums[:, :zone_count]
    second_sum = sums[:, zone_count:2 * zone_count]
    both_sum = sums[:, 2 * zone_count:]
    if slope_mode:
        imag_sum = both_sum - first_sum + second_sum
    else:
        imag_sum = first_sum - second_sum - both_sum
    combined = jnp.concatenate([first_sum + second_sum, imag_sum], 1)
    if store_out:
        return (combined,) + tuple(outs[1:])
    return combined


def panel_call(slope_mode, wavenumber, own_table, all_table, vector_rows, stored, store_out):
    own_total = own_table.shape[0]
    columns = vector_rows.shape[0]
    panel_total = all_table.shape[1]
    elements = own_total * panel_total
    stored_in = stored is not None
    operands = [wavenumber, own_table, all_table, vector_rows]
    out_shape = [jax.ShapeDtypeStruct((own_total, columns), jnp.float32)]
    matrix_bytes = 0
    if stored_in:
        operands += list(stored)
        matrix_bytes = 8 * elements
    if store_out:
        out_shape += [jax.ShapeDtypeStruct((own_total, panel_total), jnp.float32)] * 2
        matrix_bytes = 8 * elements
    vmem = pl.BlockSpec(memory_space=pltpu.VMEM)
    hbm = pl.BlockSpec(memory_space=pl.ANY)
    params = {}
    if matrix_bytes:
        params["scratch_shapes"] = [
            pltpu.VMEM((2, 8, panel_total), jnp.float32),
            pltpu.VMEM((2, 8, panel_total), jnp.float32),
            pltpu.SemaphoreType.DMA((2, 2)),
        ]
    if stored_in and not slope_mode:
        flops, transcendentals = 32 * elements, 0
    elif stored_in:
        flops, transcendentals = 60 * elements, 2 * elements
    else:
        flops, transcendentals = 150 * elements, 4 * elements
    return pl.pallas_call(
        functools.partial(panel_kernel, slope_mode, stored_in, store_out),
        out_shape=tuple(out_shape) if store_out else out_shape[0],
        in_specs=[pl.BlockSpec(memory_space=pltpu.SMEM)] + [vmem] * 3 + [hbm] * (len(operands) - 4),
        out_specs=tuple([vmem] + [hbm] * (len(out_shape) - 1)) if store_out else vmem,
        cost_estimate=pl.CostEstimate(
            flops=flops,
            transcendentals=transcendentals,
            bytes_accessed=4 * (own_table.size + all_table.size + vector_rows.size + own_total * columns) + matrix_bytes,
        ),
        **params,
    )(*operands)


def gather_axis(vector, name):
    count = lax.axis_size(name)
    if count > 8:
        return lax.all_gather(vector, name, axis=0, tiled=True)
    index = lax.axis_index(name)
    parts = [vector]
    for shift in range(1, count):
        parts.append(lax.ppermute(vector, name, [(i, (i + shift) % count) for i in range(count)]))
    stacked = jnp.stack([parts[(-offset) % count] for offset in range(count)])
    ordered = jnp.roll(stacked, index, axis=0)
    return ordered.reshape((count * vector.shape[0],) + vector.shape[1:])


def gather_panels(vector):
    return gather_axis(gather_axis(vector, "col"), "row")


def chunk_size_of(count, limit):
    return math.gcd(count, limit)


def rows_sum(block_fn, count, limit):
    size = chunk_size_of(count, limit)
    starts = jnp.arange(count // size, dtype=jnp.int32) * size
    return jnp.sum(lax.map(lambda start: block_fn(start, size), starts), 0)


def local(
    centers,
    panel_areas,
    jump_term,
    displacement,
    design_ids,
    primal_field,
    adjoint_start,
    mic_panels,
    wavenumber,
):
    zone_count = adjoint_start.shape[1] // 2
    owned_count = centers.shape[1]
    axes = ("row", "col")
    wave_value = wavenumber[0]
    packed = jnp.concatenate([centers.T, panel_areas[:, None], adjoint_start], 1)
    gathered = gather_panels(packed)
    panel_total = gathered.shape[0]
    all_xyz = gathered[:, :3].T
    all_area = gathered[:, 3]
    start_full = gathered[:, 4:]
    all_table = gathered[:, :4].T
    own_table = jnp.concatenate(
        [centers.T, panel_areas[:, None], displacement.T, jnp.zeros((owned_count, 1), jnp.float32)], 1
    )

    store = 8 * owned_count * panel_total <= STORE_LIMIT
    saved = []

    def apply_adjoint(vector_full, vector_own):
        if store and saved:
            summed = panel_contract(False, wavenumber, own_table, all_table, vector_full, stored=saved)
        elif store:
            summed, real_part, imag_part = panel_contract(
                False, wavenumber, own_table, all_table, vector_full, store_out=True
            )
            saved.extend([real_part, imag_part])
        else:
            summed = panel_contract(False, wavenumber, own_table, all_table, vector_full)
        return panel_areas[:, None] * summed + jump_term[:, None] * vector_own

    first_panel = (
        lax.axis_index("row") * lax.axis_size("col") + lax.axis_index("col")
    ) * owned_count
    panel_ids = first_panel + jnp.arange(owned_count, dtype=jnp.int32)
    mic_hits = jnp.sum(
        (panel_ids[:, None, None] == mic_panels[None, :, :]).astype(jnp.float32), axis=2
    )
    right_side = jnp.concatenate(
        [mic_hits * primal_field[0][:, None], mic_hits * primal_field[1][:, None]], 1
    )
    residual = right_side - apply_adjoint(start_full, adjoint_start)
    residual_full = gather_panels(residual)
    start_norm = jnp.sqrt(square_sum(residual_full))
    start_scale = jnp.concatenate([start_norm, start_norm])[None, :]
    basis_one = residual / start_scale
    basis_one_full = residual_full / start_scale
    image_one = apply_adjoint(basis_one_full, basis_one)
    image_one_full = gather_panels(image_one)
    first_re, first_im = inner_parts(basis_one_full, image_one_full, zone_count)
    lean_one_full = image_one_full - complex_scale(first_re, first_im, basis_one_full, zone_count)
    lean_one = image_one - complex_scale(first_re, first_im, basis_one, zone_count)
    first_norm = jnp.sqrt(square_sum(lean_one_full))
    first_scale = jnp.concatenate([first_norm, first_norm])[None, :]
    basis_two = lean_one / first_scale
    basis_two_full = lean_one_full / first_scale
    image_two = apply_adjoint(basis_two_full, basis_two)
    image_two_full = gather_panels(image_two)
    cross_re, cross_im = inner_parts(basis_one_full, image_two_full, zone_count)
    second_re, second_im = inner_parts(basis_two_full, image_two_full, zone_count)
    lean_two_full = (
        image_two_full
        - complex_scale(cross_re, cross_im, basis_one_full, zone_count)
        - complex_scale(second_re, second_im, basis_two_full, zone_count)
    )
    second_norm = jnp.sqrt(square_sum(lean_two_full))
    coef_one_re, coef_one_im, coef_two_re, coef_two_im = least_squares(
        start_norm,
        first_re,
        first_im,
        first_norm,
        cross_re,
        cross_im,
        second_re,
        second_im,
        second_norm,
    )
    adjoint_field = (
        adjoint_start
        + complex_scale(coef_one_re, coef_one_im, basis_one, zone_count)
        + complex_scale(coef_two_re, coef_two_im, basis_two, zone_count)
    )
    field_full = (
        start_full
        + complex_scale(coef_one_re, coef_one_im, basis_one_full, zone_count)
        + complex_scale(coef_two_re, coef_two_im, basis_two_full, zone_count)
    )

    contracted = panel_contract(True, wavenumber, own_table, all_table, field_full, stored=saved or None)
    contrib = panel_areas[:, None] * (
        primal_field[0][:, None] * contracted[:, :zone_count]
        - primal_field[1][:, None] * contracted[:, zone_count:]
    )
    onehot = (design_ids[:, None] == jnp.arange(DESIGN, dtype=jnp.int32)[None, :]).astype(
        jnp.float32
    )
    local_sums = contract_first(contrib, onehot)
    sensitivity = lax.psum(lax.psum(local_sums, "col"), "row")
    return (adjoint_field, sensitivity)


def solution(mesh):
    return jax.shard_map(
        local,
        mesh=mesh,
        in_specs=(
            P(None, ("row", "col")),
            P(("row", "col")),
            P(("row", "col")),
            P(None, ("row", "col")),
            P(("row", "col")),
            P(None, ("row", "col")),
            P(("row", "col"), None),
            P(),
            P(),
        ),
        out_specs=(P(("row", "col"), None), P()),
        check_vma=False,
    )
```

```python
import functools
import math

import jax
import jax.numpy as jnp
from jax import lax
from jax.experimental import pallas as pl
from jax.experimental.pallas import tpu as pltpu
from jax.sharding import PartitionSpec as P

DESIGN = 128


highest = lax.Precision.HIGHEST
four_pi = 4.0 * math.pi


def distances(rows_xyz, rows_area, cols_xyz, cols_area):
    diff_x = rows_xyz[0][:, None] - cols_xyz[0][None, :]
    diff_y = rows_xyz[1][:, None] - cols_xyz[1][None, :]
    diff_z = rows_xyz[2][:, None] - cols_xyz[2][None, :]
    square = (
        diff_x * diff_x
        + diff_y * diff_y
        + diff_z * diff_z
        + 0.5 * (rows_area[:, None] + cols_area[None, :])
    )
    return (diff_x, diff_y, diff_z, jnp.sqrt(square))


def kernel_parts(rows_xyz, rows_area, cols_xyz, cols_area, wave_value):
    radius = distances(rows_xyz, rows_area, cols_xyz, cols_area)[3]
    phase = wave_value * radius
    factor = 1.0 / (four_pi * radius)
    return (jnp.cos(phase) * factor, jnp.sin(phase) * factor)


def slope_parts(rows_xyz, rows_area, cols_xyz, cols_area, cols_move, wave_value):
    diff_x, diff_y, diff_z, radius = distances(rows_xyz, rows_area, cols_xyz, cols_area)
    along_move = (
        diff_x * cols_move[0][None, :]
        + diff_y * cols_move[1][None, :]
        + diff_z * cols_move[2][None, :]
    )
    phase = wave_value * radius
    cosine_part = jnp.cos(phase)
    sine_part = jnp.sin(phase)
    factor = along_move / (four_pi * radius * radius * radius)
    return ((-cosine_part - phase * sine_part) * factor, (phase * cosine_part - sine_part) * factor)


def contract_first(matrix, vector):
    return lax.dot_general(matrix, vector, (((0,), (0,)), ((), ())), precision=highest)


def conj_columns(real_part, imag_part, vector, zone_count):
    left_part = contract_first(real_part, vector)
    right_part = contract_first(imag_part, vector)
    return jnp.concatenate(
        [
            left_part[:, :zone_count] + right_part[:, zone_count:],
            left_part[:, zone_count:] - right_part[:, :zone_count],
        ],
        1,
    )


def inner_parts(left_part, right_part, zone_count):
    left_re, left_im = (left_part[:, :zone_count], left_part[:, zone_count:])
    right_re, right_im = (right_part[:, :zone_count], right_part[:, zone_count:])
    return (
        jnp.sum(left_re * right_re + left_im * right_im, 0),
        jnp.sum(left_re * right_im - left_im * right_re, 0),
    )


def square_sum(vector):
    return jnp.sum(vector * vector, 0).reshape(2, -1).sum(0)


def complex_scale(scale_re, scale_im, vector, zone_count):
    vec_re, vec_im = (vector[:, :zone_count], vector[:, zone_count:])
    return jnp.concatenate(
        [scale_re * vec_re - scale_im * vec_im, scale_re * vec_im + scale_im * vec_re], 1
    )


def least_squares(
    start_norm,
    first_re,
    first_im,
    first_norm,
    cross_re,
    cross_im,
    second_re,
    second_im,
    second_norm,
):
    gram_one = first_re * first_re + first_im * first_im + first_norm * first_norm
    gram_off_re = first_re * cross_re + first_im * cross_im + first_norm * second_re
    gram_off_im = first_re * cross_im - first_im * cross_re + first_norm * second_im
    gram_two = (
        cross_re * cross_re
        + cross_im * cross_im
        + second_re * second_re
        + second_im * second_im
        + second_norm * second_norm
    )
    rhs_one_re = start_norm * first_re
    rhs_one_im = -start_norm * first_im
    rhs_two_re = start_norm * cross_re
    rhs_two_im = -start_norm * cross_im
    determinant = gram_one * gram_two - gram_off_re * gram_off_re - gram_off_im * gram_off_im
    coef_one_re = (
        gram_two * rhs_one_re - (gram_off_re * rhs_two_re - gram_off_im * rhs_two_im)
    ) / determinant
    coef_one_im = (
        gram_two * rhs_one_im - (gram_off_re * rhs_two_im + gram_off_im * rhs_two_re)
    ) / determinant
    coef_two_re = (
        gram_one * rhs_two_re - (gram_off_re * rhs_one_re + gram_off_im * rhs_one_im)
    ) / determinant
    coef_two_im = (
        gram_one * rhs_two_im - (gram_off_re * rhs_one_im - gram_off_im * rhs_one_re)
    ) / determinant
    return (coef_one_re, coef_one_im, coef_two_re, coef_two_im)


def slope_parts_t(own_xyz, own_area, own_move, all_xyz, all_area, wave_value):
    diff_x = all_xyz[0][None, :] - own_xyz[0][:, None]
    diff_y = all_xyz[1][None, :] - own_xyz[1][:, None]
    diff_z = all_xyz[2][None, :] - own_xyz[2][:, None]
    square = (
        diff_x * diff_x
        + diff_y * diff_y
        + diff_z * diff_z
        + 0.5 * (all_area[None, :] + own_area[:, None])
    )
    radius = jnp.sqrt(square)
    along_move = (
        diff_x * own_move[0][:, None]
        + diff_y * own_move[1][:, None]
        + diff_z * own_move[2][:, None]
    )
    phase = wave_value * radius
    cosine_part = jnp.cos(phase)
    sine_part = jnp.sin(phase)
    factor = along_move / (four_pi * radius * radius * radius)
    return ((-cosine_part - phase * sine_part) * factor, (phase * cosine_part - sine_part) * factor)


TWO_OVER_PI = 0.6366197723675814
HALF_PI_HI = 1.5703125
HALF_PI_MID = 4.837512969970703125e-4
HALF_PI_LO = 7.54978995489188216e-8


def sin_cos(angle):
    turns = jnp.floor(angle * TWO_OVER_PI + 0.5)
    rest = angle - turns * HALF_PI_HI
    rest = rest - turns * HALF_PI_MID
    rest = rest - turns * HALF_PI_LO
    rest2 = rest * rest
    sine = rest + rest * rest2 * (
        -1.6666654611e-1 + rest2 * (8.3321608736e-3 + rest2 * (-1.9515295891e-4))
    )
    cosine = 1.0 - 0.5 * rest2 + rest2 * rest2 * (
        4.166664568298827e-2 + rest2 * (-1.388731625493765e-3 + rest2 * 2.443315711809948e-5)
    )
    quarter = turns.astype(jnp.int32)
    swap = (quarter & 1) == 1
    sine_out = jnp.where(swap, cosine, sine)
    cosine_out = jnp.where(swap, sine, cosine)
    sine_out = jnp.where((quarter & 2) == 2, -sine_out, sine_out)
    cosine_out = jnp.where(((quarter + 1) & 2) == 2, -cosine_out, cosine_out)
    return sine_out, cosine_out


LANES = 256
STORE_LIMIT = 24 * 1024 * 1024


def panel_kernel(slope_mode, stored_in, store_out, wave_ref, own_ref, all_ref, vec_ref, *refs):
    if stored_in:
        real_hbm, imag_hbm, out_ref, real_buf, imag_buf, sems = refs
    elif store_out:
        out_ref, real_hbm, imag_hbm, real_buf, imag_buf, sems = refs
    else:
        (out_ref,) = refs
    block_count = own_ref.shape[0] // 8

    def copies(block, slot):
        rows = pl.ds(pl.multiple_of(block * 8, 8), 8)
        pairs = [(real_hbm, real_buf), (imag_hbm, imag_buf)]
        if stored_in:
            return [pltpu.make_async_copy(hbm.at[rows], buf.at[rows], sems.at[k, block]) for k, (hbm, buf) in enumerate(pairs)]
        return [pltpu.make_async_copy(buf.at[slot], hbm.at[rows], sems.at[k, slot]) for k, (hbm, buf) in enumerate(pairs)]
    wave_value = wave_ref[0]
    own_total = own_ref.shape[0]
    panel_total = all_ref.shape[1]
    width = LANES if panel_total % LANES == 0 else 128
    chunk_count = panel_total // width
    needs_geometry = slope_mode or not stored_in

    def row_block(block, carry):
        first = pl.multiple_of(block * 8, 8)
        rows = pl.ds(first, 8)
        slot = lax.rem(block, 2)
        if stored_in:
            for copy in copies(block, slot):
                copy.wait()

        if store_out:

            @pl.when(block >= 2)
            def _():
                for copy in copies(block - 2, slot):
                    copy.wait()

        own = own_ref[rows, :]
        own_x = jnp.broadcast_to(own[:, 0:1], (8, width))
        own_y = jnp.broadcast_to(own[:, 1:2], (8, width))
        own_z = jnp.broadcast_to(own[:, 2:3], (8, width))
        own_a = jnp.broadcast_to(own[:, 3:4], (8, width))
        if slope_mode:
            move_x = jnp.broadcast_to(own[:, 4:5], (8, width))
            move_y = jnp.broadcast_to(own[:, 5:6], (8, width))
            move_z = jnp.broadcast_to(own[:, 6:7], (8, width))

        def lane_block(chunk, sums):
            start = pl.multiple_of(chunk * width, width)
            span = pl.ds(start, width)
            if needs_geometry:
                diff_x = all_ref[0:1, span] - own_x
                diff_y = all_ref[1:2, span] - own_y
                diff_z = all_ref[2:3, span] - own_z
                square = (
                    diff_x * diff_x
                    + diff_y * diff_y
                    + diff_z * diff_z
                    + 0.5 * (all_ref[3:4, span] + own_a)
                )
                inverse = lax.rsqrt(square)
                radius = square * inverse
                phase = wave_value * radius
            if stored_in:
                real_part = real_buf[rows, span]
                imag_part = imag_buf[rows, span]
                if slope_mode:
                    along_move = diff_x * move_x + diff_y * move_y + diff_z * move_z
                    factor = along_move * (inverse * inverse)
                    first_part = (-real_part - phase * imag_part) * factor
                    second_part = (phase * real_part - imag_part) * factor
                else:
                    first_part = real_part
                    second_part = imag_part
            else:
                sine_part, cosine_part = sin_cos(phase)
                if slope_mode:
                    along_move = diff_x * move_x + diff_y * move_y + diff_z * move_z
                    factor = along_move * (inverse * inverse * inverse) * (1.0 / four_pi)
                    first_part = (-cosine_part - phase * sine_part) * factor
                    second_part = (phase * cosine_part - sine_part) * factor
                else:
                    factor = inverse * (1.0 / four_pi)
                    first_part = cosine_part * factor
                    second_part = sine_part * factor
                if store_out:
                    real_buf[slot, :, span] = first_part
                    imag_buf[slot, :, span] = second_part
            zone_count = len(sums) // 3
            both_parts = first_part + second_part
            new_sums = []
            for zone in range(zone_count):
                new_sums.append(sums[zone] + first_part * vec_ref[zone:zone + 1, span])
            for zone in range(zone_count, 2 * zone_count):
                new_sums.append(sums[zone] + second_part * vec_ref[zone:zone + 1, span])
            for zone in range(2 * zone_count, 3 * zone_count):
                new_sums.append(sums[zone] + both_parts * vec_ref[zone:zone + 1, span])
            return tuple(new_sums)

        columns = vec_ref.shape[0]
        zeros = tuple(jnp.zeros((8, width), jnp.float32) for _ in range(columns))
        sums = lax.fori_loop(0, chunk_count, lane_block, zeros, unroll=4 if stored_in and not slope_mode else 3)
        lane = lax.broadcasted_iota(jnp.int32, (8, columns), 1)
        result = jnp.zeros((8, columns), jnp.float32)
        for column in range(columns):
            total = jnp.sum(sums[column], axis=1, keepdims=True)
            result = jnp.where(lane == column, total, result)
        out_ref[rows, :] = result
        if store_out:
            for copy in copies(block, slot):
                copy.start()
        return carry

    if stored_in:
        for block in range(block_count):
            for copy in copies(block, 0):
                copy.start()
    lax.fori_loop(0, block_count, row_block, 0)
    if store_out:
        for block in range(max(0, block_count - 2), block_count):
            for copy in copies(block, block % 2):
                copy.wait()


def panel_contract(slope_mode, wavenumber, own_table, all_table, vector_full, stored=None, store_out=False):
    zone_count = vector_full.shape[1] // 2
    vector_rows = jnp.concatenate(
        [vector_full.T, (vector_full[:, :zone_count] - vector_full[:, zone_count:]).T], 0
    )
    outs = panel_call(slope_mode, wavenumber, own_table, all_table, vector_rows, stored, store_out)
    sums = outs[0] if store_out else outs
    first_sum = sums[:, :zone_count]
    second_sum = sums[:, zone_count:2 * zone_count]
    both_sum = sums[:, 2 * zone_count:]
    if slope_mode:
        imag_sum = both_sum - first_sum + second_sum
    else:
        imag_sum = first_sum - second_sum - both_sum
    combined = jnp.concatenate([first_sum + second_sum, imag_sum], 1)
    if store_out:
        return (combined,) + tuple(outs[1:])
    return combined


def panel_call(slope_mode, wavenumber, own_table, all_table, vector_rows, stored, store_out):
    own_total = own_table.shape[0]
    columns = vector_rows.shape[0]
    panel_total = all_table.shape[1]
    elements = own_total * panel_total
    stored_in = stored is not None
    operands = [wavenumber, own_table, all_table, vector_rows]
    out_shape = [jax.ShapeDtypeStruct((own_total, columns), jnp.float32)]
    matrix_bytes = 0
    if stored_in:
        operands += list(stored)
        matrix_bytes = 8 * elements
    if store_out:
        out_shape += [jax.ShapeDtypeStruct((own_total, panel_total), jnp.float32)] * 2
        matrix_bytes = 8 * elements
    vmem = pl.BlockSpec(memory_space=pltpu.VMEM)
    hbm = pl.BlockSpec(memory_space=pl.ANY)
    params = {}
    if stored_in:
        params["scratch_shapes"] = [
            pltpu.VMEM((own_total, panel_total), jnp.float32),
            pltpu.VMEM((own_total, panel_total), jnp.float32),
            pltpu.SemaphoreType.DMA((2, own_total // 8)),
        ]
        params["compiler_params"] = pltpu.CompilerParams(vmem_limit_bytes=matrix_bytes + 16 * 1024 * 1024)
    elif store_out:
        params["scratch_shapes"] = [
            pltpu.VMEM((2, 8, panel_total), jnp.float32),
            pltpu.VMEM((2, 8, panel_total), jnp.float32),
            pltpu.SemaphoreType.DMA((2, 2)),
        ]
    if stored_in and not slope_mode:
        flops, transcendentals = 32 * elements, 0
    elif stored_in:
        flops, transcendentals = 60 * elements, 2 * elements
    else:
        flops, transcendentals = 150 * elements, 4 * elements
    return pl.pallas_call(
        functools.partial(panel_kernel, slope_mode, stored_in, store_out),
        out_shape=tuple(out_shape) if store_out else out_shape[0],
        in_specs=[pl.BlockSpec(memory_space=pltpu.SMEM)] + [vmem] * 3 + [hbm] * (len(operands) - 4),
        out_specs=tuple([vmem] + [hbm] * (len(out_shape) - 1)) if store_out else vmem,
        cost_estimate=pl.CostEstimate(
            flops=flops,
            transcendentals=transcendentals,
            bytes_accessed=4 * (own_table.size + all_table.size + vector_rows.size + own_total * columns) + matrix_bytes,
        ),
        **params,
    )(*operands)


def gather_axis(vector, name):
    count = lax.axis_size(name)
    if count > 8:
        return lax.all_gather(vector, name, axis=0, tiled=True)
    index = lax.axis_index(name)
    parts = [vector]
    for shift in range(1, count):
        parts.append(lax.ppermute(vector, name, [(i, (i + shift) % count) for i in range(count)]))
    stacked = jnp.stack([parts[(-offset) % count] for offset in range(count)])
    ordered = jnp.roll(stacked, index, axis=0)
    return ordered.reshape((count * vector.shape[0],) + vector.shape[1:])


def gather_panels(vector):
    return gather_axis(gather_axis(vector, "col"), "row")


def chunk_size_of(count, limit):
    return math.gcd(count, limit)


def rows_sum(block_fn, count, limit):
    size = chunk_size_of(count, limit)
    starts = jnp.arange(count // size, dtype=jnp.int32) * size
    return jnp.sum(lax.map(lambda start: block_fn(start, size), starts), 0)


def local(
    centers,
    panel_areas,
    jump_term,
    displacement,
    design_ids,
    primal_field,
    adjoint_start,
    mic_panels,
    wavenumber,
):
    zone_count = adjoint_start.shape[1] // 2
    owned_count = centers.shape[1]
    axes = ("row", "col")
    wave_value = wavenumber[0]
    packed = jnp.concatenate([centers.T, panel_areas[:, None], adjoint_start], 1)
    gathered = gather_panels(packed)
    panel_total = gathered.shape[0]
    all_xyz = gathered[:, :3].T
    all_area = gathered[:, 3]
    start_full = gathered[:, 4:]
    all_table = gathered[:, :4].T
    own_table = jnp.concatenate(
        [centers.T, panel_areas[:, None], displacement.T, jnp.zeros((owned_count, 1), jnp.float32)], 1
    )

    store = 8 * owned_count * panel_total <= STORE_LIMIT
    saved = []

    def apply_adjoint(vector_full, vector_own):
        if store and saved:
            summed = panel_contract(False, wavenumber, own_table, all_table, vector_full, stored=saved)
        elif store:
            summed, real_part, imag_part = panel_contract(
                False, wavenumber, own_table, all_table, vector_full, store_out=True
            )
            saved.extend([real_part, imag_part])
        else:
            summed = panel_contract(False, wavenumber, own_table, all_table, vector_full)
        return panel_areas[:, None] * summed + jump_term[:, None] * vector_own

    first_panel = (
        lax.axis_index("row") * lax.axis_size("col") + lax.axis_index("col")
    ) * owned_count
    panel_ids = first_panel + jnp.arange(owned_count, dtype=jnp.int32)
    mic_hits = jnp.sum(
        (panel_ids[:, None, None] == mic_panels[None, :, :]).astype(jnp.float32), axis=2
    )
    right_side = jnp.concatenate(
        [mic_hits * primal_field[0][:, None], mic_hits * primal_field[1][:, None]], 1
    )
    residual = right_side - apply_adjoint(start_full, adjoint_start)
    residual_full = gather_panels(residual)
    start_norm = jnp.sqrt(square_sum(residual_full))
    start_scale = jnp.concatenate([start_norm, start_norm])[None, :]
    basis_one = residual / start_scale
    basis_one_full = residual_full / start_scale
    image_one = apply_adjoint(basis_one_full, basis_one)
    image_one_full = gather_panels(image_one)
    first_re, first_im = inner_parts(basis_one_full, image_one_full, zone_count)
    lean_one_full = image_one_full - complex_scale(first_re, first_im, basis_one_full, zone_count)
    lean_one = image_one - complex_scale(first_re, first_im, basis_one, zone_count)
    first_norm = jnp.sqrt(square_sum(lean_one_full))
    first_scale = jnp.concatenate([first_norm, first_norm])[None, :]
    basis_two = lean_one / first_scale
    basis_two_full = lean_one_full / first_scale
    image_two = apply_adjoint(basis_two_full, basis_two)
    image_two_full = gather_panels(image_two)
    cross_re, cross_im = inner_parts(basis_one_full, image_two_full, zone_count)
    second_re, second_im = inner_parts(basis_two_full, image_two_full, zone_count)
    lean_two_full = (
        image_two_full
        - complex_scale(cross_re, cross_im, basis_one_full, zone_count)
        - complex_scale(second_re, second_im, basis_two_full, zone_count)
    )
    second_norm = jnp.sqrt(square_sum(lean_two_full))
    coef_one_re, coef_one_im, coef_two_re, coef_two_im = least_squares(
        start_norm,
        first_re,
        first_im,
        first_norm,
        cross_re,
        cross_im,
        second_re,
        second_im,
        second_norm,
    )
    adjoint_field = (
        adjoint_start
        + complex_scale(coef_one_re, coef_one_im, basis_one, zone_count)
        + complex_scale(coef_two_re, coef_two_im, basis_two, zone_count)
    )
    field_full = (
        start_full
        + complex_scale(coef_one_re, coef_one_im, basis_one_full, zone_count)
        + complex_scale(coef_two_re, coef_two_im, basis_two_full, zone_count)
    )

    contracted = panel_contract(True, wavenumber, own_table, all_table, field_full, stored=saved or None)
    contrib = panel_areas[:, None] * (
        primal_field[0][:, None] * contracted[:, :zone_count]
        - primal_field[1][:, None] * contracted[:, zone_count:]
    )
    onehot = (design_ids[:, None] == jnp.arange(DESIGN, dtype=jnp.int32)[None, :]).astype(
        jnp.float32
    )
    local_sums = contract_first(contrib, onehot)
    sensitivity = lax.psum(lax.psum(local_sums, "col"), "row")
    return (adjoint_field, sensitivity)


def solution(mesh):
    return jax.shard_map(
        local,
        mesh=mesh,
        in_specs=(
            P(None, ("row", "col")),
            P(("row", "col")),
            P(("row", "col")),
            P(None, ("row", "col")),
            P(("row", "col")),
            P(None, ("row", "col")),
            P(("row", "col"), None),
            P(),
            P(),
        ),
        out_specs=(P(("row", "col"), None), P()),
        check_vma=False,
    )
```

```python
import functools
import math

import jax
import jax.numpy as jnp
from jax import lax
from jax.experimental import pallas as pl
from jax.experimental.pallas import tpu as pltpu
from jax.sharding import PartitionSpec as P

DESIGN = 128


highest = lax.Precision.HIGHEST
four_pi = 4.0 * math.pi


def distances(rows_xyz, rows_area, cols_xyz, cols_area):
    diff_x = rows_xyz[0][:, None] - cols_xyz[0][None, :]
    diff_y = rows_xyz[1][:, None] - cols_xyz[1][None, :]
    diff_z = rows_xyz[2][:, None] - cols_xyz[2][None, :]
    square = (
        diff_x * diff_x
        + diff_y * diff_y
        + diff_z * diff_z
        + 0.5 * (rows_area[:, None] + cols_area[None, :])
    )
    return (diff_x, diff_y, diff_z, jnp.sqrt(square))


def kernel_parts(rows_xyz, rows_area, cols_xyz, cols_area, wave_value):
    radius = distances(rows_xyz, rows_area, cols_xyz, cols_area)[3]
    phase = wave_value * radius
    factor = 1.0 / (four_pi * radius)
    return (jnp.cos(phase) * factor, jnp.sin(phase) * factor)


def slope_parts(rows_xyz, rows_area, cols_xyz, cols_area, cols_move, wave_value):
    diff_x, diff_y, diff_z, radius = distances(rows_xyz, rows_area, cols_xyz, cols_area)
    along_move = (
        diff_x * cols_move[0][None, :]
        + diff_y * cols_move[1][None, :]
        + diff_z * cols_move[2][None, :]
    )
    phase = wave_value * radius
    cosine_part = jnp.cos(phase)
    sine_part = jnp.sin(phase)
    factor = along_move / (four_pi * radius * radius * radius)
    return ((-cosine_part - phase * sine_part) * factor, (phase * cosine_part - sine_part) * factor)


def contract_first(matrix, vector):
    return lax.dot_general(matrix, vector, (((0,), (0,)), ((), ())), precision=highest)


def conj_columns(real_part, imag_part, vector, zone_count):
    left_part = contract_first(real_part, vector)
    right_part = contract_first(imag_part, vector)
    return jnp.concatenate(
        [
            left_part[:, :zone_count] + right_part[:, zone_count:],
            left_part[:, zone_count:] - right_part[:, :zone_count],
        ],
        1,
    )


def inner_parts(left_part, right_part, zone_count):
    left_re, left_im = (left_part[:, :zone_count], left_part[:, zone_count:])
    right_re, right_im = (right_part[:, :zone_count], right_part[:, zone_count:])
    return (
        jnp.sum(left_re * right_re + left_im * right_im, 0),
        jnp.sum(left_re * right_im - left_im * right_re, 0),
    )


def square_sum(vector):
    return jnp.sum(vector * vector, 0).reshape(2, -1).sum(0)


def complex_scale(scale_re, scale_im, vector, zone_count):
    vec_re, vec_im = (vector[:, :zone_count], vector[:, zone_count:])
    return jnp.concatenate(
        [scale_re * vec_re - scale_im * vec_im, scale_re * vec_im + scale_im * vec_re], 1
    )


def least_squares(
    start_norm,
    first_re,
    first_im,
    first_norm,
    cross_re,
    cross_im,
    second_re,
    second_im,
    second_norm,
):
    gram_one = first_re * first_re + first_im * first_im + first_norm * first_norm
    gram_off_re = first_re * cross_re + first_im * cross_im + first_norm * second_re
    gram_off_im = first_re * cross_im - first_im * cross_re + first_norm * second_im
    gram_two = (
        cross_re * cross_re
        + cross_im * cross_im
        + second_re * second_re
        + second_im * second_im
        + second_norm * second_norm
    )
    rhs_one_re = start_norm * first_re
    rhs_one_im = -start_norm * first_im
    rhs_two_re = start_norm * cross_re
    rhs_two_im = -start_norm * cross_im
    determinant = gram_one * gram_two - gram_off_re * gram_off_re - gram_off_im * gram_off_im
    coef_one_re = (
        gram_two * rhs_one_re - (gram_off_re * rhs_two_re - gram_off_im * rhs_two_im)
    ) / determinant
    coef_one_im = (
        gram_two * rhs_one_im - (gram_off_re * rhs_two_im + gram_off_im * rhs_two_re)
    ) / determinant
    coef_two_re = (
        gram_one * rhs_two_re - (gram_off_re * rhs_one_re + gram_off_im * rhs_one_im)
    ) / determinant
    coef_two_im = (
        gram_one * rhs_two_im - (gram_off_re * rhs_one_im - gram_off_im * rhs_one_re)
    ) / determinant
    return (coef_one_re, coef_one_im, coef_two_re, coef_two_im)


def slope_parts_t(own_xyz, own_area, own_move, all_xyz, all_area, wave_value):
    diff_x = all_xyz[0][None, :] - own_xyz[0][:, None]
    diff_y = all_xyz[1][None, :] - own_xyz[1][:, None]
    diff_z = all_xyz[2][None, :] - own_xyz[2][:, None]
    square = (
        diff_x * diff_x
        + diff_y * diff_y
        + diff_z * diff_z
        + 0.5 * (all_area[None, :] + own_area[:, None])
    )
    radius = jnp.sqrt(square)
    along_move = (
        diff_x * own_move[0][:, None]
        + diff_y * own_move[1][:, None]
        + diff_z * own_move[2][:, None]
    )
    phase = wave_value * radius
    cosine_part = jnp.cos(phase)
    sine_part = jnp.sin(phase)
    factor = along_move / (four_pi * radius * radius * radius)
    return ((-cosine_part - phase * sine_part) * factor, (phase * cosine_part - sine_part) * factor)


TWO_OVER_PI = 0.6366197723675814
HALF_PI_HI = 1.5703125
HALF_PI_MID = 4.837512969970703125e-4
HALF_PI_LO = 7.54978995489188216e-8


def sin_cos(angle):
    turns = jnp.floor(angle * TWO_OVER_PI + 0.5)
    rest = angle - turns * HALF_PI_HI
    rest = rest - turns * HALF_PI_MID
    rest = rest - turns * HALF_PI_LO
    rest2 = rest * rest
    sine = rest + rest * rest2 * (
        -1.6666654611e-1 + rest2 * (8.3321608736e-3 + rest2 * (-1.9515295891e-4))
    )
    cosine = 1.0 - 0.5 * rest2 + rest2 * rest2 * (
        4.166664568298827e-2 + rest2 * (-1.388731625493765e-3 + rest2 * 2.443315711809948e-5)
    )
    quarter = turns.astype(jnp.int32)
    swap = (quarter & 1) == 1
    sine_out = jnp.where(swap, cosine, sine)
    cosine_out = jnp.where(swap, sine, cosine)
    sine_out = jnp.where((quarter & 2) == 2, -sine_out, sine_out)
    cosine_out = jnp.where(((quarter + 1) & 2) == 2, -cosine_out, cosine_out)
    return sine_out, cosine_out


LANES = 256
STORE_LIMIT = 24 * 1024 * 1024


def panel_kernel(slope_mode, stored_in, store_out, wave_ref, own_ref, all_ref, vec_ref, *refs):
    if stored_in:
        real_hbm, imag_hbm, out_ref, real_buf, imag_buf, sems = refs
    elif store_out:
        out_ref, real_hbm, imag_hbm, real_buf, imag_buf, sems = refs
    else:
        (out_ref,) = refs
    block_count = own_ref.shape[0] // 8

    def copies(block, slot):
        rows = pl.ds(pl.multiple_of(block * 8, 8), 8)
        pairs = [(real_hbm, real_buf), (imag_hbm, imag_buf)]
        if stored_in:
            return [pltpu.make_async_copy(hbm.at[rows], buf.at[rows], sems.at[k, block]) for k, (hbm, buf) in enumerate(pairs)]
        return [pltpu.make_async_copy(buf.at[slot], hbm.at[rows], sems.at[k, slot]) for k, (hbm, buf) in enumerate(pairs)]
    wave_value = wave_ref[0]
    own_total = own_ref.shape[0]
    panel_total = all_ref.shape[1]
    width = LANES if panel_total % LANES == 0 else 128
    chunk_count = panel_total // width
    needs_geometry = slope_mode or not stored_in

    def row_block(block, carry):
        first = pl.multiple_of(block * 8, 8)
        rows = pl.ds(first, 8)
        slot = lax.rem(block, 2)
        if stored_in:
            for copy in copies(block, slot):
                copy.wait()

        if store_out:

            @pl.when(block >= 2)
            def _():
                for copy in copies(block - 2, slot):
                    copy.wait()

        own = own_ref[rows, :]
        own_x = jnp.broadcast_to(own[:, 0:1], (8, width))
        own_y = jnp.broadcast_to(own[:, 1:2], (8, width))
        own_z = jnp.broadcast_to(own[:, 2:3], (8, width))
        own_a = jnp.broadcast_to(own[:, 3:4], (8, width))
        if slope_mode:
            move_x = jnp.broadcast_to(own[:, 4:5], (8, width))
            move_y = jnp.broadcast_to(own[:, 5:6], (8, width))
            move_z = jnp.broadcast_to(own[:, 6:7], (8, width))

        def lane_block(chunk, sums):
            start = pl.multiple_of(chunk * width, width)
            span = pl.ds(start, width)
            if needs_geometry:
                diff_x = all_ref[0:1, span] - own_x
                diff_y = all_ref[1:2, span] - own_y
                diff_z = all_ref[2:3, span] - own_z
                square = (
                    diff_x * diff_x
                    + diff_y * diff_y
                    + diff_z * diff_z
                    + 0.5 * (all_ref[3:4, span] + own_a)
                )
                inverse = lax.rsqrt(square)
                radius = square * inverse
                phase = wave_value * radius
            if stored_in:
                real_part = real_buf[rows, span]
                imag_part = imag_buf[rows, span]
                if slope_mode:
                    along_move = diff_x * move_x + diff_y * move_y + diff_z * move_z
                    factor = along_move * (inverse * inverse)
                    first_part = (-real_part - phase * imag_part) * factor
                    second_part = (phase * real_part - imag_part) * factor
                else:
                    first_part = real_part
                    second_part = imag_part
            else:
                sine_part, cosine_part = sin_cos(phase)
                if slope_mode:
                    along_move = diff_x * move_x + diff_y * move_y + diff_z * move_z
                    factor = along_move * (inverse * inverse * inverse) * (1.0 / four_pi)
                    first_part = (-cosine_part - phase * sine_part) * factor
                    second_part = (phase * cosine_part - sine_part) * factor
                else:
                    factor = inverse * (1.0 / four_pi)
                    first_part = cosine_part * factor
                    second_part = sine_part * factor
                if store_out:
                    real_buf[slot, :, span] = first_part
                    imag_buf[slot, :, span] = second_part
            zone_count = len(sums) // 3
            both_parts = first_part + second_part
            new_sums = []
            for zone in range(zone_count):
                new_sums.append(sums[zone] + first_part * vec_ref[zone:zone + 1, span])
            for zone in range(zone_count, 2 * zone_count):
                new_sums.append(sums[zone] + second_part * vec_ref[zone:zone + 1, span])
            for zone in range(2 * zone_count, 3 * zone_count):
                new_sums.append(sums[zone] + both_parts * vec_ref[zone:zone + 1, span])
            return tuple(new_sums)

        columns = vec_ref.shape[0]
        zeros = tuple(jnp.zeros((8, width), jnp.float32) for _ in range(columns))
        sums = lax.fori_loop(0, chunk_count, lane_block, zeros, unroll=4 if stored_in and not slope_mode else 3)
        lane = lax.broadcasted_iota(jnp.int32, (8, columns), 1)
        result = jnp.zeros((8, columns), jnp.float32)
        for column in range(columns):
            total = jnp.sum(sums[column], axis=1, keepdims=True)
            result = jnp.where(lane == column, total, result)
        out_ref[rows, :] = result
        if store_out:
            for copy in copies(block, slot):
                copy.start()
        return carry

    if stored_in:
        for block in range(block_count):
            for copy in copies(block, 0):
                copy.start()
    lax.fori_loop(0, block_count, row_block, 0)
    if store_out:
        for block in range(max(0, block_count - 2), block_count):
            for copy in copies(block, block % 2):
                copy.wait()


def panel_contract(slope_mode, wavenumber, own_table, all_table, vector_full, stored=None, store_out=False):
    zone_count = vector_full.shape[1] // 2
    vector_rows = jnp.concatenate(
        [vector_full.T, (vector_full[:, :zone_count] - vector_full[:, zone_count:]).T], 0
    )
    outs = panel_call(slope_mode, wavenumber, own_table, all_table, vector_rows, stored, store_out)
    sums = outs[0] if store_out else outs
    first_sum = sums[:, :zone_count]
    second_sum = sums[:, zone_count:2 * zone_count]
    both_sum = sums[:, 2 * zone_count:]
    if slope_mode:
        imag_sum = both_sum - first_sum + second_sum
    else:
        imag_sum = first_sum - second_sum - both_sum
    combined = jnp.concatenate([first_sum + second_sum, imag_sum], 1)
    if store_out:
        return (combined,) + tuple(outs[1:])
    return combined


def panel_call(slope_mode, wavenumber, own_table, all_table, vector_rows, stored, store_out):
    own_total = own_table.shape[0]
    columns = vector_rows.shape[0]
    panel_total = all_table.shape[1]
    elements = own_total * panel_total
    stored_in = stored is not None
    operands = [wavenumber, own_table, all_table, vector_rows]
    out_shape = [jax.ShapeDtypeStruct((own_total, columns), jnp.float32)]
    matrix_bytes = 0
    if stored_in:
        operands += list(stored)
        matrix_bytes = 8 * elements
    if store_out:
        out_shape += [jax.ShapeDtypeStruct((own_total, panel_total), jnp.float32)] * 2
        matrix_bytes = 8 * elements
    vmem = pl.BlockSpec(memory_space=pltpu.VMEM)
    hbm = pl.BlockSpec(memory_space=pltpu.HBM)
    params = {}
    if stored_in:
        params["scratch_shapes"] = [
            pltpu.VMEM((own_total, panel_total), jnp.float32),
            pltpu.VMEM((own_total, panel_total), jnp.float32),
            pltpu.SemaphoreType.DMA((2, own_total // 8)),
        ]
        params["compiler_params"] = pltpu.CompilerParams(vmem_limit_bytes=60 * 1024 * 1024)
    elif store_out:
        params["scratch_shapes"] = [
            pltpu.VMEM((2, 8, panel_total), jnp.float32),
            pltpu.VMEM((2, 8, panel_total), jnp.float32),
            pltpu.SemaphoreType.DMA((2, 2)),
        ]
    if stored_in and not slope_mode:
        flops, transcendentals = 32 * elements, 0
    elif stored_in:
        flops, transcendentals = 60 * elements, 2 * elements
    else:
        flops, transcendentals = 150 * elements, 4 * elements
    return pl.pallas_call(
        functools.partial(panel_kernel, slope_mode, stored_in, store_out),
        out_shape=tuple(out_shape) if store_out else out_shape[0],
        in_specs=[pl.BlockSpec(memory_space=pltpu.SMEM)] + [vmem] * 3 + [hbm] * (len(operands) - 4),
        out_specs=tuple([vmem] + [hbm] * (len(out_shape) - 1)) if store_out else vmem,
        cost_estimate=pl.CostEstimate(
            flops=flops,
            transcendentals=transcendentals,
            bytes_accessed=4 * (own_table.size + all_table.size + vector_rows.size + own_total * columns) + matrix_bytes,
        ),
        **params,
    )(*operands)


def gather_axis(vector, name):
    count = lax.axis_size(name)
    if count > 8:
        return lax.all_gather(vector, name, axis=0, tiled=True)
    index = lax.axis_index(name)
    parts = [vector]
    for shift in range(1, count):
        parts.append(lax.ppermute(vector, name, [(i, (i + shift) % count) for i in range(count)]))
    stacked = jnp.stack([parts[(-offset) % count] for offset in range(count)])
    ordered = jnp.roll(stacked, index, axis=0)
    return ordered.reshape((count * vector.shape[0],) + vector.shape[1:])


def gather_panels(vector):
    return gather_axis(gather_axis(vector, "col"), "row")


def chunk_size_of(count, limit):
    return math.gcd(count, limit)


def rows_sum(block_fn, count, limit):
    size = chunk_size_of(count, limit)
    starts = jnp.arange(count // size, dtype=jnp.int32) * size
    return jnp.sum(lax.map(lambda start: block_fn(start, size), starts), 0)


def local(
    centers,
    panel_areas,
    jump_term,
    displacement,
    design_ids,
    primal_field,
    adjoint_start,
    mic_panels,
    wavenumber,
):
    zone_count = adjoint_start.shape[1] // 2
    owned_count = centers.shape[1]
    axes = ("row", "col")
    wave_value = wavenumber[0]
    packed = jnp.concatenate([centers.T, panel_areas[:, None], adjoint_start], 1)
    gathered = gather_panels(packed)
    panel_total = gathered.shape[0]
    all_xyz = gathered[:, :3].T
    all_area = gathered[:, 3]
    start_full = gathered[:, 4:]
    all_table = gathered[:, :4].T
    own_table = jnp.concatenate(
        [centers.T, panel_areas[:, None], displacement.T, jnp.zeros((owned_count, 1), jnp.float32)], 1
    )

    store = 8 * owned_count * panel_total <= STORE_LIMIT
    saved = []

    def apply_adjoint(vector_full, vector_own):
        if store and saved:
            summed = panel_contract(False, wavenumber, own_table, all_table, vector_full, stored=saved)
        elif store:
            summed, real_part, imag_part = panel_contract(
                False, wavenumber, own_table, all_table, vector_full, store_out=True
            )
            saved.extend([real_part, imag_part])
        else:
            summed = panel_contract(False, wavenumber, own_table, all_table, vector_full)
        return panel_areas[:, None] * summed + jump_term[:, None] * vector_own

    first_panel = (
        lax.axis_index("row") * lax.axis_size("col") + lax.axis_index("col")
    ) * owned_count
    panel_ids = first_panel + jnp.arange(owned_count, dtype=jnp.int32)
    mic_hits = jnp.sum(
        (panel_ids[:, None, None] == mic_panels[None, :, :]).astype(jnp.float32), axis=2
    )
    right_side = jnp.concatenate(
        [mic_hits * primal_field[0][:, None], mic_hits * primal_field[1][:, None]], 1
    )
    residual = right_side - apply_adjoint(start_full, adjoint_start)
    residual_full = gather_panels(residual)
    start_norm = jnp.sqrt(square_sum(residual_full))
    start_scale = jnp.concatenate([start_norm, start_norm])[None, :]
    basis_one = residual / start_scale
    basis_one_full = residual_full / start_scale
    image_one = apply_adjoint(basis_one_full, basis_one)
    image_one_full = gather_panels(image_one)
    first_re, first_im = inner_parts(basis_one_full, image_one_full, zone_count)
    lean_one_full = image_one_full - complex_scale(first_re, first_im, basis_one_full, zone_count)
    lean_one = image_one - complex_scale(first_re, first_im, basis_one, zone_count)
    first_norm = jnp.sqrt(square_sum(lean_one_full))
    first_scale = jnp.concatenate([first_norm, first_norm])[None, :]
    basis_two = lean_one / first_scale
    basis_two_full = lean_one_full / first_scale
    image_two = apply_adjoint(basis_two_full, basis_two)
    image_two_full = gather_panels(image_two)
    cross_re, cross_im = inner_parts(basis_one_full, image_two_full, zone_count)
    second_re, second_im = inner_parts(basis_two_full, image_two_full, zone_count)
    lean_two_full = (
        image_two_full
        - complex_scale(cross_re, cross_im, basis_one_full, zone_count)
        - complex_scale(second_re, second_im, basis_two_full, zone_count)
    )
    second_norm = jnp.sqrt(square_sum(lean_two_full))
    coef_one_re, coef_one_im, coef_two_re, coef_two_im = least_squares(
        start_norm,
        first_re,
        first_im,
        first_norm,
        cross_re,
        cross_im,
        second_re,
        second_im,
        second_norm,
    )
    adjoint_field = (
        adjoint_start
        + complex_scale(coef_one_re, coef_one_im, basis_one, zone_count)
        + complex_scale(coef_two_re, coef_two_im, basis_two, zone_count)
    )
    field_full = (
        start_full
        + complex_scale(coef_one_re, coef_one_im, basis_one_full, zone_count)
        + complex_scale(coef_two_re, coef_two_im, basis_two_full, zone_count)
    )

    contracted = panel_contract(True, wavenumber, own_table, all_table, field_full, stored=saved or None)
    contrib = panel_areas[:, None] * (
        primal_field[0][:, None] * contracted[:, :zone_count]
        - primal_field[1][:, None] * contracted[:, zone_count:]
    )
    onehot = (design_ids[:, None] == jnp.arange(DESIGN, dtype=jnp.int32)[None, :]).astype(
        jnp.float32
    )
    local_sums = contract_first(contrib, onehot)
    sensitivity = lax.psum(lax.psum(local_sums, "col"), "row")
    return (adjoint_field, sensitivity)


def solution(mesh):
    return jax.shard_map(
        local,
        mesh=mesh,
        in_specs=(
            P(None, ("row", "col")),
            P(("row", "col")),
            P(("row", "col")),
            P(None, ("row", "col")),
            P(("row", "col")),
            P(None, ("row", "col")),
            P(("row", "col"), None),
            P(),
            P(),
        ),
        out_specs=(P(("row", "col"), None), P()),
        check_vma=False,
    )
```

```python
import functools
import math

import jax
import jax.numpy as jnp
from jax import lax
from jax.experimental import pallas as pl
from jax.experimental.pallas import tpu as pltpu
from jax.sharding import PartitionSpec as P

DESIGN = 128


highest = lax.Precision.HIGHEST
four_pi = 4.0 * math.pi


def distances(rows_xyz, rows_area, cols_xyz, cols_area):
    diff_x = rows_xyz[0][:, None] - cols_xyz[0][None, :]
    diff_y = rows_xyz[1][:, None] - cols_xyz[1][None, :]
    diff_z = rows_xyz[2][:, None] - cols_xyz[2][None, :]
    square = (
        diff_x * diff_x
        + diff_y * diff_y
        + diff_z * diff_z
        + 0.5 * (rows_area[:, None] + cols_area[None, :])
    )
    return (diff_x, diff_y, diff_z, jnp.sqrt(square))


def kernel_parts(rows_xyz, rows_area, cols_xyz, cols_area, wave_value):
    radius = distances(rows_xyz, rows_area, cols_xyz, cols_area)[3]
    phase = wave_value * radius
    factor = 1.0 / (four_pi * radius)
    return (jnp.cos(phase) * factor, jnp.sin(phase) * factor)


def slope_parts(rows_xyz, rows_area, cols_xyz, cols_area, cols_move, wave_value):
    diff_x, diff_y, diff_z, radius = distances(rows_xyz, rows_area, cols_xyz, cols_area)
    along_move = (
        diff_x * cols_move[0][None, :]
        + diff_y * cols_move[1][None, :]
        + diff_z * cols_move[2][None, :]
    )
    phase = wave_value * radius
    cosine_part = jnp.cos(phase)
    sine_part = jnp.sin(phase)
    factor = along_move / (four_pi * radius * radius * radius)
    return ((-cosine_part - phase * sine_part) * factor, (phase * cosine_part - sine_part) * factor)


def contract_first(matrix, vector):
    return lax.dot_general(matrix, vector, (((0,), (0,)), ((), ())), precision=highest)


def conj_columns(real_part, imag_part, vector, zone_count):
    left_part = contract_first(real_part, vector)
    right_part = contract_first(imag_part, vector)
    return jnp.concatenate(
        [
            left_part[:, :zone_count] + right_part[:, zone_count:],
            left_part[:, zone_count:] - right_part[:, :zone_count],
        ],
        1,
    )


def inner_parts(left_part, right_part, zone_count):
    left_re, left_im = (left_part[:, :zone_count], left_part[:, zone_count:])
    right_re, right_im = (right_part[:, :zone_count], right_part[:, zone_count:])
    return (
        jnp.sum(left_re * right_re + left_im * right_im, 0),
        jnp.sum(left_re * right_im - left_im * right_re, 0),
    )


def square_sum(vector):
    return jnp.sum(vector * vector, 0).reshape(2, -1).sum(0)


def complex_scale(scale_re, scale_im, vector, zone_count):
    vec_re, vec_im = (vector[:, :zone_count], vector[:, zone_count:])
    return jnp.concatenate(
        [scale_re * vec_re - scale_im * vec_im, scale_re * vec_im + scale_im * vec_re], 1
    )


def least_squares(
    start_norm,
    first_re,
    first_im,
    first_norm,
    cross_re,
    cross_im,
    second_re,
    second_im,
    second_norm,
):
    gram_one = first_re * first_re + first_im * first_im + first_norm * first_norm
    gram_off_re = first_re * cross_re + first_im * cross_im + first_norm * second_re
    gram_off_im = first_re * cross_im - first_im * cross_re + first_norm * second_im
    gram_two = (
        cross_re * cross_re
        + cross_im * cross_im
        + second_re * second_re
        + second_im * second_im
        + second_norm * second_norm
    )
    rhs_one_re = start_norm * first_re
    rhs_one_im = -start_norm * first_im
    rhs_two_re = start_norm * cross_re
    rhs_two_im = -start_norm * cross_im
    determinant = gram_one * gram_two - gram_off_re * gram_off_re - gram_off_im * gram_off_im
    coef_one_re = (
        gram_two * rhs_one_re - (gram_off_re * rhs_two_re - gram_off_im * rhs_two_im)
    ) / determinant
    coef_one_im = (
        gram_two * rhs_one_im - (gram_off_re * rhs_two_im + gram_off_im * rhs_two_re)
    ) / determinant
    coef_two_re = (
        gram_one * rhs_two_re - (gram_off_re * rhs_one_re + gram_off_im * rhs_one_im)
    ) / determinant
    coef_two_im = (
        gram_one * rhs_two_im - (gram_off_re * rhs_one_im - gram_off_im * rhs_one_re)
    ) / determinant
    return (coef_one_re, coef_one_im, coef_two_re, coef_two_im)


def slope_parts_t(own_xyz, own_area, own_move, all_xyz, all_area, wave_value):
    diff_x = all_xyz[0][None, :] - own_xyz[0][:, None]
    diff_y = all_xyz[1][None, :] - own_xyz[1][:, None]
    diff_z = all_xyz[2][None, :] - own_xyz[2][:, None]
    square = (
        diff_x * diff_x
        + diff_y * diff_y
        + diff_z * diff_z
        + 0.5 * (all_area[None, :] + own_area[:, None])
    )
    radius = jnp.sqrt(square)
    along_move = (
        diff_x * own_move[0][:, None]
        + diff_y * own_move[1][:, None]
        + diff_z * own_move[2][:, None]
    )
    phase = wave_value * radius
    cosine_part = jnp.cos(phase)
    sine_part = jnp.sin(phase)
    factor = along_move / (four_pi * radius * radius * radius)
    return ((-cosine_part - phase * sine_part) * factor, (phase * cosine_part - sine_part) * factor)


TWO_OVER_PI = 0.6366197723675814
HALF_PI_HI = 1.5703125
HALF_PI_MID = 4.837512969970703125e-4
HALF_PI_LO = 7.54978995489188216e-8


def sin_cos(angle):
    turns = jnp.floor(angle * TWO_OVER_PI + 0.5)
    rest = angle - turns * HALF_PI_HI
    rest = rest - turns * HALF_PI_MID
    rest = rest - turns * HALF_PI_LO
    rest2 = rest * rest
    sine = rest + rest * rest2 * (
        -1.6666654611e-1 + rest2 * (8.3321608736e-3 + rest2 * (-1.9515295891e-4))
    )
    cosine = 1.0 - 0.5 * rest2 + rest2 * rest2 * (
        4.166664568298827e-2 + rest2 * (-1.388731625493765e-3 + rest2 * 2.443315711809948e-5)
    )
    quarter = turns.astype(jnp.int32)
    swap = (quarter & 1) == 1
    sine_out = jnp.where(swap, cosine, sine)
    cosine_out = jnp.where(swap, sine, cosine)
    sine_out = jnp.where((quarter & 2) == 2, -sine_out, sine_out)
    cosine_out = jnp.where(((quarter + 1) & 2) == 2, -cosine_out, cosine_out)
    return sine_out, cosine_out


LANES = 256
STORE_LIMIT = 24 * 1024 * 1024


def panel_kernel(slope_mode, stored_in, store_out, wave_ref, own_ref, all_ref, vec_ref, *refs):
    if stored_in:
        real_hbm, imag_hbm, out_ref, real_buf, imag_buf, sems = refs
    elif store_out:
        out_ref, real_hbm, imag_hbm, real_buf, imag_buf, sems = refs
    else:
        (out_ref,) = refs
    block_count = own_ref.shape[0] // 8

    def copies(block, slot):
        rows = pl.ds(pl.multiple_of(block * 8, 8), 8)
        pairs = [(real_hbm, real_buf), (imag_hbm, imag_buf)]
        if stored_in:
            return [pltpu.make_async_copy(hbm.at[rows], buf.at[rows], sems.at[k, block]) for k, (hbm, buf) in enumerate(pairs)]
        return [pltpu.make_async_copy(buf.at[slot], hbm.at[rows], sems.at[k, slot]) for k, (hbm, buf) in enumerate(pairs)]
    wave_value = wave_ref[0]
    own_total = own_ref.shape[0]
    panel_total = all_ref.shape[1]
    width = LANES if panel_total % LANES == 0 else 128
    chunk_count = panel_total // width
    needs_geometry = slope_mode or not stored_in

    def row_block(block, carry):
        first = pl.multiple_of(block * 8, 8)
        rows = pl.ds(first, 8)
        slot = lax.rem(block, 2)
        if stored_in:
            for copy in copies(block, slot):
                copy.wait()

        if store_out:

            @pl.when(block >= 2)
            def _():
                for copy in copies(block - 2, slot):
                    copy.wait()

        own = own_ref[rows, :]
        own_x = jnp.broadcast_to(own[:, 0:1], (8, width))
        own_y = jnp.broadcast_to(own[:, 1:2], (8, width))
        own_z = jnp.broadcast_to(own[:, 2:3], (8, width))
        own_a = jnp.broadcast_to(own[:, 3:4], (8, width))
        if slope_mode:
            move_x = jnp.broadcast_to(own[:, 4:5], (8, width))
            move_y = jnp.broadcast_to(own[:, 5:6], (8, width))
            move_z = jnp.broadcast_to(own[:, 6:7], (8, width))

        def lane_block(chunk, sums):
            start = pl.multiple_of(chunk * width, width)
            span = pl.ds(start, width)
            if needs_geometry:
                diff_x = all_ref[0:1, span] - own_x
                diff_y = all_ref[1:2, span] - own_y
                diff_z = all_ref[2:3, span] - own_z
                square = (
                    diff_x * diff_x
                    + diff_y * diff_y
                    + diff_z * diff_z
                    + 0.5 * (all_ref[3:4, span] + own_a)
                )
                inverse = lax.rsqrt(square)
                radius = square * inverse
                phase = wave_value * radius
            if stored_in:
                real_part = real_buf[rows, span]
                imag_part = imag_buf[rows, span]
                if slope_mode:
                    along_move = diff_x * move_x + diff_y * move_y + diff_z * move_z
                    factor = along_move * (inverse * inverse)
                    first_part = (-real_part - phase * imag_part) * factor
                    second_part = (phase * real_part - imag_part) * factor
                else:
                    first_part = real_part
                    second_part = imag_part
            else:
                sine_part, cosine_part = sin_cos(phase)
                if slope_mode:
                    along_move = diff_x * move_x + diff_y * move_y + diff_z * move_z
                    factor = along_move * (inverse * inverse * inverse) * (1.0 / four_pi)
                    first_part = (-cosine_part - phase * sine_part) * factor
                    second_part = (phase * cosine_part - sine_part) * factor
                else:
                    factor = inverse * (1.0 / four_pi)
                    first_part = cosine_part * factor
                    second_part = sine_part * factor
                if store_out:
                    real_buf[slot, :, span] = first_part
                    imag_buf[slot, :, span] = second_part
            zone_count = len(sums) // 3
            both_parts = first_part + second_part
            new_sums = []
            for zone in range(zone_count):
                new_sums.append(sums[zone] + first_part * vec_ref[zone:zone + 1, span])
            for zone in range(zone_count, 2 * zone_count):
                new_sums.append(sums[zone] + second_part * vec_ref[zone:zone + 1, span])
            for zone in range(2 * zone_count, 3 * zone_count):
                new_sums.append(sums[zone] + both_parts * vec_ref[zone:zone + 1, span])
            return tuple(new_sums)

        columns = vec_ref.shape[0]
        zeros = tuple(jnp.zeros((8, width), jnp.float32) for _ in range(columns))
        sums = lax.fori_loop(0, chunk_count, lane_block, zeros, unroll=4 if stored_in and not slope_mode else 3)
        lane = lax.broadcasted_iota(jnp.int32, (8, columns), 1)
        result = jnp.zeros((8, columns), jnp.float32)
        for column in range(columns):
            total = jnp.sum(sums[column], axis=1, keepdims=True)
            result = jnp.where(lane == column, total, result)
        out_ref[rows, :] = result
        if store_out:
            for copy in copies(block, slot):
                copy.start()
        return carry

    if stored_in:
        for block in range(block_count):
            for copy in copies(block, 0):
                copy.start()
    lax.fori_loop(0, block_count, row_block, 0)
    if store_out:
        for block in range(max(0, block_count - 2), block_count):
            for copy in copies(block, block % 2):
                copy.wait()


def panel_contract(slope_mode, wavenumber, own_table, all_table, vector_full, stored=None, store_out=False):
    zone_count = vector_full.shape[1] // 2
    vector_rows = jnp.concatenate(
        [vector_full.T, (vector_full[:, :zone_count] - vector_full[:, zone_count:]).T], 0
    )
    outs = panel_call(slope_mode, wavenumber, own_table, all_table, vector_rows, stored, store_out)
    sums = outs[0] if store_out else outs
    first_sum = sums[:, :zone_count]
    second_sum = sums[:, zone_count:2 * zone_count]
    both_sum = sums[:, 2 * zone_count:]
    if slope_mode:
        imag_sum = both_sum - first_sum + second_sum
    else:
        imag_sum = first_sum - second_sum - both_sum
    combined = jnp.concatenate([first_sum + second_sum, imag_sum], 1)
    if store_out:
        return (combined,) + tuple(outs[1:])
    return combined


def panel_call(slope_mode, wavenumber, own_table, all_table, vector_rows, stored, store_out):
    own_total = own_table.shape[0]
    columns = vector_rows.shape[0]
    panel_total = all_table.shape[1]
    elements = own_total * panel_total
    stored_in = stored is not None
    operands = [wavenumber, own_table, all_table, vector_rows]
    out_shape = [jax.ShapeDtypeStruct((own_total, columns), jnp.float32)]
    matrix_bytes = 0
    if stored_in:
        operands += list(stored)
        matrix_bytes = 8 * elements
    if store_out:
        out_shape += [jax.ShapeDtypeStruct((own_total, panel_total), jnp.float32)] * 2
        matrix_bytes = 8 * elements
    vmem = pl.BlockSpec(memory_space=pltpu.VMEM)
    hbm = pl.BlockSpec(memory_space=pltpu.HBM)
    params = {}
    if stored_in:
        params["scratch_shapes"] = [
            pltpu.VMEM((own_total, panel_total), jnp.float32),
            pltpu.VMEM((own_total, panel_total), jnp.float32),
            pltpu.SemaphoreType.DMA((2, own_total // 8)),
        ]
        params["compiler_params"] = pltpu.CompilerParams(vmem_limit_bytes=60 * 1024 * 1024)
    elif store_out:
        params["scratch_shapes"] = [
            pltpu.VMEM((2, 8, panel_total), jnp.float32),
            pltpu.VMEM((2, 8, panel_total), jnp.float32),
            pltpu.SemaphoreType.DMA((2, 2)),
        ]
    if stored_in and not slope_mode:
        flops, transcendentals = 32 * elements, 0
    elif stored_in:
        flops, transcendentals = 60 * elements, 2 * elements
    else:
        flops, transcendentals = 150 * elements, 4 * elements
    return pl.pallas_call(
        functools.partial(panel_kernel, slope_mode, stored_in, store_out),
        out_shape=tuple(out_shape) if store_out else out_shape[0],
        in_specs=[pl.BlockSpec(memory_space=pltpu.SMEM)] + [vmem] * 3 + [hbm] * (len(operands) - 4),
        out_specs=tuple([vmem] + [hbm] * (len(out_shape) - 1)) if store_out else vmem,
        cost_estimate=pl.CostEstimate(
            flops=flops,
            transcendentals=transcendentals,
            bytes_accessed=4 * (own_table.size + all_table.size + vector_rows.size + own_total * columns) + matrix_bytes,
        ),
        **params,
    )(*operands)


def gather_axis(vector, name):
    count = lax.axis_size(name)
    if count > 8:
        return lax.all_gather(vector, name, axis=0, tiled=True)
    index = lax.axis_index(name)
    parts = [vector]
    for shift in range(1, count):
        parts.append(lax.ppermute(vector, name, [(i, (i + shift) % count) for i in range(count)]))
    stacked = jnp.stack([parts[(-offset) % count] for offset in range(count)])
    ordered = jnp.roll(stacked, index, axis=0)
    return ordered.reshape((count * vector.shape[0],) + vector.shape[1:])


def gather_panels(vector):
    return gather_axis(gather_axis(vector, "col"), "row")


def chunk_size_of(count, limit):
    return math.gcd(count, limit)


def rows_sum(block_fn, count, limit):
    size = chunk_size_of(count, limit)
    starts = jnp.arange(count // size, dtype=jnp.int32) * size
    return jnp.sum(lax.map(lambda start: block_fn(start, size), starts), 0)


def local(
    centers,
    panel_areas,
    jump_term,
    displacement,
    design_ids,
    primal_field,
    adjoint_start,
    mic_panels,
    wavenumber,
):
    zone_count = adjoint_start.shape[1] // 2
    owned_count = centers.shape[1]
    axes = ("row", "col")
    wave_value = wavenumber[0]
    packed = jnp.concatenate([centers.T, panel_areas[:, None], adjoint_start], 1)
    gathered = gather_panels(packed)
    panel_total = gathered.shape[0]
    all_xyz = gathered[:, :3].T
    all_area = gathered[:, 3]
    start_full = gathered[:, 4:]
    all_table = gathered[:, :4].T
    own_table = jnp.concatenate(
        [centers.T, panel_areas[:, None], displacement.T, jnp.zeros((owned_count, 1), jnp.float32)], 1
    )

    store = 8 * owned_count * panel_total <= STORE_LIMIT
    saved = []

    def apply_adjoint(vector_full, vector_own):
        if store and saved:
            summed = panel_contract(False, wavenumber, own_table, all_table, vector_full, stored=saved)
        elif store:
            summed, real_part, imag_part = panel_contract(
                False, wavenumber, own_table, all_table, vector_full, store_out=True
            )
            saved.extend([real_part, imag_part])
        else:
            summed = panel_contract(False, wavenumber, own_table, all_table, vector_full)
        return panel_areas[:, None] * summed + jump_term[:, None] * vector_own

    first_panel = (
        lax.axis_index("row") * lax.axis_size("col") + lax.axis_index("col")
    ) * owned_count
    panel_ids = first_panel + jnp.arange(owned_count, dtype=jnp.int32)
    mic_hits = jnp.sum(
        (panel_ids[:, None, None] == mic_panels[None, :, :]).astype(jnp.float32), axis=2
    )
    right_side = jnp.concatenate(
        [mic_hits * primal_field[0][:, None], mic_hits * primal_field[1][:, None]], 1
    )
    residual = right_side - apply_adjoint(start_full, adjoint_start)
    residual_full = gather_panels(residual)
    start_norm = jnp.sqrt(square_sum(residual_full))
    start_scale = jnp.concatenate([start_norm, start_norm])[None, :]
    basis_one = residual / start_scale
    basis_one_full = residual_full / start_scale
    image_one = apply_adjoint(basis_one_full, basis_one)
    image_one_full = gather_panels(image_one)
    first_re, first_im = inner_parts(basis_one_full, image_one_full, zone_count)
    lean_one_full = image_one_full - complex_scale(first_re, first_im, basis_one_full, zone_count)
    lean_one = image_one - complex_scale(first_re, first_im, basis_one, zone_count)
    first_norm = jnp.sqrt(square_sum(lean_one_full))
    first_scale = jnp.concatenate([first_norm, first_norm])[None, :]
    basis_two = lean_one / first_scale
    basis_two_full = lean_one_full / first_scale
    image_two = apply_adjoint(basis_two_full, basis_two)
    image_two_full = gather_panels(image_two)
    cross_re, cross_im = inner_parts(basis_one_full, image_two_full, zone_count)
    second_re, second_im = inner_parts(basis_two_full, image_two_full, zone_count)
    lean_two_full = (
        image_two_full
        - complex_scale(cross_re, cross_im, basis_one_full, zone_count)
        - complex_scale(second_re, second_im, basis_two_full, zone_count)
    )
    second_norm = jnp.sqrt(square_sum(lean_two_full))
    coef_one_re, coef_one_im, coef_two_re, coef_two_im = least_squares(
        start_norm,
        first_re,
        first_im,
        first_norm,
        cross_re,
        cross_im,
        second_re,
        second_im,
        second_norm,
    )
    adjoint_field = (
        adjoint_start
        + complex_scale(coef_one_re, coef_one_im, basis_one, zone_count)
        + complex_scale(coef_two_re, coef_two_im, basis_two, zone_count)
    )
    field_full = (
        start_full
        + complex_scale(coef_one_re, coef_one_im, basis_one_full, zone_count)
        + complex_scale(coef_two_re, coef_two_im, basis_two_full, zone_count)
    )

    contracted = panel_contract(True, wavenumber, own_table, all_table, field_full, stored=saved or None)
    contrib = panel_areas[:, None] * (
        primal_field[0][:, None] * contracted[:, :zone_count]
        - primal_field[1][:, None] * contracted[:, zone_count:]
    )
    onehot = (design_ids[:, None] == jnp.arange(DESIGN, dtype=jnp.int32)[None, :]).astype(
        jnp.float32
    )
    local_sums = contract_first(contrib, onehot)
    if lax.axis_size("row") > 8:
        sensitivity = lax.psum(lax.psum(local_sums, "col"), "row")
    else:
        sensitivity = jnp.sum(gather_axis(lax.psum(local_sums, "col")[None], "row"), 0)
    return (adjoint_field, sensitivity)


def solution(mesh):
    return jax.shard_map(
        local,
        mesh=mesh,
        in_specs=(
            P(None, ("row", "col")),
            P(("row", "col")),
            P(("row", "col")),
            P(None, ("row", "col")),
            P(("row", "col")),
            P(None, ("row", "col")),
            P(("row", "col"), None),
            P(),
            P(),
        ),
        out_specs=(P(("row", "col"), None), P()),
        check_vma=False,
    )
```

```python
import functools
import math

import jax
import jax.numpy as jnp
from jax import lax
from jax.experimental import pallas as pl
from jax.experimental.pallas import tpu as pltpu
from jax.sharding import PartitionSpec as P

DESIGN = 128


highest = lax.Precision.HIGHEST
four_pi = 4.0 * math.pi


def distances(rows_xyz, rows_area, cols_xyz, cols_area):
    diff_x = rows_xyz[0][:, None] - cols_xyz[0][None, :]
    diff_y = rows_xyz[1][:, None] - cols_xyz[1][None, :]
    diff_z = rows_xyz[2][:, None] - cols_xyz[2][None, :]
    square = (
        diff_x * diff_x
        + diff_y * diff_y
        + diff_z * diff_z
        + 0.5 * (rows_area[:, None] + cols_area[None, :])
    )
    return (diff_x, diff_y, diff_z, jnp.sqrt(square))


def kernel_parts(rows_xyz, rows_area, cols_xyz, cols_area, wave_value):
    radius = distances(rows_xyz, rows_area, cols_xyz, cols_area)[3]
    phase = wave_value * radius
    factor = 1.0 / (four_pi * radius)
    return (jnp.cos(phase) * factor, jnp.sin(phase) * factor)


def slope_parts(rows_xyz, rows_area, cols_xyz, cols_area, cols_move, wave_value):
    diff_x, diff_y, diff_z, radius = distances(rows_xyz, rows_area, cols_xyz, cols_area)
    along_move = (
        diff_x * cols_move[0][None, :]
        + diff_y * cols_move[1][None, :]
        + diff_z * cols_move[2][None, :]
    )
    phase = wave_value * radius
    cosine_part = jnp.cos(phase)
    sine_part = jnp.sin(phase)
    factor = along_move / (four_pi * radius * radius * radius)
    return ((-cosine_part - phase * sine_part) * factor, (phase * cosine_part - sine_part) * factor)


def contract_first(matrix, vector):
    return lax.dot_general(matrix, vector, (((0,), (0,)), ((), ())), precision=highest)


def conj_columns(real_part, imag_part, vector, zone_count):
    left_part = contract_first(real_part, vector)
    right_part = contract_first(imag_part, vector)
    return jnp.concatenate(
        [
            left_part[:, :zone_count] + right_part[:, zone_count:],
            left_part[:, zone_count:] - right_part[:, :zone_count],
        ],
        1,
    )


def inner_parts(left_part, right_part, zone_count):
    left_re, left_im = (left_part[:, :zone_count], left_part[:, zone_count:])
    right_re, right_im = (right_part[:, :zone_count], right_part[:, zone_count:])
    return (
        jnp.sum(left_re * right_re + left_im * right_im, 0),
        jnp.sum(left_re * right_im - left_im * right_re, 0),
    )


def square_sum(vector):
    return jnp.sum(vector * vector, 0).reshape(2, -1).sum(0)


def complex_scale(scale_re, scale_im, vector, zone_count):
    vec_re, vec_im = (vector[:, :zone_count], vector[:, zone_count:])
    return jnp.concatenate(
        [scale_re * vec_re - scale_im * vec_im, scale_re * vec_im + scale_im * vec_re], 1
    )


def least_squares(
    start_norm,
    first_re,
    first_im,
    first_norm,
    cross_re,
    cross_im,
    second_re,
    second_im,
    second_norm,
):
    gram_one = first_re * first_re + first_im * first_im + first_norm * first_norm
    gram_off_re = first_re * cross_re + first_im * cross_im + first_norm * second_re
    gram_off_im = first_re * cross_im - first_im * cross_re + first_norm * second_im
    gram_two = (
        cross_re * cross_re
        + cross_im * cross_im
        + second_re * second_re
        + second_im * second_im
        + second_norm * second_norm
    )
    rhs_one_re = start_norm * first_re
    rhs_one_im = -start_norm * first_im
    rhs_two_re = start_norm * cross_re
    rhs_two_im = -start_norm * cross_im
    determinant = gram_one * gram_two - gram_off_re * gram_off_re - gram_off_im * gram_off_im
    coef_one_re = (
        gram_two * rhs_one_re - (gram_off_re * rhs_two_re - gram_off_im * rhs_two_im)
    ) / determinant
    coef_one_im = (
        gram_two * rhs_one_im - (gram_off_re * rhs_two_im + gram_off_im * rhs_two_re)
    ) / determinant
    coef_two_re = (
        gram_one * rhs_two_re - (gram_off_re * rhs_one_re + gram_off_im * rhs_one_im)
    ) / determinant
    coef_two_im = (
        gram_one * rhs_two_im - (gram_off_re * rhs_one_im - gram_off_im * rhs_one_re)
    ) / determinant
    return (coef_one_re, coef_one_im, coef_two_re, coef_two_im)


def slope_parts_t(own_xyz, own_area, own_move, all_xyz, all_area, wave_value):
    diff_x = all_xyz[0][None, :] - own_xyz[0][:, None]
    diff_y = all_xyz[1][None, :] - own_xyz[1][:, None]
    diff_z = all_xyz[2][None, :] - own_xyz[2][:, None]
    square = (
        diff_x * diff_x
        + diff_y * diff_y
        + diff_z * diff_z
        + 0.5 * (all_area[None, :] + own_area[:, None])
    )
    radius = jnp.sqrt(square)
    along_move = (
        diff_x * own_move[0][:, None]
        + diff_y * own_move[1][:, None]
        + diff_z * own_move[2][:, None]
    )
    phase = wave_value * radius
    cosine_part = jnp.cos(phase)
    sine_part = jnp.sin(phase)
    factor = along_move / (four_pi * radius * radius * radius)
    return ((-cosine_part - phase * sine_part) * factor, (phase * cosine_part - sine_part) * factor)


TWO_OVER_PI = 0.6366197723675814
HALF_PI_HI = 1.5703125
HALF_PI_MID = 4.837512969970703125e-4
HALF_PI_LO = 7.54978995489188216e-8


def sin_cos(angle):
    turns = jnp.floor(angle * TWO_OVER_PI + 0.5)
    rest = angle - turns * HALF_PI_HI
    rest = rest - turns * HALF_PI_MID
    rest = rest - turns * HALF_PI_LO
    rest2 = rest * rest
    sine = rest + rest * rest2 * (
        -1.6666654611e-1 + rest2 * (8.3321608736e-3 + rest2 * (-1.9515295891e-4))
    )
    cosine = 1.0 - 0.5 * rest2 + rest2 * rest2 * (
        4.166664568298827e-2 + rest2 * (-1.388731625493765e-3 + rest2 * 2.443315711809948e-5)
    )
    quarter = turns.astype(jnp.int32)
    swap = (quarter & 1) == 1
    sine_out = jnp.where(swap, cosine, sine)
    cosine_out = jnp.where(swap, sine, cosine)
    sine_out = jnp.where((quarter & 2) == 2, -sine_out, sine_out)
    cosine_out = jnp.where(((quarter + 1) & 2) == 2, -cosine_out, cosine_out)
    return sine_out, cosine_out


LANES = 256
STORE_LIMIT = 24 * 1024 * 1024


def panel_kernel(slope_mode, stored_in, store_out, wave_ref, own_ref, all_ref, vec_ref, *refs):
    if stored_in:
        real_hbm, imag_hbm, out_ref, real_buf, imag_buf, sems = refs
        hbm_refs, buf_refs = [real_hbm, imag_hbm], [real_buf, imag_buf]
    elif store_out:
        out_ref = refs[0]
        hbm_refs = list(refs[1:1 + store_out])
        buf_refs = list(refs[1 + store_out:1 + 2 * store_out])
        sems = refs[-1]
    else:
        (out_ref,) = refs
    block_count = own_ref.shape[0] // 8

    def copies(block, slot):
        rows = pl.ds(pl.multiple_of(block * 8, 8), 8)
        pairs = list(zip(hbm_refs, buf_refs))
        if stored_in:
            return [pltpu.make_async_copy(hbm.at[rows], buf.at[rows], sems.at[k, block]) for k, (hbm, buf) in enumerate(pairs)]
        return [pltpu.make_async_copy(buf.at[slot], hbm.at[rows], sems.at[k, slot]) for k, (hbm, buf) in enumerate(pairs)]
    wave_value = wave_ref[0]
    own_total = own_ref.shape[0]
    panel_total = all_ref.shape[1]
    width = LANES if panel_total % LANES == 0 else 128
    chunk_count = panel_total // width
    needs_geometry = not stored_in or (slope_mode and stored_in == 1)

    def row_block(block, carry):
        first = pl.multiple_of(block * 8, 8)
        rows = pl.ds(first, 8)
        slot = lax.rem(block, 2)
        if stored_in:
            for copy in copies(block, slot):
                copy.wait()

        if store_out:

            @pl.when(block >= 2)
            def _():
                for copy in copies(block - 2, slot):
                    copy.wait()

        own = own_ref[rows, :]
        own_x = jnp.broadcast_to(own[:, 0:1], (8, width))
        own_y = jnp.broadcast_to(own[:, 1:2], (8, width))
        own_z = jnp.broadcast_to(own[:, 2:3], (8, width))
        own_a = jnp.broadcast_to(own[:, 3:4], (8, width))
        if slope_mode or store_out == 4:
            move_x = jnp.broadcast_to(own[:, 4:5], (8, width))
            move_y = jnp.broadcast_to(own[:, 5:6], (8, width))
            move_z = jnp.broadcast_to(own[:, 6:7], (8, width))

        def lane_block(chunk, sums):
            start = pl.multiple_of(chunk * width, width)
            span = pl.ds(start, width)
            if needs_geometry:
                diff_x = all_ref[0:1, span] - own_x
                diff_y = all_ref[1:2, span] - own_y
                diff_z = all_ref[2:3, span] - own_z
                square = (
                    diff_x * diff_x
                    + diff_y * diff_y
                    + diff_z * diff_z
                    + 0.5 * (all_ref[3:4, span] + own_a)
                )
                inverse = lax.rsqrt(square)
                radius = square * inverse
                phase = wave_value * radius
            if stored_in:
                real_part = real_buf[rows, span]
                imag_part = imag_buf[rows, span]
                if stored_in == 2:
                    first_part = real_part
                    second_part = imag_part
                elif slope_mode:
                    along_move = diff_x * move_x + diff_y * move_y + diff_z * move_z
                    factor = along_move * (inverse * inverse)
                    first_part = (-real_part - phase * imag_part) * factor
                    second_part = (phase * real_part - imag_part) * factor
                else:
                    first_part = real_part
                    second_part = imag_part
            else:
                sine_part, cosine_part = sin_cos(phase)
                if slope_mode:
                    along_move = diff_x * move_x + diff_y * move_y + diff_z * move_z
                    factor = along_move * (inverse * inverse * inverse) * (1.0 / four_pi)
                    first_part = (-cosine_part - phase * sine_part) * factor
                    second_part = (phase * cosine_part - sine_part) * factor
                else:
                    factor = inverse * (1.0 / four_pi)
                    first_part = cosine_part * factor
                    second_part = sine_part * factor
                if store_out:
                    buf_refs[0][slot, :, span] = first_part
                    buf_refs[1][slot, :, span] = second_part
                if store_out == 4:
                    along_move = diff_x * move_x + diff_y * move_y + diff_z * move_z
                    slope_factor = along_move * (inverse * inverse * inverse) * (1.0 / four_pi)
                    buf_refs[2][slot, :, span] = (-cosine_part - phase * sine_part) * slope_factor
                    buf_refs[3][slot, :, span] = (phase * cosine_part - sine_part) * slope_factor
            zone_count = len(sums) // 3
            both_parts = first_part + second_part
            new_sums = []
            for zone in range(zone_count):
                new_sums.append(sums[zone] + first_part * vec_ref[zone:zone + 1, span])
            for zone in range(zone_count, 2 * zone_count):
                new_sums.append(sums[zone] + second_part * vec_ref[zone:zone + 1, span])
            for zone in range(2 * zone_count, 3 * zone_count):
                new_sums.append(sums[zone] + both_parts * vec_ref[zone:zone + 1, span])
            return tuple(new_sums)

        columns = vec_ref.shape[0]
        zeros = tuple(jnp.zeros((8, width), jnp.float32) for _ in range(columns))
        sums = lax.fori_loop(0, chunk_count, lane_block, zeros, unroll=4 if stored_in and not slope_mode else 3)
        lane = lax.broadcasted_iota(jnp.int32, (8, columns), 1)
        result = jnp.zeros((8, columns), jnp.float32)
        for column in range(columns):
            total = jnp.sum(sums[column], axis=1, keepdims=True)
            result = jnp.where(lane == column, total, result)
        out_ref[rows, :] = result
        if store_out:
            for copy in copies(block, slot):
                copy.start()
        return carry

    if stored_in:
        for block in range(block_count):
            for copy in copies(block, 0):
                copy.start()
    lax.fori_loop(0, block_count, row_block, 0)
    if store_out:
        for block in range(max(0, block_count - 2), block_count):
            for copy in copies(block, block % 2):
                copy.wait()


def panel_contract(slope_mode, wavenumber, own_table, all_table, vector_full, stored=None, store_out=0, direct=False):
    zone_count = vector_full.shape[1] // 2
    vector_rows = jnp.concatenate(
        [vector_full.T, (vector_full[:, :zone_count] - vector_full[:, zone_count:]).T], 0
    )
    outs = panel_call(slope_mode, wavenumber, own_table, all_table, vector_rows, stored, store_out, direct)
    sums = outs[0] if store_out else outs
    first_sum = sums[:, :zone_count]
    second_sum = sums[:, zone_count:2 * zone_count]
    both_sum = sums[:, 2 * zone_count:]
    if slope_mode:
        imag_sum = both_sum - first_sum + second_sum
    else:
        imag_sum = first_sum - second_sum - both_sum
    combined = jnp.concatenate([first_sum + second_sum, imag_sum], 1)
    if store_out:
        return (combined,) + tuple(outs[1:])
    return combined


def panel_call(slope_mode, wavenumber, own_table, all_table, vector_rows, stored, store_out, direct):
    own_total = own_table.shape[0]
    columns = vector_rows.shape[0]
    panel_total = all_table.shape[1]
    elements = own_total * panel_total
    stored_in = 0 if stored is None else (2 if direct else 1)
    operands = [wavenumber, own_table, all_table, vector_rows]
    out_shape = [jax.ShapeDtypeStruct((own_total, columns), jnp.float32)]
    matrix_bytes = 0
    if stored_in:
        operands += list(stored)
        matrix_bytes = 8 * elements
    if store_out:
        out_shape += [jax.ShapeDtypeStruct((own_total, panel_total), jnp.float32)] * store_out
        matrix_bytes = 4 * store_out * elements
    vmem = pl.BlockSpec(memory_space=pltpu.VMEM)
    hbm = pl.BlockSpec(memory_space=pltpu.HBM)
    params = {}
    if stored_in:
        params["scratch_shapes"] = [
            pltpu.VMEM((own_total, panel_total), jnp.float32),
            pltpu.VMEM((own_total, panel_total), jnp.float32),
            pltpu.SemaphoreType.DMA((2, own_total // 8)),
        ]
        params["compiler_params"] = pltpu.CompilerParams(vmem_limit_bytes=60 * 1024 * 1024)
    elif store_out:
        params["scratch_shapes"] = [pltpu.VMEM((2, 8, panel_total), jnp.float32)] * store_out + [
            pltpu.SemaphoreType.DMA((store_out, 2))
        ]
    if stored_in == 2 or (stored_in and not slope_mode):
        flops, transcendentals = 32 * elements, 0
    elif stored_in:
        flops, transcendentals = 60 * elements, 2 * elements
    else:
        flops, transcendentals = 150 * elements, 4 * elements
    return pl.pallas_call(
        functools.partial(panel_kernel, slope_mode, stored_in, store_out),
        out_shape=tuple(out_shape) if store_out else out_shape[0],
        in_specs=[pl.BlockSpec(memory_space=pltpu.SMEM)] + [vmem] * 3 + [hbm] * (len(operands) - 4),
        out_specs=tuple([vmem] + [hbm] * (len(out_shape) - 1)) if store_out else vmem,
        cost_estimate=pl.CostEstimate(
            flops=flops,
            transcendentals=transcendentals,
            bytes_accessed=4 * (own_table.size + all_table.size + vector_rows.size + own_total * columns) + matrix_bytes,
        ),
        **params,
    )(*operands)


def gather_axis(vector, name):
    count = lax.axis_size(name)
    if count > 8:
        return lax.all_gather(vector, name, axis=0, tiled=True)
    index = lax.axis_index(name)
    parts = [vector]
    for shift in range(1, count):
        parts.append(lax.ppermute(vector, name, [(i, (i + shift) % count) for i in range(count)]))
    stacked = jnp.stack([parts[(-offset) % count] for offset in range(count)])
    ordered = jnp.roll(stacked, index, axis=0)
    return ordered.reshape((count * vector.shape[0],) + vector.shape[1:])


def gather_panels(vector):
    return gather_axis(gather_axis(vector, "col"), "row")


def chunk_size_of(count, limit):
    return math.gcd(count, limit)


def rows_sum(block_fn, count, limit):
    size = chunk_size_of(count, limit)
    starts = jnp.arange(count // size, dtype=jnp.int32) * size
    return jnp.sum(lax.map(lambda start: block_fn(start, size), starts), 0)


def local(
    centers,
    panel_areas,
    jump_term,
    displacement,
    design_ids,
    primal_field,
    adjoint_start,
    mic_panels,
    wavenumber,
):
    zone_count = adjoint_start.shape[1] // 2
    owned_count = centers.shape[1]
    axes = ("row", "col")
    wave_value = wavenumber[0]
    packed = jnp.concatenate([centers.T, panel_areas[:, None], adjoint_start], 1)
    gathered = gather_panels(packed)
    panel_total = gathered.shape[0]
    all_xyz = gathered[:, :3].T
    all_area = gathered[:, 3]
    start_full = gathered[:, 4:]
    all_table = gathered[:, :4].T
    own_table = jnp.concatenate(
        [centers.T, panel_areas[:, None], displacement.T, jnp.zeros((owned_count, 1), jnp.float32)], 1
    )

    store = 8 * owned_count * panel_total <= STORE_LIMIT
    store_slope = 16 * owned_count * panel_total <= 2 * STORE_LIMIT
    saved = []
    slope_saved = []

    def apply_adjoint(vector_full, vector_own):
        if store and saved:
            summed = panel_contract(False, wavenumber, own_table, all_table, vector_full, stored=saved)
        elif store:
            summed, *parts = panel_contract(
                False, wavenumber, own_table, all_table, vector_full, store_out=4 if store_slope else 2
            )
            saved.extend(parts[:2])
            slope_saved.extend(parts[2:])
        else:
            summed = panel_contract(False, wavenumber, own_table, all_table, vector_full)
        return panel_areas[:, None] * summed + jump_term[:, None] * vector_own

    first_panel = (
        lax.axis_index("row") * lax.axis_size("col") + lax.axis_index("col")
    ) * owned_count
    panel_ids = first_panel + jnp.arange(owned_count, dtype=jnp.int32)
    mic_hits = jnp.sum(
        (panel_ids[:, None, None] == mic_panels[None, :, :]).astype(jnp.float32), axis=2
    )
    right_side = jnp.concatenate(
        [mic_hits * primal_field[0][:, None], mic_hits * primal_field[1][:, None]], 1
    )
    residual = right_side - apply_adjoint(start_full, adjoint_start)
    residual_full = gather_panels(residual)
    start_norm = jnp.sqrt(square_sum(residual_full))
    start_scale = jnp.concatenate([start_norm, start_norm])[None, :]
    basis_one = residual / start_scale
    basis_one_full = residual_full / start_scale
    image_one = apply_adjoint(basis_one_full, basis_one)
    image_one_full = gather_panels(image_one)
    first_re, first_im = inner_parts(basis_one_full, image_one_full, zone_count)
    lean_one_full = image_one_full - complex_scale(first_re, first_im, basis_one_full, zone_count)
    lean_one = image_one - complex_scale(first_re, first_im, basis_one, zone_count)
    first_norm = jnp.sqrt(square_sum(lean_one_full))
    first_scale = jnp.concatenate([first_norm, first_norm])[None, :]
    basis_two = lean_one / first_scale
    basis_two_full = lean_one_full / first_scale
    image_two = apply_adjoint(basis_two_full, basis_two)
    image_two_full = gather_panels(image_two)
    cross_re, cross_im = inner_parts(basis_one_full, image_two_full, zone_count)
    second_re, second_im = inner_parts(basis_two_full, image_two_full, zone_count)
    lean_two_full = (
        image_two_full
        - complex_scale(cross_re, cross_im, basis_one_full, zone_count)
        - complex_scale(second_re, second_im, basis_two_full, zone_count)
    )
    second_norm = jnp.sqrt(square_sum(lean_two_full))
    coef_one_re, coef_one_im, coef_two_re, coef_two_im = least_squares(
        start_norm,
        first_re,
        first_im,
        first_norm,
        cross_re,
        cross_im,
        second_re,
        second_im,
        second_norm,
    )
    adjoint_field = (
        adjoint_start
        + complex_scale(coef_one_re, coef_one_im, basis_one, zone_count)
        + complex_scale(coef_two_re, coef_two_im, basis_two, zone_count)
    )
    field_full = (
        start_full
        + complex_scale(coef_one_re, coef_one_im, basis_one_full, zone_count)
        + complex_scale(coef_two_re, coef_two_im, basis_two_full, zone_count)
    )

    if slope_saved:
        contracted = panel_contract(True, wavenumber, own_table, all_table, field_full, stored=slope_saved, direct=True)
    else:
        contracted = panel_contract(True, wavenumber, own_table, all_table, field_full, stored=saved or None)
    contrib = panel_areas[:, None] * (
        primal_field[0][:, None] * contracted[:, :zone_count]
        - primal_field[1][:, None] * contracted[:, zone_count:]
    )
    onehot = (design_ids[:, None] == jnp.arange(DESIGN, dtype=jnp.int32)[None, :]).astype(
        jnp.float32
    )
    local_sums = contract_first(contrib, onehot)
    if lax.axis_size("row") > 8:
        sensitivity = lax.psum(lax.psum(local_sums, "col"), "row")
    else:
        sensitivity = jnp.sum(gather_axis(lax.psum(local_sums, "col")[None], "row"), 0)
    return (adjoint_field, sensitivity)


def solution(mesh):
    return jax.shard_map(
        local,
        mesh=mesh,
        in_specs=(
            P(None, ("row", "col")),
            P(("row", "col")),
            P(("row", "col")),
            P(None, ("row", "col")),
            P(("row", "col")),
            P(None, ("row", "col")),
            P(("row", "col"), None),
            P(),
            P(),
        ),
        out_specs=(P(("row", "col"), None), P()),
        check_vma=False,
    )
```

```python
import functools
import math

import jax
import jax.numpy as jnp
from jax import lax
from jax.experimental import pallas as pl
from jax.experimental.pallas import tpu as pltpu
from jax.sharding import PartitionSpec as P

DESIGN = 128


highest = lax.Precision.HIGHEST
four_pi = 4.0 * math.pi


def distances(rows_xyz, rows_area, cols_xyz, cols_area):
    diff_x = rows_xyz[0][:, None] - cols_xyz[0][None, :]
    diff_y = rows_xyz[1][:, None] - cols_xyz[1][None, :]
    diff_z = rows_xyz[2][:, None] - cols_xyz[2][None, :]
    square = (
        diff_x * diff_x
        + diff_y * diff_y
        + diff_z * diff_z
        + 0.5 * (rows_area[:, None] + cols_area[None, :])
    )
    return (diff_x, diff_y, diff_z, jnp.sqrt(square))


def kernel_parts(rows_xyz, rows_area, cols_xyz, cols_area, wave_value):
    radius = distances(rows_xyz, rows_area, cols_xyz, cols_area)[3]
    phase = wave_value * radius
    factor = 1.0 / (four_pi * radius)
    return (jnp.cos(phase) * factor, jnp.sin(phase) * factor)


def slope_parts(rows_xyz, rows_area, cols_xyz, cols_area, cols_move, wave_value):
    diff_x, diff_y, diff_z, radius = distances(rows_xyz, rows_area, cols_xyz, cols_area)
    along_move = (
        diff_x * cols_move[0][None, :]
        + diff_y * cols_move[1][None, :]
        + diff_z * cols_move[2][None, :]
    )
    phase = wave_value * radius
    cosine_part = jnp.cos(phase)
    sine_part = jnp.sin(phase)
    factor = along_move / (four_pi * radius * radius * radius)
    return ((-cosine_part - phase * sine_part) * factor, (phase * cosine_part - sine_part) * factor)


def contract_first(matrix, vector):
    return lax.dot_general(matrix, vector, (((0,), (0,)), ((), ())), precision=highest)


def conj_columns(real_part, imag_part, vector, zone_count):
    left_part = contract_first(real_part, vector)
    right_part = contract_first(imag_part, vector)
    return jnp.concatenate(
        [
            left_part[:, :zone_count] + right_part[:, zone_count:],
            left_part[:, zone_count:] - right_part[:, :zone_count],
        ],
        1,
    )


def inner_parts(left_part, right_part, zone_count):
    left_re, left_im = (left_part[:, :zone_count], left_part[:, zone_count:])
    right_re, right_im = (right_part[:, :zone_count], right_part[:, zone_count:])
    return (
        jnp.sum(left_re * right_re + left_im * right_im, 0),
        jnp.sum(left_re * right_im - left_im * right_re, 0),
    )


def square_sum(vector):
    return jnp.sum(vector * vector, 0).reshape(2, -1).sum(0)


def complex_scale(scale_re, scale_im, vector, zone_count):
    vec_re, vec_im = (vector[:, :zone_count], vector[:, zone_count:])
    return jnp.concatenate(
        [scale_re * vec_re - scale_im * vec_im, scale_re * vec_im + scale_im * vec_re], 1
    )


def least_squares(
    start_norm,
    first_re,
    first_im,
    first_norm,
    cross_re,
    cross_im,
    second_re,
    second_im,
    second_norm,
):
    gram_one = first_re * first_re + first_im * first_im + first_norm * first_norm
    gram_off_re = first_re * cross_re + first_im * cross_im + first_norm * second_re
    gram_off_im = first_re * cross_im - first_im * cross_re + first_norm * second_im
    gram_two = (
        cross_re * cross_re
        + cross_im * cross_im
        + second_re * second_re
        + second_im * second_im
        + second_norm * second_norm
    )
    rhs_one_re = start_norm * first_re
    rhs_one_im = -start_norm * first_im
    rhs_two_re = start_norm * cross_re
    rhs_two_im = -start_norm * cross_im
    determinant = gram_one * gram_two - gram_off_re * gram_off_re - gram_off_im * gram_off_im
    coef_one_re = (
        gram_two * rhs_one_re - (gram_off_re * rhs_two_re - gram_off_im * rhs_two_im)
    ) / determinant
    coef_one_im = (
        gram_two * rhs_one_im - (gram_off_re * rhs_two_im + gram_off_im * rhs_two_re)
    ) / determinant
    coef_two_re = (
        gram_one * rhs_two_re - (gram_off_re * rhs_one_re + gram_off_im * rhs_one_im)
    ) / determinant
    coef_two_im = (
        gram_one * rhs_two_im - (gram_off_re * rhs_one_im - gram_off_im * rhs_one_re)
    ) / determinant
    return (coef_one_re, coef_one_im, coef_two_re, coef_two_im)


def slope_parts_t(own_xyz, own_area, own_move, all_xyz, all_area, wave_value):
    diff_x = all_xyz[0][None, :] - own_xyz[0][:, None]
    diff_y = all_xyz[1][None, :] - own_xyz[1][:, None]
    diff_z = all_xyz[2][None, :] - own_xyz[2][:, None]
    square = (
        diff_x * diff_x
        + diff_y * diff_y
        + diff_z * diff_z
        + 0.5 * (all_area[None, :] + own_area[:, None])
    )
    radius = jnp.sqrt(square)
    along_move = (
        diff_x * own_move[0][:, None]
        + diff_y * own_move[1][:, None]
        + diff_z * own_move[2][:, None]
    )
    phase = wave_value * radius
    cosine_part = jnp.cos(phase)
    sine_part = jnp.sin(phase)
    factor = along_move / (four_pi * radius * radius * radius)
    return ((-cosine_part - phase * sine_part) * factor, (phase * cosine_part - sine_part) * factor)


TWO_OVER_PI = 0.6366197723675814
HALF_PI_HI = 1.5703125
HALF_PI_MID = 4.837512969970703125e-4
HALF_PI_LO = 7.54978995489188216e-8


def sin_cos(angle):
    turns = jnp.floor(angle * TWO_OVER_PI + 0.5)
    rest = angle - turns * HALF_PI_HI
    rest = rest - turns * HALF_PI_MID
    rest = rest - turns * HALF_PI_LO
    rest2 = rest * rest
    sine = rest + rest * rest2 * (
        -1.6666654611e-1 + rest2 * (8.3321608736e-3 + rest2 * (-1.9515295891e-4))
    )
    cosine = 1.0 - 0.5 * rest2 + rest2 * rest2 * (
        4.166664568298827e-2 + rest2 * (-1.388731625493765e-3 + rest2 * 2.443315711809948e-5)
    )
    quarter = turns.astype(jnp.int32)
    swap = (quarter & 1) == 1
    sine_out = jnp.where(swap, cosine, sine)
    cosine_out = jnp.where(swap, sine, cosine)
    sine_out = jnp.where((quarter & 2) == 2, -sine_out, sine_out)
    cosine_out = jnp.where(((quarter + 1) & 2) == 2, -cosine_out, cosine_out)
    return sine_out, cosine_out


LANES = 256
STORE_LIMIT = 24 * 1024 * 1024


def panel_kernel(slope_mode, stored_in, store_out, wave_ref, own_ref, all_ref, vec_ref, *refs):
    if stored_in:
        real_hbm, imag_hbm, out_ref, real_buf, imag_buf, sems = refs
        hbm_refs, buf_refs = [real_hbm, imag_hbm], [real_buf, imag_buf]
    elif store_out:
        out_ref = refs[0]
        hbm_refs = list(refs[1:1 + store_out])
        buf_refs = list(refs[1 + store_out:1 + 2 * store_out])
        sems = refs[-1]
    else:
        (out_ref,) = refs
    block_count = own_ref.shape[0] // 8

    def copies(block, slot):
        rows = pl.ds(pl.multiple_of(block * 8, 8), 8)
        pairs = list(zip(hbm_refs, buf_refs))
        if stored_in:
            return [pltpu.make_async_copy(hbm.at[rows], buf.at[rows], sems.at[k, block]) for k, (hbm, buf) in enumerate(pairs)]
        return [pltpu.make_async_copy(buf.at[slot], hbm.at[rows], sems.at[k, slot]) for k, (hbm, buf) in enumerate(pairs)]
    wave_value = wave_ref[0]
    own_total = own_ref.shape[0]
    panel_total = all_ref.shape[1]
    width = LANES if panel_total % LANES == 0 else 128
    chunk_count = panel_total // width
    needs_geometry = not stored_in or (slope_mode and stored_in == 1)

    def row_block(block, carry):
        first = pl.multiple_of(block * 8, 8)
        rows = pl.ds(first, 8)
        slot = lax.rem(block, 2)
        if stored_in:
            for copy in copies(block, slot):
                copy.wait()

        if store_out:

            @pl.when(block >= 2)
            def _():
                for copy in copies(block - 2, slot):
                    copy.wait()

        own = own_ref[rows, :]
        own_x = jnp.broadcast_to(own[:, 0:1], (8, width))
        own_y = jnp.broadcast_to(own[:, 1:2], (8, width))
        own_z = jnp.broadcast_to(own[:, 2:3], (8, width))
        own_a = jnp.broadcast_to(own[:, 3:4], (8, width))
        if slope_mode or store_out == 4:
            move_x = jnp.broadcast_to(own[:, 4:5], (8, width))
            move_y = jnp.broadcast_to(own[:, 5:6], (8, width))
            move_z = jnp.broadcast_to(own[:, 6:7], (8, width))

        def lane_block(chunk, sums):
            start = pl.multiple_of(chunk * width, width)
            span = pl.ds(start, width)
            if needs_geometry:
                diff_x = all_ref[0:1, span] - own_x
                diff_y = all_ref[1:2, span] - own_y
                diff_z = all_ref[2:3, span] - own_z
                square = (
                    diff_x * diff_x
                    + diff_y * diff_y
                    + diff_z * diff_z
                    + 0.5 * (all_ref[3:4, span] + own_a)
                )
                inverse = lax.rsqrt(square)
                radius = square * inverse
                phase = wave_value * radius
            if stored_in:
                real_part = real_buf[rows, span]
                imag_part = imag_buf[rows, span]
                if stored_in == 2:
                    first_part = real_part
                    second_part = imag_part
                elif slope_mode:
                    along_move = diff_x * move_x + diff_y * move_y + diff_z * move_z
                    factor = along_move * (inverse * inverse)
                    first_part = (-real_part - phase * imag_part) * factor
                    second_part = (phase * real_part - imag_part) * factor
                else:
                    first_part = real_part
                    second_part = imag_part
            else:
                sine_part, cosine_part = sin_cos(phase)
                if slope_mode:
                    along_move = diff_x * move_x + diff_y * move_y + diff_z * move_z
                    factor = along_move * (inverse * inverse * inverse) * (1.0 / four_pi)
                    first_part = (-cosine_part - phase * sine_part) * factor
                    second_part = (phase * cosine_part - sine_part) * factor
                else:
                    factor = inverse * (1.0 / four_pi)
                    first_part = cosine_part * factor
                    second_part = sine_part * factor
                if store_out:
                    buf_refs[0][slot, :, span] = first_part
                    buf_refs[1][slot, :, span] = second_part
                if store_out == 4:
                    along_move = diff_x * move_x + diff_y * move_y + diff_z * move_z
                    slope_factor = along_move * (inverse * inverse * inverse) * (1.0 / four_pi)
                    buf_refs[2][slot, :, span] = (-cosine_part - phase * sine_part) * slope_factor
                    buf_refs[3][slot, :, span] = (phase * cosine_part - sine_part) * slope_factor
            zone_count = len(sums) // 3
            both_parts = first_part + second_part
            new_sums = []
            for zone in range(zone_count):
                new_sums.append(sums[zone] + first_part * vec_ref[zone:zone + 1, span])
            for zone in range(zone_count, 2 * zone_count):
                new_sums.append(sums[zone] + second_part * vec_ref[zone:zone + 1, span])
            for zone in range(2 * zone_count, 3 * zone_count):
                new_sums.append(sums[zone] + both_parts * vec_ref[zone:zone + 1, span])
            return tuple(new_sums)

        columns = vec_ref.shape[0]
        zeros = tuple(jnp.zeros((8, width), jnp.float32) for _ in range(columns))
        sums = lax.fori_loop(0, chunk_count, lane_block, zeros, unroll=4 if stored_in or store_out else 3)
        lane = lax.broadcasted_iota(jnp.int32, (8, columns), 1)
        result = jnp.zeros((8, columns), jnp.float32)
        for column in range(columns):
            total = jnp.sum(sums[column], axis=1, keepdims=True)
            result = jnp.where(lane == column, total, result)
        out_ref[rows, :] = result
        if store_out:
            for copy in copies(block, slot):
                copy.start()
        return carry

    if stored_in:
        for block in range(block_count):
            for copy in copies(block, 0):
                copy.start()
    lax.fori_loop(0, block_count, row_block, 0)
    if store_out:
        for block in range(max(0, block_count - 2), block_count):
            for copy in copies(block, block % 2):
                copy.wait()


def panel_contract(slope_mode, wavenumber, own_table, all_table, vector_full, stored=None, store_out=0, direct=False):
    zone_count = vector_full.shape[1] // 2
    vector_rows = jnp.concatenate(
        [vector_full.T, (vector_full[:, :zone_count] - vector_full[:, zone_count:]).T], 0
    )
    outs = panel_call(slope_mode, wavenumber, own_table, all_table, vector_rows, stored, store_out, direct)
    sums = outs[0] if store_out else outs
    first_sum = sums[:, :zone_count]
    second_sum = sums[:, zone_count:2 * zone_count]
    both_sum = sums[:, 2 * zone_count:]
    if slope_mode:
        imag_sum = both_sum - first_sum + second_sum
    else:
        imag_sum = first_sum - second_sum - both_sum
    combined = jnp.concatenate([first_sum + second_sum, imag_sum], 1)
    if store_out:
        return (combined,) + tuple(outs[1:])
    return combined


def panel_call(slope_mode, wavenumber, own_table, all_table, vector_rows, stored, store_out, direct):
    own_total = own_table.shape[0]
    columns = vector_rows.shape[0]
    panel_total = all_table.shape[1]
    elements = own_total * panel_total
    stored_in = 0 if stored is None else (2 if direct else 1)
    operands = [wavenumber, own_table, all_table, vector_rows]
    out_shape = [jax.ShapeDtypeStruct((own_total, columns), jnp.float32)]
    matrix_bytes = 0
    if stored_in:
        operands += list(stored)
        matrix_bytes = 8 * elements
    if store_out:
        out_shape += [jax.ShapeDtypeStruct((own_total, panel_total), jnp.float32)] * store_out
        matrix_bytes = 4 * store_out * elements
    vmem = pl.BlockSpec(memory_space=pltpu.VMEM)
    hbm = pl.BlockSpec(memory_space=pltpu.HBM)
    params = {}
    if stored_in:
        params["scratch_shapes"] = [
            pltpu.VMEM((own_total, panel_total), jnp.float32),
            pltpu.VMEM((own_total, panel_total), jnp.float32),
            pltpu.SemaphoreType.DMA((2, own_total // 8)),
        ]
        params["compiler_params"] = pltpu.CompilerParams(vmem_limit_bytes=60 * 1024 * 1024)
    elif store_out:
        params["scratch_shapes"] = [pltpu.VMEM((2, 8, panel_total), jnp.float32)] * store_out + [
            pltpu.SemaphoreType.DMA((store_out, 2))
        ]
    if stored_in == 2 or (stored_in and not slope_mode):
        flops, transcendentals = 32 * elements, 0
    elif stored_in:
        flops, transcendentals = 60 * elements, 2 * elements
    else:
        flops, transcendentals = 150 * elements, 4 * elements
    return pl.pallas_call(
        functools.partial(panel_kernel, slope_mode, stored_in, store_out),
        out_shape=tuple(out_shape) if store_out else out_shape[0],
        in_specs=[pl.BlockSpec(memory_space=pltpu.SMEM)] + [vmem] * 3 + [hbm] * (len(operands) - 4),
        out_specs=tuple([vmem] + [hbm] * (len(out_shape) - 1)) if store_out else vmem,
        cost_estimate=pl.CostEstimate(
            flops=flops,
            transcendentals=transcendentals,
            bytes_accessed=4 * (own_table.size + all_table.size + vector_rows.size + own_total * columns) + matrix_bytes,
        ),
        **params,
    )(*operands)


def gather_axis(vector, name):
    count = lax.axis_size(name)
    if count > 8:
        return lax.all_gather(vector, name, axis=0, tiled=True)
    index = lax.axis_index(name)
    parts = [vector]
    for shift in range(1, count):
        parts.append(lax.ppermute(vector, name, [(i, (i + shift) % count) for i in range(count)]))
    stacked = jnp.stack([parts[(-offset) % count] for offset in range(count)])
    ordered = jnp.roll(stacked, index, axis=0)
    return ordered.reshape((count * vector.shape[0],) + vector.shape[1:])


def gather_panels(vector):
    return gather_axis(gather_axis(vector, "col"), "row")


def chunk_size_of(count, limit):
    return math.gcd(count, limit)


def rows_sum(block_fn, count, limit):
    size = chunk_size_of(count, limit)
    starts = jnp.arange(count // size, dtype=jnp.int32) * size
    return jnp.sum(lax.map(lambda start: block_fn(start, size), starts), 0)


def local(
    centers,
    panel_areas,
    jump_term,
    displacement,
    design_ids,
    primal_field,
    adjoint_start,
    mic_panels,
    wavenumber,
):
    zone_count = adjoint_start.shape[1] // 2
    owned_count = centers.shape[1]
    axes = ("row", "col")
    wave_value = wavenumber[0]
    packed = jnp.concatenate([centers.T, panel_areas[:, None], adjoint_start], 1)
    gathered = gather_panels(packed)
    panel_total = gathered.shape[0]
    all_xyz = gathered[:, :3].T
    all_area = gathered[:, 3]
    start_full = gathered[:, 4:]
    all_table = gathered[:, :4].T
    own_table = jnp.concatenate(
        [centers.T, panel_areas[:, None], displacement.T, jnp.zeros((owned_count, 1), jnp.float32)], 1
    )

    store = 8 * owned_count * panel_total <= STORE_LIMIT
    store_slope = 16 * owned_count * panel_total <= 2 * STORE_LIMIT
    saved = []
    slope_saved = []

    def apply_adjoint(vector_full, vector_own):
        if store and saved:
            summed = panel_contract(False, wavenumber, own_table, all_table, vector_full, stored=saved)
        elif store:
            summed, *parts = panel_contract(
                False, wavenumber, own_table, all_table, vector_full, store_out=4 if store_slope else 2
            )
            saved.extend(parts[:2])
            slope_saved.extend(parts[2:])
        else:
            summed = panel_contract(False, wavenumber, own_table, all_table, vector_full)
        return panel_areas[:, None] * summed + jump_term[:, None] * vector_own

    first_panel = (
        lax.axis_index("row") * lax.axis_size("col") + lax.axis_index("col")
    ) * owned_count
    panel_ids = first_panel + jnp.arange(owned_count, dtype=jnp.int32)
    mic_hits = jnp.sum(
        (panel_ids[:, None, None] == mic_panels[None, :, :]).astype(jnp.float32), axis=2
    )
    right_side = jnp.concatenate(
        [mic_hits * primal_field[0][:, None], mic_hits * primal_field[1][:, None]], 1
    )
    residual = right_side - apply_adjoint(start_full, adjoint_start)
    residual_full = gather_panels(residual)
    start_norm = jnp.sqrt(square_sum(residual_full))
    start_scale = jnp.concatenate([start_norm, start_norm])[None, :]
    basis_one = residual / start_scale
    basis_one_full = residual_full / start_scale
    image_one = apply_adjoint(basis_one_full, basis_one)
    image_one_full = gather_panels(image_one)
    first_re, first_im = inner_parts(basis_one_full, image_one_full, zone_count)
    lean_one_full = image_one_full - complex_scale(first_re, first_im, basis_one_full, zone_count)
    lean_one = image_one - complex_scale(first_re, first_im, basis_one, zone_count)
    first_norm = jnp.sqrt(square_sum(lean_one_full))
    first_scale = jnp.concatenate([first_norm, first_norm])[None, :]
    basis_two = lean_one / first_scale
    basis_two_full = lean_one_full / first_scale
    image_two = apply_adjoint(basis_two_full, basis_two)
    image_two_full = gather_panels(image_two)
    cross_re, cross_im = inner_parts(basis_one_full, image_two_full, zone_count)
    second_re, second_im = inner_parts(basis_two_full, image_two_full, zone_count)
    lean_two_full = (
        image_two_full
        - complex_scale(cross_re, cross_im, basis_one_full, zone_count)
        - complex_scale(second_re, second_im, basis_two_full, zone_count)
    )
    second_norm = jnp.sqrt(square_sum(lean_two_full))
    coef_one_re, coef_one_im, coef_two_re, coef_two_im = least_squares(
        start_norm,
        first_re,
        first_im,
        first_norm,
        cross_re,
        cross_im,
        second_re,
        second_im,
        second_norm,
    )
    adjoint_field = (
        adjoint_start
        + complex_scale(coef_one_re, coef_one_im, basis_one, zone_count)
        + complex_scale(coef_two_re, coef_two_im, basis_two, zone_count)
    )
    field_full = (
        start_full
        + complex_scale(coef_one_re, coef_one_im, basis_one_full, zone_count)
        + complex_scale(coef_two_re, coef_two_im, basis_two_full, zone_count)
    )

    if slope_saved:
        contracted = panel_contract(True, wavenumber, own_table, all_table, field_full, stored=slope_saved, direct=True)
    else:
        contracted = panel_contract(True, wavenumber, own_table, all_table, field_full, stored=saved or None)
    contrib = panel_areas[:, None] * (
        primal_field[0][:, None] * contracted[:, :zone_count]
        - primal_field[1][:, None] * contracted[:, zone_count:]
    )
    onehot = (design_ids[:, None] == jnp.arange(DESIGN, dtype=jnp.int32)[None, :]).astype(
        jnp.float32
    )
    local_sums = contract_first(contrib, onehot)
    if lax.axis_size("row") > 8:
        sensitivity = lax.psum(lax.psum(local_sums, "col"), "row")
    else:
        sensitivity = jnp.sum(gather_axis(lax.psum(local_sums, "col")[None], "row"), 0)
    return (adjoint_field, sensitivity)


def solution(mesh):
    return jax.shard_map(
        local,
        mesh=mesh,
        in_specs=(
            P(None, ("row", "col")),
            P(("row", "col")),
            P(("row", "col")),
            P(None, ("row", "col")),
            P(("row", "col")),
            P(None, ("row", "col")),
            P(("row", "col"), None),
            P(),
            P(),
        ),
        out_specs=(P(("row", "col"), None), P()),
        check_vma=False,
    )
```

```python
import functools
import math

import jax
import jax.numpy as jnp
from jax import lax
from jax.experimental import pallas as pl
from jax.experimental.pallas import tpu as pltpu
from jax.sharding import PartitionSpec as P

DESIGN = 128


highest = lax.Precision.HIGHEST
four_pi = 4.0 * math.pi


def distances(rows_xyz, rows_area, cols_xyz, cols_area):
    diff_x = rows_xyz[0][:, None] - cols_xyz[0][None, :]
    diff_y = rows_xyz[1][:, None] - cols_xyz[1][None, :]
    diff_z = rows_xyz[2][:, None] - cols_xyz[2][None, :]
    square = (
        diff_x * diff_x
        + diff_y * diff_y
        + diff_z * diff_z
        + 0.5 * (rows_area[:, None] + cols_area[None, :])
    )
    return (diff_x, diff_y, diff_z, jnp.sqrt(square))


def kernel_parts(rows_xyz, rows_area, cols_xyz, cols_area, wave_value):
    radius = distances(rows_xyz, rows_area, cols_xyz, cols_area)[3]
    phase = wave_value * radius
    factor = 1.0 / (four_pi * radius)
    return (jnp.cos(phase) * factor, jnp.sin(phase) * factor)


def slope_parts(rows_xyz, rows_area, cols_xyz, cols_area, cols_move, wave_value):
    diff_x, diff_y, diff_z, radius = distances(rows_xyz, rows_area, cols_xyz, cols_area)
    along_move = (
        diff_x * cols_move[0][None, :]
        + diff_y * cols_move[1][None, :]
        + diff_z * cols_move[2][None, :]
    )
    phase = wave_value * radius
    cosine_part = jnp.cos(phase)
    sine_part = jnp.sin(phase)
    factor = along_move / (four_pi * radius * radius * radius)
    return ((-cosine_part - phase * sine_part) * factor, (phase * cosine_part - sine_part) * factor)


def contract_first(matrix, vector):
    return lax.dot_general(matrix, vector, (((0,), (0,)), ((), ())), precision=highest)


def conj_columns(real_part, imag_part, vector, zone_count):
    left_part = contract_first(real_part, vector)
    right_part = contract_first(imag_part, vector)
    return jnp.concatenate(
        [
            left_part[:, :zone_count] + right_part[:, zone_count:],
            left_part[:, zone_count:] - right_part[:, :zone_count],
        ],
        1,
    )


def inner_parts(left_part, right_part, zone_count):
    left_re, left_im = (left_part[:, :zone_count], left_part[:, zone_count:])
    right_re, right_im = (right_part[:, :zone_count], right_part[:, zone_count:])
    return (
        jnp.sum(left_re * right_re + left_im * right_im, 0),
        jnp.sum(left_re * right_im - left_im * right_re, 0),
    )


def square_sum(vector):
    return jnp.sum(vector * vector, 0).reshape(2, -1).sum(0)


def complex_scale(scale_re, scale_im, vector, zone_count):
    vec_re, vec_im = (vector[:, :zone_count], vector[:, zone_count:])
    return jnp.concatenate(
        [scale_re * vec_re - scale_im * vec_im, scale_re * vec_im + scale_im * vec_re], 1
    )


def least_squares(
    start_norm,
    first_re,
    first_im,
    first_norm,
    cross_re,
    cross_im,
    second_re,
    second_im,
    second_norm,
):
    gram_one = first_re * first_re + first_im * first_im + first_norm * first_norm
    gram_off_re = first_re * cross_re + first_im * cross_im + first_norm * second_re
    gram_off_im = first_re * cross_im - first_im * cross_re + first_norm * second_im
    gram_two = (
        cross_re * cross_re
        + cross_im * cross_im
        + second_re * second_re
        + second_im * second_im
        + second_norm * second_norm
    )
    rhs_one_re = start_norm * first_re
    rhs_one_im = -start_norm * first_im
    rhs_two_re = start_norm * cross_re
    rhs_two_im = -start_norm * cross_im
    determinant = gram_one * gram_two - gram_off_re * gram_off_re - gram_off_im * gram_off_im
    coef_one_re = (
        gram_two * rhs_one_re - (gram_off_re * rhs_two_re - gram_off_im * rhs_two_im)
    ) / determinant
    coef_one_im = (
        gram_two * rhs_one_im - (gram_off_re * rhs_two_im + gram_off_im * rhs_two_re)
    ) / determinant
    coef_two_re = (
        gram_one * rhs_two_re - (gram_off_re * rhs_one_re + gram_off_im * rhs_one_im)
    ) / determinant
    coef_two_im = (
        gram_one * rhs_two_im - (gram_off_re * rhs_one_im - gram_off_im * rhs_one_re)
    ) / determinant
    return (coef_one_re, coef_one_im, coef_two_re, coef_two_im)


def slope_parts_t(own_xyz, own_area, own_move, all_xyz, all_area, wave_value):
    diff_x = all_xyz[0][None, :] - own_xyz[0][:, None]
    diff_y = all_xyz[1][None, :] - own_xyz[1][:, None]
    diff_z = all_xyz[2][None, :] - own_xyz[2][:, None]
    square = (
        diff_x * diff_x
        + diff_y * diff_y
        + diff_z * diff_z
        + 0.5 * (all_area[None, :] + own_area[:, None])
    )
    radius = jnp.sqrt(square)
    along_move = (
        diff_x * own_move[0][:, None]
        + diff_y * own_move[1][:, None]
        + diff_z * own_move[2][:, None]
    )
    phase = wave_value * radius
    cosine_part = jnp.cos(phase)
    sine_part = jnp.sin(phase)
    factor = along_move / (four_pi * radius * radius * radius)
    return ((-cosine_part - phase * sine_part) * factor, (phase * cosine_part - sine_part) * factor)


TWO_OVER_PI = 0.6366197723675814
HALF_PI_HI = 1.5703125
HALF_PI_MID = 4.837512969970703125e-4
HALF_PI_LO = 7.54978995489188216e-8


def sin_cos(angle):
    turns = jnp.floor(angle * TWO_OVER_PI + 0.5)
    rest = angle - turns * HALF_PI_HI
    rest = rest - turns * HALF_PI_MID
    rest = rest - turns * HALF_PI_LO
    rest2 = rest * rest
    sine = rest + rest * rest2 * (
        -1.6666654611e-1 + rest2 * (8.3321608736e-3 + rest2 * (-1.9515295891e-4))
    )
    cosine = 1.0 - 0.5 * rest2 + rest2 * rest2 * (
        4.166664568298827e-2 + rest2 * (-1.388731625493765e-3 + rest2 * 2.443315711809948e-5)
    )
    quarter = turns.astype(jnp.int32)
    swap = (quarter & 1) == 1
    sine_out = jnp.where(swap, cosine, sine)
    cosine_out = jnp.where(swap, sine, cosine)
    sine_out = jnp.where((quarter & 2) == 2, -sine_out, sine_out)
    cosine_out = jnp.where(((quarter + 1) & 2) == 2, -cosine_out, cosine_out)
    return sine_out, cosine_out


LANES = 256
STORE_LIMIT = 24 * 1024 * 1024


def panel_kernel(slope_mode, stored_in, store_out, wave_ref, own_ref, all_ref, vec_ref, *refs):
    if stored_in:
        real_hbm, imag_hbm, out_ref, real_buf, imag_buf, sems = refs
        hbm_refs, buf_refs = [real_hbm, imag_hbm], [real_buf, imag_buf]
    elif store_out:
        out_ref = refs[0]
        hbm_refs = list(refs[1:1 + store_out])
        buf_refs = list(refs[1 + store_out:1 + 2 * store_out])
        sems = refs[-1]
    else:
        (out_ref,) = refs
    block_count = own_ref.shape[0] // 8

    def copies(block, slot):
        rows = pl.ds(pl.multiple_of(block * 8, 8), 8)
        pairs = list(zip(hbm_refs, buf_refs))
        if stored_in:
            return [pltpu.make_async_copy(hbm.at[rows], buf.at[rows], sems.at[k, block]) for k, (hbm, buf) in enumerate(pairs)]
        return [pltpu.make_async_copy(buf.at[slot], hbm.at[rows], sems.at[k, slot]) for k, (hbm, buf) in enumerate(pairs)]
    wave_value = wave_ref[0]
    own_total = own_ref.shape[0]
    panel_total = all_ref.shape[1]
    width = LANES if panel_total % LANES == 0 else 128
    chunk_count = panel_total // width
    needs_geometry = not stored_in or (slope_mode and stored_in == 1)

    def row_block(block, carry):
        first = pl.multiple_of(block * 8, 8)
        rows = pl.ds(first, 8)
        slot = lax.rem(block, 2)
        if stored_in:
            for copy in copies(block, slot):
                copy.wait()

        if store_out:

            @pl.when(block >= 2)
            def _():
                for copy in copies(block - 2, slot):
                    copy.wait()

        own = own_ref[rows, :]
        own_x = jnp.broadcast_to(own[:, 0:1], (8, width))
        own_y = jnp.broadcast_to(own[:, 1:2], (8, width))
        own_z = jnp.broadcast_to(own[:, 2:3], (8, width))
        own_a = jnp.broadcast_to(own[:, 3:4], (8, width))
        if slope_mode or store_out == 4:
            move_x = jnp.broadcast_to(own[:, 4:5], (8, width))
            move_y = jnp.broadcast_to(own[:, 5:6], (8, width))
            move_z = jnp.broadcast_to(own[:, 6:7], (8, width))

        def lane_block(chunk, sums):
            start = pl.multiple_of(chunk * width, width)
            span = pl.ds(start, width)
            if needs_geometry:
                diff_x = all_ref[0:1, span] - own_x
                diff_y = all_ref[1:2, span] - own_y
                diff_z = all_ref[2:3, span] - own_z
                square = (
                    diff_x * diff_x
                    + diff_y * diff_y
                    + diff_z * diff_z
                    + 0.5 * (all_ref[3:4, span] + own_a)
                )
                inverse = lax.rsqrt(square)
                radius = square * inverse
                phase = wave_value * radius
            if stored_in:
                real_part = real_buf[rows, span]
                imag_part = imag_buf[rows, span]
                if stored_in == 2:
                    first_part = real_part
                    second_part = imag_part
                elif slope_mode:
                    along_move = diff_x * move_x + diff_y * move_y + diff_z * move_z
                    factor = along_move * (inverse * inverse)
                    first_part = (-real_part - phase * imag_part) * factor
                    second_part = (phase * real_part - imag_part) * factor
                else:
                    first_part = real_part
                    second_part = imag_part
            else:
                sine_part, cosine_part = sin_cos(phase)
                if slope_mode:
                    along_move = diff_x * move_x + diff_y * move_y + diff_z * move_z
                    factor = along_move * (inverse * inverse * inverse) * (1.0 / four_pi)
                    first_part = (-cosine_part - phase * sine_part) * factor
                    second_part = (phase * cosine_part - sine_part) * factor
                else:
                    factor = inverse * (1.0 / four_pi)
                    first_part = cosine_part * factor
                    second_part = sine_part * factor
                if store_out:
                    buf_refs[0][slot, :, span] = first_part
                    buf_refs[1][slot, :, span] = second_part
                if store_out == 4:
                    along_move = diff_x * move_x + diff_y * move_y + diff_z * move_z
                    slope_factor = along_move * (inverse * inverse * inverse) * (1.0 / four_pi)
                    buf_refs[2][slot, :, span] = (-cosine_part - phase * sine_part) * slope_factor
                    buf_refs[3][slot, :, span] = (phase * cosine_part - sine_part) * slope_factor
            zone_count = len(sums) // 3
            both_parts = first_part + second_part
            new_sums = []
            for zone in range(zone_count):
                new_sums.append(sums[zone] + first_part * vec_ref[zone:zone + 1, span])
            for zone in range(zone_count, 2 * zone_count):
                new_sums.append(sums[zone] + second_part * vec_ref[zone:zone + 1, span])
            for zone in range(2 * zone_count, 3 * zone_count):
                new_sums.append(sums[zone] + both_parts * vec_ref[zone:zone + 1, span])
            return tuple(new_sums)

        columns = vec_ref.shape[0]
        zeros = tuple(jnp.zeros((8, width), jnp.float32) for _ in range(columns))
        sums = lax.fori_loop(0, chunk_count, lane_block, zeros, unroll=6 if stored_in or store_out else 3)
        lane = lax.broadcasted_iota(jnp.int32, (8, columns), 1)
        result = jnp.zeros((8, columns), jnp.float32)
        for column in range(columns):
            total = jnp.sum(sums[column], axis=1, keepdims=True)
            result = jnp.where(lane == column, total, result)
        out_ref[rows, :] = result
        if store_out:
            for copy in copies(block, slot):
                copy.start()
        return carry

    if stored_in:
        for block in range(block_count):
            for copy in copies(block, 0):
                copy.start()
    lax.fori_loop(0, block_count, row_block, 0)
    if store_out:
        for block in range(max(0, block_count - 2), block_count):
            for copy in copies(block, block % 2):
                copy.wait()


def panel_contract(slope_mode, wavenumber, own_table, all_table, vector_full, stored=None, store_out=0, direct=False):
    zone_count = vector_full.shape[1] // 2
    vector_rows = jnp.concatenate(
        [vector_full.T, (vector_full[:, :zone_count] - vector_full[:, zone_count:]).T], 0
    )
    outs = panel_call(slope_mode, wavenumber, own_table, all_table, vector_rows, stored, store_out, direct)
    sums = outs[0] if store_out else outs
    first_sum = sums[:, :zone_count]
    second_sum = sums[:, zone_count:2 * zone_count]
    both_sum = sums[:, 2 * zone_count:]
    if slope_mode:
        imag_sum = both_sum - first_sum + second_sum
    else:
        imag_sum = first_sum - second_sum - both_sum
    combined = jnp.concatenate([first_sum + second_sum, imag_sum], 1)
    if store_out:
        return (combined,) + tuple(outs[1:])
    return combined


def panel_call(slope_mode, wavenumber, own_table, all_table, vector_rows, stored, store_out, direct):
    own_total = own_table.shape[0]
    columns = vector_rows.shape[0]
    panel_total = all_table.shape[1]
    elements = own_total * panel_total
    stored_in = 0 if stored is None else (2 if direct else 1)
    operands = [wavenumber, own_table, all_table, vector_rows]
    out_shape = [jax.ShapeDtypeStruct((own_total, columns), jnp.float32)]
    matrix_bytes = 0
    if stored_in:
        operands += list(stored)
        matrix_bytes = 8 * elements
    if store_out:
        out_shape += [jax.ShapeDtypeStruct((own_total, panel_total), jnp.float32)] * store_out
        matrix_bytes = 4 * store_out * elements
    vmem = pl.BlockSpec(memory_space=pltpu.VMEM)
    hbm = pl.BlockSpec(memory_space=pltpu.HBM)
    params = {}
    if stored_in:
        params["scratch_shapes"] = [
            pltpu.VMEM((own_total, panel_total), jnp.float32),
            pltpu.VMEM((own_total, panel_total), jnp.float32),
            pltpu.SemaphoreType.DMA((2, own_total // 8)),
        ]
        params["compiler_params"] = pltpu.CompilerParams(vmem_limit_bytes=60 * 1024 * 1024)
    elif store_out:
        params["scratch_shapes"] = [pltpu.VMEM((2, 8, panel_total), jnp.float32)] * store_out + [
            pltpu.SemaphoreType.DMA((store_out, 2))
        ]
    if stored_in == 2 or (stored_in and not slope_mode):
        flops, transcendentals = 32 * elements, 0
    elif stored_in:
        flops, transcendentals = 60 * elements, 2 * elements
    else:
        flops, transcendentals = 150 * elements, 4 * elements
    return pl.pallas_call(
        functools.partial(panel_kernel, slope_mode, stored_in, store_out),
        out_shape=tuple(out_shape) if store_out else out_shape[0],
        in_specs=[pl.BlockSpec(memory_space=pltpu.SMEM)] + [vmem] * 3 + [hbm] * (len(operands) - 4),
        out_specs=tuple([vmem] + [hbm] * (len(out_shape) - 1)) if store_out else vmem,
        cost_estimate=pl.CostEstimate(
            flops=flops,
            transcendentals=transcendentals,
            bytes_accessed=4 * (own_table.size + all_table.size + vector_rows.size + own_total * columns) + matrix_bytes,
        ),
        **params,
    )(*operands)


def gather_axis(vector, name):
    count = lax.axis_size(name)
    if count > 8:
        return lax.all_gather(vector, name, axis=0, tiled=True)
    index = lax.axis_index(name)
    parts = [vector]
    for shift in range(1, count):
        parts.append(lax.ppermute(vector, name, [(i, (i + shift) % count) for i in range(count)]))
    stacked = jnp.stack([parts[(-offset) % count] for offset in range(count)])
    ordered = jnp.roll(stacked, index, axis=0)
    return ordered.reshape((count * vector.shape[0],) + vector.shape[1:])


def gather_panels(vector):
    return gather_axis(gather_axis(vector, "col"), "row")


def chunk_size_of(count, limit):
    return math.gcd(count, limit)


def rows_sum(block_fn, count, limit):
    size = chunk_size_of(count, limit)
    starts = jnp.arange(count // size, dtype=jnp.int32) * size
    return jnp.sum(lax.map(lambda start: block_fn(start, size), starts), 0)


def local(
    centers,
    panel_areas,
    jump_term,
    displacement,
    design_ids,
    primal_field,
    adjoint_start,
    mic_panels,
    wavenumber,
):
    zone_count = adjoint_start.shape[1] // 2
    owned_count = centers.shape[1]
    axes = ("row", "col")
    wave_value = wavenumber[0]
    packed = jnp.concatenate([centers.T, panel_areas[:, None], adjoint_start], 1)
    gathered = gather_panels(packed)
    panel_total = gathered.shape[0]
    all_xyz = gathered[:, :3].T
    all_area = gathered[:, 3]
    start_full = gathered[:, 4:]
    all_table = gathered[:, :4].T
    own_table = jnp.concatenate(
        [centers.T, panel_areas[:, None], displacement.T, jnp.zeros((owned_count, 1), jnp.float32)], 1
    )

    store = 8 * owned_count * panel_total <= STORE_LIMIT
    store_slope = 16 * owned_count * panel_total <= 2 * STORE_LIMIT
    saved = []
    slope_saved = []

    def apply_adjoint(vector_full, vector_own):
        if store and saved:
            summed = panel_contract(False, wavenumber, own_table, all_table, vector_full, stored=saved)
        elif store:
            summed, *parts = panel_contract(
                False, wavenumber, own_table, all_table, vector_full, store_out=4 if store_slope else 2
            )
            saved.extend(parts[:2])
            slope_saved.extend(parts[2:])
        else:
            summed = panel_contract(False, wavenumber, own_table, all_table, vector_full)
        return panel_areas[:, None] * summed + jump_term[:, None] * vector_own

    first_panel = (
        lax.axis_index("row") * lax.axis_size("col") + lax.axis_index("col")
    ) * owned_count
    panel_ids = first_panel + jnp.arange(owned_count, dtype=jnp.int32)
    mic_hits = jnp.sum(
        (panel_ids[:, None, None] == mic_panels[None, :, :]).astype(jnp.float32), axis=2
    )
    right_side = jnp.concatenate(
        [mic_hits * primal_field[0][:, None], mic_hits * primal_field[1][:, None]], 1
    )
    residual = right_side - apply_adjoint(start_full, adjoint_start)
    residual_full = gather_panels(residual)
    start_norm = jnp.sqrt(square_sum(residual_full))
    start_scale = jnp.concatenate([start_norm, start_norm])[None, :]
    basis_one = residual / start_scale
    basis_one_full = residual_full / start_scale
    image_one = apply_adjoint(basis_one_full, basis_one)
    image_one_full = gather_panels(image_one)
    first_re, first_im = inner_parts(basis_one_full, image_one_full, zone_count)
    lean_one_full = image_one_full - complex_scale(first_re, first_im, basis_one_full, zone_count)
    lean_one = image_one - complex_scale(first_re, first_im, basis_one, zone_count)
    first_norm = jnp.sqrt(square_sum(lean_one_full))
    first_scale = jnp.concatenate([first_norm, first_norm])[None, :]
    basis_two = lean_one / first_scale
    basis_two_full = lean_one_full / first_scale
    image_two = apply_adjoint(basis_two_full, basis_two)
    image_two_full = gather_panels(image_two)
    cross_re, cross_im = inner_parts(basis_one_full, image_two_full, zone_count)
    second_re, second_im = inner_parts(basis_two_full, image_two_full, zone_count)
    lean_two_full = (
        image_two_full
        - complex_scale(cross_re, cross_im, basis_one_full, zone_count)
        - complex_scale(second_re, second_im, basis_two_full, zone_count)
    )
    second_norm = jnp.sqrt(square_sum(lean_two_full))
    coef_one_re, coef_one_im, coef_two_re, coef_two_im = least_squares(
        start_norm,
        first_re,
        first_im,
        first_norm,
        cross_re,
        cross_im,
        second_re,
        second_im,
        second_norm,
    )
    adjoint_field = (
        adjoint_start
        + complex_scale(coef_one_re, coef_one_im, basis_one, zone_count)
        + complex_scale(coef_two_re, coef_two_im, basis_two, zone_count)
    )
    field_full = (
        start_full
        + complex_scale(coef_one_re, coef_one_im, basis_one_full, zone_count)
        + complex_scale(coef_two_re, coef_two_im, basis_two_full, zone_count)
    )

    if slope_saved:
        contracted = panel_contract(True, wavenumber, own_table, all_table, field_full, stored=slope_saved, direct=True)
    else:
        contracted = panel_contract(True, wavenumber, own_table, all_table, field_full, stored=saved or None)
    contrib = panel_areas[:, None] * (
        primal_field[0][:, None] * contracted[:, :zone_count]
        - primal_field[1][:, None] * contracted[:, zone_count:]
    )
    onehot = (design_ids[:, None] == jnp.arange(DESIGN, dtype=jnp.int32)[None, :]).astype(
        jnp.float32
    )
    local_sums = contract_first(contrib, onehot)
    if lax.axis_size("row") > 8:
        sensitivity = lax.psum(lax.psum(local_sums, "col"), "row")
    else:
        sensitivity = jnp.sum(gather_axis(lax.psum(local_sums, "col")[None], "row"), 0)
    return (adjoint_field, sensitivity)


def solution(mesh):
    return jax.shard_map(
        local,
        mesh=mesh,
        in_specs=(
            P(None, ("row", "col")),
            P(("row", "col")),
            P(("row", "col")),
            P(None, ("row", "col")),
            P(("row", "col")),
            P(None, ("row", "col")),
            P(("row", "col"), None),
            P(),
            P(),
        ),
        out_specs=(P(("row", "col"), None), P()),
        check_vma=False,
    )
```

```python
import functools
import math

import jax
import jax.numpy as jnp
from jax import lax
from jax.experimental import pallas as pl
from jax.experimental.pallas import tpu as pltpu
from jax.sharding import PartitionSpec as P

DESIGN = 128


highest = lax.Precision.HIGHEST
four_pi = 4.0 * math.pi


def distances(rows_xyz, rows_area, cols_xyz, cols_area):
    diff_x = rows_xyz[0][:, None] - cols_xyz[0][None, :]
    diff_y = rows_xyz[1][:, None] - cols_xyz[1][None, :]
    diff_z = rows_xyz[2][:, None] - cols_xyz[2][None, :]
    square = (
        diff_x * diff_x
        + diff_y * diff_y
        + diff_z * diff_z
        + 0.5 * (rows_area[:, None] + cols_area[None, :])
    )
    return (diff_x, diff_y, diff_z, jnp.sqrt(square))


def kernel_parts(rows_xyz, rows_area, cols_xyz, cols_area, wave_value):
    radius = distances(rows_xyz, rows_area, cols_xyz, cols_area)[3]
    phase = wave_value * radius
    factor = 1.0 / (four_pi * radius)
    return (jnp.cos(phase) * factor, jnp.sin(phase) * factor)


def slope_parts(rows_xyz, rows_area, cols_xyz, cols_area, cols_move, wave_value):
    diff_x, diff_y, diff_z, radius = distances(rows_xyz, rows_area, cols_xyz, cols_area)
    along_move = (
        diff_x * cols_move[0][None, :]
        + diff_y * cols_move[1][None, :]
        + diff_z * cols_move[2][None, :]
    )
    phase = wave_value * radius
    cosine_part = jnp.cos(phase)
    sine_part = jnp.sin(phase)
    factor = along_move / (four_pi * radius * radius * radius)
    return ((-cosine_part - phase * sine_part) * factor, (phase * cosine_part - sine_part) * factor)


def contract_first(matrix, vector):
    return lax.dot_general(matrix, vector, (((0,), (0,)), ((), ())), precision=highest)


def conj_columns(real_part, imag_part, vector, zone_count):
    left_part = contract_first(real_part, vector)
    right_part = contract_first(imag_part, vector)
    return jnp.concatenate(
        [
            left_part[:, :zone_count] + right_part[:, zone_count:],
            left_part[:, zone_count:] - right_part[:, :zone_count],
        ],
        1,
    )


def inner_parts(left_part, right_part, zone_count):
    left_re, left_im = (left_part[:, :zone_count], left_part[:, zone_count:])
    right_re, right_im = (right_part[:, :zone_count], right_part[:, zone_count:])
    return (
        jnp.sum(left_re * right_re + left_im * right_im, 0),
        jnp.sum(left_re * right_im - left_im * right_re, 0),
    )


def square_sum(vector):
    return jnp.sum(vector * vector, 0).reshape(2, -1).sum(0)


def complex_scale(scale_re, scale_im, vector, zone_count):
    vec_re, vec_im = (vector[:, :zone_count], vector[:, zone_count:])
    return jnp.concatenate(
        [scale_re * vec_re - scale_im * vec_im, scale_re * vec_im + scale_im * vec_re], 1
    )


def least_squares(
    start_norm,
    first_re,
    first_im,
    first_norm,
    cross_re,
    cross_im,
    second_re,
    second_im,
    second_norm,
):
    gram_one = first_re * first_re + first_im * first_im + first_norm * first_norm
    gram_off_re = first_re * cross_re + first_im * cross_im + first_norm * second_re
    gram_off_im = first_re * cross_im - first_im * cross_re + first_norm * second_im
    gram_two = (
        cross_re * cross_re
        + cross_im * cross_im
        + second_re * second_re
        + second_im * second_im
        + second_norm * second_norm
    )
    rhs_one_re = start_norm * first_re
    rhs_one_im = -start_norm * first_im
    rhs_two_re = start_norm * cross_re
    rhs_two_im = -start_norm * cross_im
    determinant = gram_one * gram_two - gram_off_re * gram_off_re - gram_off_im * gram_off_im
    coef_one_re = (
        gram_two * rhs_one_re - (gram_off_re * rhs_two_re - gram_off_im * rhs_two_im)
    ) / determinant
    coef_one_im = (
        gram_two * rhs_one_im - (gram_off_re * rhs_two_im + gram_off_im * rhs_two_re)
    ) / determinant
    coef_two_re = (
        gram_one * rhs_two_re - (gram_off_re * rhs_one_re + gram_off_im * rhs_one_im)
    ) / determinant
    coef_two_im = (
        gram_one * rhs_two_im - (gram_off_re * rhs_one_im - gram_off_im * rhs_one_re)
    ) / determinant
    return (coef_one_re, coef_one_im, coef_two_re, coef_two_im)


def slope_parts_t(own_xyz, own_area, own_move, all_xyz, all_area, wave_value):
    diff_x = all_xyz[0][None, :] - own_xyz[0][:, None]
    diff_y = all_xyz[1][None, :] - own_xyz[1][:, None]
    diff_z = all_xyz[2][None, :] - own_xyz[2][:, None]
    square = (
        diff_x * diff_x
        + diff_y * diff_y
        + diff_z * diff_z
        + 0.5 * (all_area[None, :] + own_area[:, None])
    )
    radius = jnp.sqrt(square)
    along_move = (
        diff_x * own_move[0][:, None]
        + diff_y * own_move[1][:, None]
        + diff_z * own_move[2][:, None]
    )
    phase = wave_value * radius
    cosine_part = jnp.cos(phase)
    sine_part = jnp.sin(phase)
    factor = along_move / (four_pi * radius * radius * radius)
    return ((-cosine_part - phase * sine_part) * factor, (phase * cosine_part - sine_part) * factor)


TWO_OVER_PI = 0.6366197723675814
HALF_PI_HI = 1.5703125
HALF_PI_MID = 4.837512969970703125e-4
HALF_PI_LO = 7.54978995489188216e-8


def sin_cos(angle):
    turns = jnp.floor(angle * TWO_OVER_PI + 0.5)
    rest = angle - turns * HALF_PI_HI
    rest = rest - turns * HALF_PI_MID
    rest = rest - turns * HALF_PI_LO
    rest2 = rest * rest
    sine = rest + rest * rest2 * (
        -1.6666654611e-1 + rest2 * (8.3321608736e-3 + rest2 * (-1.9515295891e-4))
    )
    cosine = 1.0 - 0.5 * rest2 + rest2 * rest2 * (
        4.166664568298827e-2 + rest2 * (-1.388731625493765e-3 + rest2 * 2.443315711809948e-5)
    )
    quarter = turns.astype(jnp.int32)
    swap = (quarter & 1) == 1
    sine_out = jnp.where(swap, cosine, sine)
    cosine_out = jnp.where(swap, sine, cosine)
    sine_out = jnp.where((quarter & 2) == 2, -sine_out, sine_out)
    cosine_out = jnp.where(((quarter + 1) & 2) == 2, -cosine_out, cosine_out)
    return sine_out, cosine_out


LANES = 256
STORE_LIMIT = 24 * 1024 * 1024


def panel_kernel(slope_mode, stored_in, store_out, wave_ref, own_ref, all_ref, vec_ref, *refs):
    if stored_in:
        real_hbm, imag_hbm, out_ref, real_buf, imag_buf, sems = refs
        hbm_refs, buf_refs = [real_hbm, imag_hbm], [real_buf, imag_buf]
    elif store_out:
        out_ref = refs[0]
        hbm_refs = list(refs[1:1 + store_out])
        buf_refs = list(refs[1 + store_out:1 + 2 * store_out])
        sems = refs[-1]
    else:
        (out_ref,) = refs
    block_count = own_ref.shape[0] // 8

    def copies(block, slot):
        rows = pl.ds(pl.multiple_of(block * 8, 8), 8)
        pairs = list(zip(hbm_refs, buf_refs))
        if stored_in:
            return [pltpu.make_async_copy(hbm.at[rows], buf.at[rows], sems.at[k, block]) for k, (hbm, buf) in enumerate(pairs)]
        return [pltpu.make_async_copy(buf.at[slot], hbm.at[rows], sems.at[k, slot]) for k, (hbm, buf) in enumerate(pairs)]
    wave_value = wave_ref[0]
    own_total = own_ref.shape[0]
    panel_total = all_ref.shape[1]
    width = LANES if panel_total % LANES == 0 else 128
    chunk_count = panel_total // width
    needs_geometry = not stored_in or (slope_mode and stored_in == 1)

    def row_block(block, carry):
        first = pl.multiple_of(block * 8, 8)
        rows = pl.ds(first, 8)
        slot = lax.rem(block, 2)
        if stored_in:
            for copy in copies(block, slot):
                copy.wait()

        if store_out:

            @pl.when(block >= 2)
            def _():
                for copy in copies(block - 2, slot):
                    copy.wait()

        own = own_ref[rows, :]
        own_x = jnp.broadcast_to(own[:, 0:1], (8, width))
        own_y = jnp.broadcast_to(own[:, 1:2], (8, width))
        own_z = jnp.broadcast_to(own[:, 2:3], (8, width))
        own_a = jnp.broadcast_to(own[:, 3:4], (8, width))
        if slope_mode or store_out == 4:
            move_x = jnp.broadcast_to(own[:, 4:5], (8, width))
            move_y = jnp.broadcast_to(own[:, 5:6], (8, width))
            move_z = jnp.broadcast_to(own[:, 6:7], (8, width))

        def lane_block(chunk, sums):
            start = pl.multiple_of(chunk * width, width)
            span = pl.ds(start, width)
            if needs_geometry:
                diff_x = all_ref[0:1, span] - own_x
                diff_y = all_ref[1:2, span] - own_y
                diff_z = all_ref[2:3, span] - own_z
                square = (
                    diff_x * diff_x
                    + diff_y * diff_y
                    + diff_z * diff_z
                    + 0.5 * (all_ref[3:4, span] + own_a)
                )
                inverse = lax.rsqrt(square)
                radius = square * inverse
                phase = wave_value * radius
            if stored_in:
                real_part = real_buf[rows, span]
                imag_part = imag_buf[rows, span]
                if stored_in == 2:
                    first_part = real_part
                    second_part = imag_part
                elif slope_mode:
                    along_move = diff_x * move_x + diff_y * move_y + diff_z * move_z
                    factor = along_move * (inverse * inverse)
                    first_part = (-real_part - phase * imag_part) * factor
                    second_part = (phase * real_part - imag_part) * factor
                else:
                    first_part = real_part
                    second_part = imag_part
            else:
                sine_part, cosine_part = sin_cos(phase)
                if slope_mode:
                    along_move = diff_x * move_x + diff_y * move_y + diff_z * move_z
                    factor = along_move * (inverse * inverse * inverse) * (1.0 / four_pi)
                    first_part = (-cosine_part - phase * sine_part) * factor
                    second_part = (phase * cosine_part - sine_part) * factor
                else:
                    factor = inverse * (1.0 / four_pi)
                    first_part = cosine_part * factor
                    second_part = sine_part * factor
                if store_out:
                    buf_refs[0][slot, :, span] = first_part
                    buf_refs[1][slot, :, span] = second_part
                if store_out == 4:
                    along_move = diff_x * move_x + diff_y * move_y + diff_z * move_z
                    slope_factor = along_move * (inverse * inverse * inverse) * (1.0 / four_pi)
                    buf_refs[2][slot, :, span] = (-cosine_part - phase * sine_part) * slope_factor
                    buf_refs[3][slot, :, span] = (phase * cosine_part - sine_part) * slope_factor
            zone_count = len(sums) // 3
            both_parts = first_part + second_part
            new_sums = []
            for zone in range(zone_count):
                new_sums.append(sums[zone] + first_part * vec_ref[zone:zone + 1, span])
            for zone in range(zone_count, 2 * zone_count):
                new_sums.append(sums[zone] + second_part * vec_ref[zone:zone + 1, span])
            for zone in range(2 * zone_count, 3 * zone_count):
                new_sums.append(sums[zone] + both_parts * vec_ref[zone:zone + 1, span])
            return tuple(new_sums)

        columns = vec_ref.shape[0]
        zeros = tuple(jnp.zeros((8, width), jnp.float32) for _ in range(columns))
        sums = lax.fori_loop(0, chunk_count, lane_block, zeros, unroll=9 if stored_in else (6 if store_out else 3))
        lane = lax.broadcasted_iota(jnp.int32, (8, columns), 1)
        result = jnp.zeros((8, columns), jnp.float32)
        for column in range(columns):
            total = jnp.sum(sums[column], axis=1, keepdims=True)
            result = jnp.where(lane == column, total, result)
        out_ref[rows, :] = result
        if store_out:
            for copy in copies(block, slot):
                copy.start()
        return carry

    if stored_in:
        for block in range(block_count):
            for copy in copies(block, 0):
                copy.start()
    lax.fori_loop(0, block_count, row_block, 0)
    if store_out:
        for block in range(max(0, block_count - 2), block_count):
            for copy in copies(block, block % 2):
                copy.wait()


def panel_contract(slope_mode, wavenumber, own_table, all_table, vector_full, stored=None, store_out=0, direct=False):
    zone_count = vector_full.shape[1] // 2
    vector_rows = jnp.concatenate(
        [vector_full.T, (vector_full[:, :zone_count] - vector_full[:, zone_count:]).T], 0
    )
    outs = panel_call(slope_mode, wavenumber, own_table, all_table, vector_rows, stored, store_out, direct)
    sums = outs[0] if store_out else outs
    first_sum = sums[:, :zone_count]
    second_sum = sums[:, zone_count:2 * zone_count]
    both_sum = sums[:, 2 * zone_count:]
    if slope_mode:
        imag_sum = both_sum - first_sum + second_sum
    else:
        imag_sum = first_sum - second_sum - both_sum
    combined = jnp.concatenate([first_sum + second_sum, imag_sum], 1)
    if store_out:
        return (combined,) + tuple(outs[1:])
    return combined


def panel_call(slope_mode, wavenumber, own_table, all_table, vector_rows, stored, store_out, direct):
    own_total = own_table.shape[0]
    columns = vector_rows.shape[0]
    panel_total = all_table.shape[1]
    elements = own_total * panel_total
    stored_in = 0 if stored is None else (2 if direct else 1)
    operands = [wavenumber, own_table, all_table, vector_rows]
    out_shape = [jax.ShapeDtypeStruct((own_total, columns), jnp.float32)]
    matrix_bytes = 0
    if stored_in:
        operands += list(stored)
        matrix_bytes = 8 * elements
    if store_out:
        out_shape += [jax.ShapeDtypeStruct((own_total, panel_total), jnp.float32)] * store_out
        matrix_bytes = 4 * store_out * elements
    vmem = pl.BlockSpec(memory_space=pltpu.VMEM)
    hbm = pl.BlockSpec(memory_space=pltpu.HBM)
    params = {}
    if stored_in:
        params["scratch_shapes"] = [
            pltpu.VMEM((own_total, panel_total), jnp.float32),
            pltpu.VMEM((own_total, panel_total), jnp.float32),
            pltpu.SemaphoreType.DMA((2, own_total // 8)),
        ]
        params["compiler_params"] = pltpu.CompilerParams(vmem_limit_bytes=60 * 1024 * 1024)
    elif store_out:
        params["scratch_shapes"] = [pltpu.VMEM((2, 8, panel_total), jnp.float32)] * store_out + [
            pltpu.SemaphoreType.DMA((store_out, 2))
        ]
    if stored_in == 2 or (stored_in and not slope_mode):
        flops, transcendentals = 32 * elements, 0
    elif stored_in:
        flops, transcendentals = 60 * elements, 2 * elements
    else:
        flops, transcendentals = 150 * elements, 4 * elements
    return pl.pallas_call(
        functools.partial(panel_kernel, slope_mode, stored_in, store_out),
        out_shape=tuple(out_shape) if store_out else out_shape[0],
        in_specs=[pl.BlockSpec(memory_space=pltpu.SMEM)] + [vmem] * 3 + [hbm] * (len(operands) - 4),
        out_specs=tuple([vmem] + [hbm] * (len(out_shape) - 1)) if store_out else vmem,
        cost_estimate=pl.CostEstimate(
            flops=flops,
            transcendentals=transcendentals,
            bytes_accessed=4 * (own_table.size + all_table.size + vector_rows.size + own_total * columns) + matrix_bytes,
        ),
        **params,
    )(*operands)


def gather_axis(vector, name):
    count = lax.axis_size(name)
    if count > 8:
        return lax.all_gather(vector, name, axis=0, tiled=True)
    index = lax.axis_index(name)
    parts = [vector]
    for shift in range(1, count):
        parts.append(lax.ppermute(vector, name, [(i, (i + shift) % count) for i in range(count)]))
    stacked = jnp.stack([parts[(-offset) % count] for offset in range(count)])
    ordered = jnp.roll(stacked, index, axis=0)
    return ordered.reshape((count * vector.shape[0],) + vector.shape[1:])


def gather_panels(vector):
    return gather_axis(gather_axis(vector, "col"), "row")


def chunk_size_of(count, limit):
    return math.gcd(count, limit)


def rows_sum(block_fn, count, limit):
    size = chunk_size_of(count, limit)
    starts = jnp.arange(count // size, dtype=jnp.int32) * size
    return jnp.sum(lax.map(lambda start: block_fn(start, size), starts), 0)


def local(
    centers,
    panel_areas,
    jump_term,
    displacement,
    design_ids,
    primal_field,
    adjoint_start,
    mic_panels,
    wavenumber,
):
    zone_count = adjoint_start.shape[1] // 2
    owned_count = centers.shape[1]
    axes = ("row", "col")
    wave_value = wavenumber[0]
    packed = jnp.concatenate([centers.T, panel_areas[:, None], adjoint_start], 1)
    gathered = gather_panels(packed)
    panel_total = gathered.shape[0]
    all_xyz = gathered[:, :3].T
    all_area = gathered[:, 3]
    start_full = gathered[:, 4:]
    all_table = gathered[:, :4].T
    own_table = jnp.concatenate(
        [centers.T, panel_areas[:, None], displacement.T, jnp.zeros((owned_count, 1), jnp.float32)], 1
    )

    store = 8 * owned_count * panel_total <= STORE_LIMIT
    store_slope = 16 * owned_count * panel_total <= 2 * STORE_LIMIT
    saved = []
    slope_saved = []

    def apply_adjoint(vector_full, vector_own):
        if store and saved:
            summed = panel_contract(False, wavenumber, own_table, all_table, vector_full, stored=saved)
        elif store:
            summed, *parts = panel_contract(
                False, wavenumber, own_table, all_table, vector_full, store_out=4 if store_slope else 2
            )
            saved.extend(parts[:2])
            slope_saved.extend(parts[2:])
        else:
            summed = panel_contract(False, wavenumber, own_table, all_table, vector_full)
        return panel_areas[:, None] * summed + jump_term[:, None] * vector_own

    first_panel = (
        lax.axis_index("row") * lax.axis_size("col") + lax.axis_index("col")
    ) * owned_count
    panel_ids = first_panel + jnp.arange(owned_count, dtype=jnp.int32)
    mic_hits = jnp.sum(
        (panel_ids[:, None, None] == mic_panels[None, :, :]).astype(jnp.float32), axis=2
    )
    right_side = jnp.concatenate(
        [mic_hits * primal_field[0][:, None], mic_hits * primal_field[1][:, None]], 1
    )
    residual = right_side - apply_adjoint(start_full, adjoint_start)
    residual_full = gather_panels(residual)
    start_norm = jnp.sqrt(square_sum(residual_full))
    start_scale = jnp.concatenate([start_norm, start_norm])[None, :]
    basis_one = residual / start_scale
    basis_one_full = residual_full / start_scale
    image_one = apply_adjoint(basis_one_full, basis_one)
    image_one_full = gather_panels(image_one)
    first_re, first_im = inner_parts(basis_one_full, image_one_full, zone_count)
    lean_one_full = image_one_full - complex_scale(first_re, first_im, basis_one_full, zone_count)
    lean_one = image_one - complex_scale(first_re, first_im, basis_one, zone_count)
    first_norm = jnp.sqrt(square_sum(lean_one_full))
    first_scale = jnp.concatenate([first_norm, first_norm])[None, :]
    basis_two = lean_one / first_scale
    basis_two_full = lean_one_full / first_scale
    image_two = apply_adjoint(basis_two_full, basis_two)
    image_two_full = gather_panels(image_two)
    cross_re, cross_im = inner_parts(basis_one_full, image_two_full, zone_count)
    second_re, second_im = inner_parts(basis_two_full, image_two_full, zone_count)
    lean_two_full = (
        image_two_full
        - complex_scale(cross_re, cross_im, basis_one_full, zone_count)
        - complex_scale(second_re, second_im, basis_two_full, zone_count)
    )
    second_norm = jnp.sqrt(square_sum(lean_two_full))
    coef_one_re, coef_one_im, coef_two_re, coef_two_im = least_squares(
        start_norm,
        first_re,
        first_im,
        first_norm,
        cross_re,
        cross_im,
        second_re,
        second_im,
        second_norm,
    )
    adjoint_field = (
        adjoint_start
        + complex_scale(coef_one_re, coef_one_im, basis_one, zone_count)
        + complex_scale(coef_two_re, coef_two_im, basis_two, zone_count)
    )
    field_full = (
        start_full
        + complex_scale(coef_one_re, coef_one_im, basis_one_full, zone_count)
        + complex_scale(coef_two_re, coef_two_im, basis_two_full, zone_count)
    )

    if slope_saved:
        contracted = panel_contract(True, wavenumber, own_table, all_table, field_full, stored=slope_saved, direct=True)
    else:
        contracted = panel_contract(True, wavenumber, own_table, all_table, field_full, stored=saved or None)
    contrib = panel_areas[:, None] * (
        primal_field[0][:, None] * contracted[:, :zone_count]
        - primal_field[1][:, None] * contracted[:, zone_count:]
    )
    onehot = (design_ids[:, None] == jnp.arange(DESIGN, dtype=jnp.int32)[None, :]).astype(
        jnp.float32
    )
    local_sums = contract_first(contrib, onehot)
    if lax.axis_size("row") > 8:
        sensitivity = lax.psum(lax.psum(local_sums, "col"), "row")
    else:
        sensitivity = jnp.sum(gather_axis(lax.psum(local_sums, "col")[None], "row"), 0)
    return (adjoint_field, sensitivity)


def solution(mesh):
    return jax.shard_map(
        local,
        mesh=mesh,
        in_specs=(
            P(None, ("row", "col")),
            P(("row", "col")),
            P(("row", "col")),
            P(None, ("row", "col")),
            P(("row", "col")),
            P(None, ("row", "col")),
            P(("row", "col"), None),
            P(),
            P(),
        ),
        out_specs=(P(("row", "col"), None), P()),
        check_vma=False,
    )
```

```python
import functools
import math

import jax
import jax.numpy as jnp
from jax import lax
from jax.experimental import pallas as pl
from jax.experimental.pallas import tpu as pltpu
from jax.sharding import PartitionSpec as P

DESIGN = 128


highest = lax.Precision.HIGHEST
four_pi = 4.0 * math.pi


def distances(rows_xyz, rows_area, cols_xyz, cols_area):
    diff_x = rows_xyz[0][:, None] - cols_xyz[0][None, :]
    diff_y = rows_xyz[1][:, None] - cols_xyz[1][None, :]
    diff_z = rows_xyz[2][:, None] - cols_xyz[2][None, :]
    square = (
        diff_x * diff_x
        + diff_y * diff_y
        + diff_z * diff_z
        + 0.5 * (rows_area[:, None] + cols_area[None, :])
    )
    return (diff_x, diff_y, diff_z, jnp.sqrt(square))


def kernel_parts(rows_xyz, rows_area, cols_xyz, cols_area, wave_value):
    radius = distances(rows_xyz, rows_area, cols_xyz, cols_area)[3]
    phase = wave_value * radius
    factor = 1.0 / (four_pi * radius)
    return (jnp.cos(phase) * factor, jnp.sin(phase) * factor)


def slope_parts(rows_xyz, rows_area, cols_xyz, cols_area, cols_move, wave_value):
    diff_x, diff_y, diff_z, radius = distances(rows_xyz, rows_area, cols_xyz, cols_area)
    along_move = (
        diff_x * cols_move[0][None, :]
        + diff_y * cols_move[1][None, :]
        + diff_z * cols_move[2][None, :]
    )
    phase = wave_value * radius
    cosine_part = jnp.cos(phase)
    sine_part = jnp.sin(phase)
    factor = along_move / (four_pi * radius * radius * radius)
    return ((-cosine_part - phase * sine_part) * factor, (phase * cosine_part - sine_part) * factor)


def contract_first(matrix, vector):
    return lax.dot_general(matrix, vector, (((0,), (0,)), ((), ())), precision=highest)


def conj_columns(real_part, imag_part, vector, zone_count):
    left_part = contract_first(real_part, vector)
    right_part = contract_first(imag_part, vector)
    return jnp.concatenate(
        [
            left_part[:, :zone_count] + right_part[:, zone_count:],
            left_part[:, zone_count:] - right_part[:, :zone_count],
        ],
        1,
    )


def inner_parts(left_part, right_part, zone_count):
    left_re, left_im = (left_part[:, :zone_count], left_part[:, zone_count:])
    right_re, right_im = (right_part[:, :zone_count], right_part[:, zone_count:])
    return (
        jnp.sum(left_re * right_re + left_im * right_im, 0),
        jnp.sum(left_re * right_im - left_im * right_re, 0),
    )


def square_sum(vector):
    return jnp.sum(vector * vector, 0).reshape(2, -1).sum(0)


def complex_scale(scale_re, scale_im, vector, zone_count):
    vec_re, vec_im = (vector[:, :zone_count], vector[:, zone_count:])
    return jnp.concatenate(
        [scale_re * vec_re - scale_im * vec_im, scale_re * vec_im + scale_im * vec_re], 1
    )


def least_squares(
    start_norm,
    first_re,
    first_im,
    first_norm,
    cross_re,
    cross_im,
    second_re,
    second_im,
    second_norm,
):
    gram_one = first_re * first_re + first_im * first_im + first_norm * first_norm
    gram_off_re = first_re * cross_re + first_im * cross_im + first_norm * second_re
    gram_off_im = first_re * cross_im - first_im * cross_re + first_norm * second_im
    gram_two = (
        cross_re * cross_re
        + cross_im * cross_im
        + second_re * second_re
        + second_im * second_im
        + second_norm * second_norm
    )
    rhs_one_re = start_norm * first_re
    rhs_one_im = -start_norm * first_im
    rhs_two_re = start_norm * cross_re
    rhs_two_im = -start_norm * cross_im
    determinant = gram_one * gram_two - gram_off_re * gram_off_re - gram_off_im * gram_off_im
    coef_one_re = (
        gram_two * rhs_one_re - (gram_off_re * rhs_two_re - gram_off_im * rhs_two_im)
    ) / determinant
    coef_one_im = (
        gram_two * rhs_one_im - (gram_off_re * rhs_two_im + gram_off_im * rhs_two_re)
    ) / determinant
    coef_two_re = (
        gram_one * rhs_two_re - (gram_off_re * rhs_one_re + gram_off_im * rhs_one_im)
    ) / determinant
    coef_two_im = (
        gram_one * rhs_two_im - (gram_off_re * rhs_one_im - gram_off_im * rhs_one_re)
    ) / determinant
    return (coef_one_re, coef_one_im, coef_two_re, coef_two_im)


def slope_parts_t(own_xyz, own_area, own_move, all_xyz, all_area, wave_value):
    diff_x = all_xyz[0][None, :] - own_xyz[0][:, None]
    diff_y = all_xyz[1][None, :] - own_xyz[1][:, None]
    diff_z = all_xyz[2][None, :] - own_xyz[2][:, None]
    square = (
        diff_x * diff_x
        + diff_y * diff_y
        + diff_z * diff_z
        + 0.5 * (all_area[None, :] + own_area[:, None])
    )
    radius = jnp.sqrt(square)
    along_move = (
        diff_x * own_move[0][:, None]
        + diff_y * own_move[1][:, None]
        + diff_z * own_move[2][:, None]
    )
    phase = wave_value * radius
    cosine_part = jnp.cos(phase)
    sine_part = jnp.sin(phase)
    factor = along_move / (four_pi * radius * radius * radius)
    return ((-cosine_part - phase * sine_part) * factor, (phase * cosine_part - sine_part) * factor)


TWO_OVER_PI = 0.6366197723675814
HALF_PI_HI = 1.5703125
HALF_PI_MID = 4.837512969970703125e-4
HALF_PI_LO = 7.54978995489188216e-8


def sin_cos(angle):
    turns = jnp.floor(angle * TWO_OVER_PI + 0.5)
    rest = angle - turns * HALF_PI_HI
    rest = rest - turns * HALF_PI_MID
    rest = rest - turns * HALF_PI_LO
    rest2 = rest * rest
    sine = rest + rest * rest2 * (
        -1.6666654611e-1 + rest2 * (8.3321608736e-3 + rest2 * (-1.9515295891e-4))
    )
    cosine = 1.0 - 0.5 * rest2 + rest2 * rest2 * (
        4.166664568298827e-2 + rest2 * (-1.388731625493765e-3 + rest2 * 2.443315711809948e-5)
    )
    quarter = turns.astype(jnp.int32)
    swap = (quarter & 1) == 1
    sine_out = jnp.where(swap, cosine, sine)
    cosine_out = jnp.where(swap, sine, cosine)
    sine_out = jnp.where((quarter & 2) == 2, -sine_out, sine_out)
    cosine_out = jnp.where(((quarter + 1) & 2) == 2, -cosine_out, cosine_out)
    return sine_out, cosine_out


LANES = 256
STORE_LIMIT = 24 * 1024 * 1024


def panel_kernel(slope_mode, stored_in, store_out, wave_ref, own_ref, all_ref, vec_ref, *refs):
    if stored_in:
        real_hbm, imag_hbm, out_ref, real_buf, imag_buf, sems = refs
        hbm_refs, buf_refs = [real_hbm, imag_hbm], [real_buf, imag_buf]
    elif store_out:
        out_ref = refs[0]
        hbm_refs = list(refs[1:1 + store_out])
        buf_refs = list(refs[1 + store_out:1 + 2 * store_out])
        sems = refs[-1]
    else:
        (out_ref,) = refs
    block_count = own_ref.shape[0] // 8

    def copies(block, slot):
        rows = pl.ds(pl.multiple_of(block * 8, 8), 8)
        pairs = list(zip(hbm_refs, buf_refs))
        if stored_in:
            return [pltpu.make_async_copy(hbm.at[rows], buf.at[rows], sems.at[k, block]) for k, (hbm, buf) in enumerate(pairs)]
        return [pltpu.make_async_copy(buf.at[slot], hbm.at[rows], sems.at[k, slot]) for k, (hbm, buf) in enumerate(pairs)]
    wave_value = wave_ref[0]
    own_total = own_ref.shape[0]
    panel_total = all_ref.shape[1]
    width = LANES if panel_total % LANES == 0 else 128
    chunk_count = panel_total // width
    needs_geometry = not stored_in or (slope_mode and stored_in == 1)

    def row_block(block, carry):
        first = pl.multiple_of(block * 8, 8)
        rows = pl.ds(first, 8)
        slot = lax.rem(block, 2)
        if stored_in:
            for copy in copies(block, slot):
                copy.wait()

        if store_out:

            @pl.when(block >= 2)
            def _():
                for copy in copies(block - 2, slot):
                    copy.wait()

        own = own_ref[rows, :]
        own_x = jnp.broadcast_to(own[:, 0:1], (8, width))
        own_y = jnp.broadcast_to(own[:, 1:2], (8, width))
        own_z = jnp.broadcast_to(own[:, 2:3], (8, width))
        own_a = jnp.broadcast_to(own[:, 3:4], (8, width))
        if slope_mode or store_out == 4:
            move_x = jnp.broadcast_to(own[:, 4:5], (8, width))
            move_y = jnp.broadcast_to(own[:, 5:6], (8, width))
            move_z = jnp.broadcast_to(own[:, 6:7], (8, width))

        def lane_block(chunk, sums):
            start = pl.multiple_of(chunk * width, width)
            span = pl.ds(start, width)
            if needs_geometry:
                diff_x = all_ref[0:1, span] - own_x
                diff_y = all_ref[1:2, span] - own_y
                diff_z = all_ref[2:3, span] - own_z
                square = (
                    diff_x * diff_x
                    + diff_y * diff_y
                    + diff_z * diff_z
                    + 0.5 * (all_ref[3:4, span] + own_a)
                )
                inverse = lax.rsqrt(square)
                radius = square * inverse
                phase = wave_value * radius
            if stored_in:
                real_part = real_buf[rows, span]
                imag_part = imag_buf[rows, span]
                if stored_in == 2:
                    first_part = real_part
                    second_part = imag_part
                elif slope_mode:
                    along_move = diff_x * move_x + diff_y * move_y + diff_z * move_z
                    factor = along_move * (inverse * inverse)
                    first_part = (-real_part - phase * imag_part) * factor
                    second_part = (phase * real_part - imag_part) * factor
                else:
                    first_part = real_part
                    second_part = imag_part
            else:
                sine_part, cosine_part = sin_cos(phase)
                if slope_mode:
                    along_move = diff_x * move_x + diff_y * move_y + diff_z * move_z
                    factor = along_move * (inverse * inverse * inverse) * (1.0 / four_pi)
                    first_part = (-cosine_part - phase * sine_part) * factor
                    second_part = (phase * cosine_part - sine_part) * factor
                else:
                    factor = inverse * (1.0 / four_pi)
                    first_part = cosine_part * factor
                    second_part = sine_part * factor
                if store_out:
                    buf_refs[0][slot, :, span] = first_part
                    buf_refs[1][slot, :, span] = second_part
                if store_out == 4:
                    along_move = diff_x * move_x + diff_y * move_y + diff_z * move_z
                    slope_factor = along_move * (inverse * inverse * inverse) * (1.0 / four_pi)
                    buf_refs[2][slot, :, span] = (-cosine_part - phase * sine_part) * slope_factor
                    buf_refs[3][slot, :, span] = (phase * cosine_part - sine_part) * slope_factor
            zone_count = len(sums) // 3
            both_parts = first_part + second_part
            new_sums = []
            for zone in range(zone_count):
                new_sums.append(sums[zone] + first_part * vec_ref[zone:zone + 1, span])
            for zone in range(zone_count, 2 * zone_count):
                new_sums.append(sums[zone] + second_part * vec_ref[zone:zone + 1, span])
            for zone in range(2 * zone_count, 3 * zone_count):
                new_sums.append(sums[zone] + both_parts * vec_ref[zone:zone + 1, span])
            return tuple(new_sums)

        columns = vec_ref.shape[0]
        zeros = tuple(jnp.zeros((8, width), jnp.float32) for _ in range(columns))
        sums = lax.fori_loop(0, chunk_count, lane_block, zeros, unroll=12 if stored_in else (6 if store_out else 3))
        lane = lax.broadcasted_iota(jnp.int32, (8, columns), 1)
        result = jnp.zeros((8, columns), jnp.float32)
        for column in range(columns):
            total = jnp.sum(sums[column], axis=1, keepdims=True)
            result = jnp.where(lane == column, total, result)
        out_ref[rows, :] = result
        if store_out:
            for copy in copies(block, slot):
                copy.start()
        return carry

    if stored_in:
        for block in range(block_count):
            for copy in copies(block, 0):
                copy.start()
    lax.fori_loop(0, block_count, row_block, 0)
    if store_out:
        for block in range(max(0, block_count - 2), block_count):
            for copy in copies(block, block % 2):
                copy.wait()


def panel_contract(slope_mode, wavenumber, own_table, all_table, vector_full, stored=None, store_out=0, direct=False):
    zone_count = vector_full.shape[1] // 2
    vector_rows = jnp.concatenate(
        [vector_full.T, (vector_full[:, :zone_count] - vector_full[:, zone_count:]).T], 0
    )
    outs = panel_call(slope_mode, wavenumber, own_table, all_table, vector_rows, stored, store_out, direct)
    sums = outs[0] if store_out else outs
    first_sum = sums[:, :zone_count]
    second_sum = sums[:, zone_count:2 * zone_count]
    both_sum = sums[:, 2 * zone_count:]
    if slope_mode:
        imag_sum = both_sum - first_sum + second_sum
    else:
        imag_sum = first_sum - second_sum - both_sum
    combined = jnp.concatenate([first_sum + second_sum, imag_sum], 1)
    if store_out:
        return (combined,) + tuple(outs[1:])
    return combined


def panel_call(slope_mode, wavenumber, own_table, all_table, vector_rows, stored, store_out, direct):
    own_total = own_table.shape[0]
    columns = vector_rows.shape[0]
    panel_total = all_table.shape[1]
    elements = own_total * panel_total
    stored_in = 0 if stored is None else (2 if direct else 1)
    operands = [wavenumber, own_table, all_table, vector_rows]
    out_shape = [jax.ShapeDtypeStruct((own_total, columns), jnp.float32)]
    matrix_bytes = 0
    if stored_in:
        operands += list(stored)
        matrix_bytes = 8 * elements
    if store_out:
        out_shape += [jax.ShapeDtypeStruct((own_total, panel_total), jnp.float32)] * store_out
        matrix_bytes = 4 * store_out * elements
    vmem = pl.BlockSpec(memory_space=pltpu.VMEM)
    hbm = pl.BlockSpec(memory_space=pltpu.HBM)
    params = {}
    if stored_in:
        params["scratch_shapes"] = [
            pltpu.VMEM((own_total, panel_total), jnp.float32),
            pltpu.VMEM((own_total, panel_total), jnp.float32),
            pltpu.SemaphoreType.DMA((2, own_total // 8)),
        ]
        params["compiler_params"] = pltpu.CompilerParams(vmem_limit_bytes=60 * 1024 * 1024)
    elif store_out:
        params["scratch_shapes"] = [pltpu.VMEM((2, 8, panel_total), jnp.float32)] * store_out + [
            pltpu.SemaphoreType.DMA((store_out, 2))
        ]
    if stored_in == 2 or (stored_in and not slope_mode):
        flops, transcendentals = 32 * elements, 0
    elif stored_in:
        flops, transcendentals = 60 * elements, 2 * elements
    else:
        flops, transcendentals = 150 * elements, 4 * elements
    return pl.pallas_call(
        functools.partial(panel_kernel, slope_mode, stored_in, store_out),
        out_shape=tuple(out_shape) if store_out else out_shape[0],
        in_specs=[pl.BlockSpec(memory_space=pltpu.SMEM)] + [vmem] * 3 + [hbm] * (len(operands) - 4),
        out_specs=tuple([vmem] + [hbm] * (len(out_shape) - 1)) if store_out else vmem,
        cost_estimate=pl.CostEstimate(
            flops=flops,
            transcendentals=transcendentals,
            bytes_accessed=4 * (own_table.size + all_table.size + vector_rows.size + own_total * columns) + matrix_bytes,
        ),
        **params,
    )(*operands)


def gather_axis(vector, name):
    count = lax.axis_size(name)
    if count > 8:
        return lax.all_gather(vector, name, axis=0, tiled=True)
    index = lax.axis_index(name)
    parts = [vector]
    for shift in range(1, count):
        parts.append(lax.ppermute(vector, name, [(i, (i + shift) % count) for i in range(count)]))
    stacked = jnp.stack([parts[(-offset) % count] for offset in range(count)])
    ordered = jnp.roll(stacked, index, axis=0)
    return ordered.reshape((count * vector.shape[0],) + vector.shape[1:])


def gather_panels(vector):
    return gather_axis(gather_axis(vector, "col"), "row")


def chunk_size_of(count, limit):
    return math.gcd(count, limit)


def rows_sum(block_fn, count, limit):
    size = chunk_size_of(count, limit)
    starts = jnp.arange(count // size, dtype=jnp.int32) * size
    return jnp.sum(lax.map(lambda start: block_fn(start, size), starts), 0)


def local(
    centers,
    panel_areas,
    jump_term,
    displacement,
    design_ids,
    primal_field,
    adjoint_start,
    mic_panels,
    wavenumber,
):
    zone_count = adjoint_start.shape[1] // 2
    owned_count = centers.shape[1]
    axes = ("row", "col")
    wave_value = wavenumber[0]
    packed = jnp.concatenate([centers.T, panel_areas[:, None], adjoint_start], 1)
    gathered = gather_panels(packed)
    panel_total = gathered.shape[0]
    all_xyz = gathered[:, :3].T
    all_area = gathered[:, 3]
    start_full = gathered[:, 4:]
    all_table = gathered[:, :4].T
    own_table = jnp.concatenate(
        [centers.T, panel_areas[:, None], displacement.T, jnp.zeros((owned_count, 1), jnp.float32)], 1
    )

    store = 8 * owned_count * panel_total <= STORE_LIMIT
    store_slope = 16 * owned_count * panel_total <= 2 * STORE_LIMIT
    saved = []
    slope_saved = []

    def apply_adjoint(vector_full, vector_own):
        if store and saved:
            summed = panel_contract(False, wavenumber, own_table, all_table, vector_full, stored=saved)
        elif store:
            summed, *parts = panel_contract(
                False, wavenumber, own_table, all_table, vector_full, store_out=4 if store_slope else 2
            )
            saved.extend(parts[:2])
            slope_saved.extend(parts[2:])
        else:
            summed = panel_contract(False, wavenumber, own_table, all_table, vector_full)
        return panel_areas[:, None] * summed + jump_term[:, None] * vector_own

    first_panel = (
        lax.axis_index("row") * lax.axis_size("col") + lax.axis_index("col")
    ) * owned_count
    panel_ids = first_panel + jnp.arange(owned_count, dtype=jnp.int32)
    mic_hits = jnp.sum(
        (panel_ids[:, None, None] == mic_panels[None, :, :]).astype(jnp.float32), axis=2
    )
    right_side = jnp.concatenate(
        [mic_hits * primal_field[0][:, None], mic_hits * primal_field[1][:, None]], 1
    )
    residual = right_side - apply_adjoint(start_full, adjoint_start)
    residual_full = gather_panels(residual)
    start_norm = jnp.sqrt(square_sum(residual_full))
    start_scale = jnp.concatenate([start_norm, start_norm])[None, :]
    basis_one = residual / start_scale
    basis_one_full = residual_full / start_scale
    image_one = apply_adjoint(basis_one_full, basis_one)
    image_one_full = gather_panels(image_one)
    first_re, first_im = inner_parts(basis_one_full, image_one_full, zone_count)
    lean_one_full = image_one_full - complex_scale(first_re, first_im, basis_one_full, zone_count)
    lean_one = image_one - complex_scale(first_re, first_im, basis_one, zone_count)
    first_norm = jnp.sqrt(square_sum(lean_one_full))
    first_scale = jnp.concatenate([first_norm, first_norm])[None, :]
    basis_two = lean_one / first_scale
    basis_two_full = lean_one_full / first_scale
    image_two = apply_adjoint(basis_two_full, basis_two)
    image_two_full = gather_panels(image_two)
    cross_re, cross_im = inner_parts(basis_one_full, image_two_full, zone_count)
    second_re, second_im = inner_parts(basis_two_full, image_two_full, zone_count)
    lean_two_full = (
        image_two_full
        - complex_scale(cross_re, cross_im, basis_one_full, zone_count)
        - complex_scale(second_re, second_im, basis_two_full, zone_count)
    )
    second_norm = jnp.sqrt(square_sum(lean_two_full))
    coef_one_re, coef_one_im, coef_two_re, coef_two_im = least_squares(
        start_norm,
        first_re,
        first_im,
        first_norm,
        cross_re,
        cross_im,
        second_re,
        second_im,
        second_norm,
    )
    adjoint_field = (
        adjoint_start
        + complex_scale(coef_one_re, coef_one_im, basis_one, zone_count)
        + complex_scale(coef_two_re, coef_two_im, basis_two, zone_count)
    )
    field_full = (
        start_full
        + complex_scale(coef_one_re, coef_one_im, basis_one_full, zone_count)
        + complex_scale(coef_two_re, coef_two_im, basis_two_full, zone_count)
    )

    if slope_saved:
        contracted = panel_contract(True, wavenumber, own_table, all_table, field_full, stored=slope_saved, direct=True)
    else:
        contracted = panel_contract(True, wavenumber, own_table, all_table, field_full, stored=saved or None)
    contrib = panel_areas[:, None] * (
        primal_field[0][:, None] * contracted[:, :zone_count]
        - primal_field[1][:, None] * contracted[:, zone_count:]
    )
    onehot = (design_ids[:, None] == jnp.arange(DESIGN, dtype=jnp.int32)[None, :]).astype(
        jnp.float32
    )
    local_sums = contract_first(contrib, onehot)
    if lax.axis_size("row") > 8:
        sensitivity = lax.psum(lax.psum(local_sums, "col"), "row")
    else:
        sensitivity = jnp.sum(gather_axis(lax.psum(local_sums, "col")[None], "row"), 0)
    return (adjoint_field, sensitivity)


def solution(mesh):
    return jax.shard_map(
        local,
        mesh=mesh,
        in_specs=(
            P(None, ("row", "col")),
            P(("row", "col")),
            P(("row", "col")),
            P(None, ("row", "col")),
            P(("row", "col")),
            P(None, ("row", "col")),
            P(("row", "col"), None),
            P(),
            P(),
        ),
        out_specs=(P(("row", "col"), None), P()),
        check_vma=False,
    )
```
